128 devices in a mesh: src: 4 (over x), frame: 8 (over y, z_lo), tile: 4 (over z_hi, core).
Axes of the slice: x: 4, y: 4, z: 4 (z_hi: 2, z_lo: 2; z = z_hi * 2 + z_lo), core: 2. Of those that a mesh axis runs over, the one named last changes fastest.
Arguments:
- feats: float32 [196608, 512], P(('src', 'frame', 'tile')), may hold values from -40 to 40
- row_map: int32 [196608], P(('src', 'frame', 'tile')), may hold values from 0 to 196607, as said below
- clip_ids: int32 [48], replicated, may hold values from 0 to 3, never falling along the last dimension, each value on 1 to 24 neighbouring positions
- norm_gain: float32 [512], replicated, may hold values from 0.1 to 1.9
- norm_bias: float32 [512], replicated, may hold values from -3 to 3
- conv_weight: bfloat16 [3, 3, 3, 512, 512], replicated, may hold values from -0.0546875 to 0.0546875
- conv_bias: float32 [512], replicated, may hold values from -2 to 2
Outputs:
- decoded: bfloat16 [48, 32, 128, 512], P('frame', 'tile', 'src')
The draws below stay inside these ranges and needn't reach their ends.
Inputs may be any that keep to these rules, and one draw needn't show every extreme that they name: `row_map`: every decoder index occurs once; the rows of each device of src+frame+tile hold exactly 12 indices of each aligned block of 1536 decoder indices. `clip_ids`: clip numbers never fall along the frames; each clip has 1 to 24 frames, one exactly 24.
All inputs are finite; a program needn't handle non-finite values.
Results may differ from the reference program's by a relative error of at most 0.0029.
Values may be sent and summed in bfloat16 or wider, within the bound.
No kernel may reach another device: no remote copies, remote signals or barrier semaphores. Data moves between devices by JAX's collectives and lax.ppermute only.
A program may use at most 128 MiB of HBM per device.

```python
import math
import jax
import jax.numpy as jnp
import numpy as np
from jax import lax

C = 512
GROUPS = 32
CLIPS = 4
FR_DEV = 6
HR = 8
WCOL = 32
VOX_DEV = 1536
ALL_ROWS = 196608
PER_PAIR = 12
FRAMES = 48
HEIGHT = 32
WIDTH = 128
MOST = 24
N_SRC = 4
N_FRAME = 8
N_TILE = 4


feature_level = 0.1


def shuffled(subkey):
    return jax.random.permutation(subkey, VOX_DEV).astype(jnp.int32)


def row_layout(key):
    devices = ALL_ROWS // VOX_DEV
    source_keys = jax.random.split(jax.random.fold_in(key, 1), devices)
    owner_keys = jax.random.split(jax.random.fold_in(key, 2), devices)
    source_perm = jax.vmap(shuffled)(source_keys)
    owner_perm = jax.vmap(shuffled)(owner_keys)
    owners = source_perm // PER_PAIR
    within = source_perm % PER_PAIR
    senders = jnp.arange(devices, dtype=jnp.int32)[:, None]
    slot_ids = owner_perm[owners, senders * PER_PAIR + within]
    return (owners * VOX_DEV + slot_ids).reshape(-1).astype(jnp.int32)


def draw_row_map(key, part):
    return row_layout(jax.random.fold_in(key, 11))


def draw_feats(key, part):
    targets = row_layout(jax.random.fold_in(key, 11))
    n_frame = FRAMES // FR_DEV
    n_tile = HEIGHT // HR
    device = targets // VOX_DEV
    inner = targets % VOX_DEV
    width_block = device // (n_frame * n_tile)
    frame_block = device // n_tile % n_frame
    tile_block = device % n_tile
    height_index = tile_block * HR + inner // WCOL % HR
    width_index = width_block * WCOL + inner % WCOL
    parity_sign = ((height_index + width_index) % 2 * 2 - 1).astype(jnp.float32)
    frame_pos = (frame_block * FR_DEV + inner // (HR * WCOL)).astype(jnp.float32) / FRAMES
    height_pos = height_index.astype(jnp.float32) / HEIGHT
    width_pos = width_index.astype(jnp.float32) / WIDTH
    noise_rows = jax.random.uniform(jax.random.fold_in(key, 21), (ALL_ROWS,), jnp.float32, 0.0, math.log(3.0))
    row_scale = jnp.exp(width_pos * math.log(3.0) + height_pos * math.log(1.6) + frame_pos * math.log(3.0) + noise_rows)
    col_scale = jnp.exp(jax.random.uniform(jax.random.fold_in(key, 22), (C,), jnp.float32, math.log(0.5), math.log(2.0)))
    group_sign = (jax.random.randint(jax.random.fold_in(key, 31), (GROUPS,), 0, 2) * 2 - 1).astype(jnp.float32)
    channel_sign = jnp.repeat(group_sign, C // GROUPS)
    channel_size = jax.random.uniform(jax.random.fold_in(key, 32), (C,), jnp.float32, 1.0, 2.0)
    channel_offset = 3.0 * channel_sign * channel_size * col_scale
    base = jnp.clip(jax.random.normal(jax.random.fold_in(key, 23), (ALL_ROWS, C), jnp.float32), -4.0, 4.0)
    place_factor = 0.3 + 0.4 * frame_pos + 0.8 * width_pos + 1.2 * width_pos * width_pos + 0.6 * height_pos + 0.1 * parity_sign
    spread_part = base * row_scale[:, None] * col_scale[None, :]
    offset_part = place_factor[:, None] * channel_offset[None, :]
    return (feature_level * (spread_part + offset_part)).astype(jnp.float32)


def split_up(count, total, bound, slope):
    portions = [(1 << 20) // math.isqrt(standing ** slope) + 1 for standing in range(2, count + 1)]
    surplus, holding = total - bound - (count - 1), [1] * (count - 1)
    while surplus > 0:
        candidates = [i for i in range(count - 1) if holding[i] < bound]
        whole, remaining = sum([portions[i] for i in candidates]), surplus
        for i in candidates:
            extra = min(bound - holding[i], max(1, remaining * portions[i] // whole), surplus)
            holding[i] = holding[i] + extra
            surplus = surplus - extra
    return np.array([bound] + holding)


def ragged(stream_key, number_of, total, most, skew):
    if number_of == 2:
        one = jax.random.randint(stream_key, (), max(1, total - most), min(most, total - 1) + 1)
        return jnp.stack([one, total - one])
    lengths = jnp.asarray(split_up(number_of, total, most, skew), jnp.int32)
    twos = (number_of - 1) // 2
    donor, receiver = lengths[1:1 + 2 * twos:2], lengths[2:2 + 2 * twos:2]
    slack = jnp.minimum(donor - 1, most - receiver)
    moved = jax.random.randint(jax.random.fold_in(stream_key, 1), (twos,), 0, 1 << 20) % (slack + 1)
    lengths = lengths.at[1:1 + 2 * twos:2].set(donor - moved).at[2:2 + 2 * twos:2].set(receiver + moved)
    return lengths[jax.random.permutation(jax.random.fold_in(stream_key, 2), number_of)]


def normal_values(rng, dims, deviation, most, held_as=jnp.bfloat16):
    return jnp.clip(deviation * jax.random.normal(rng, dims, jnp.float32), -most, most).astype(held_as)


def setup_inputs(seed: int = 0) -> dict:
    key_of = jax.random.split(jax.random.key(seed), 8)
    return {
        "feats": draw_feats(jax.random.fold_in(key_of[7], 71), 0),
        "row_map": draw_row_map(jax.random.fold_in(key_of[7], 71), 0),
        "clip_ids": jnp.searchsorted(jnp.cumsum(ragged(key_of[2], CLIPS, FRAMES, MOST, 0)), jnp.arange(FRAMES), side="right").astype(jnp.int32),
        "norm_gain": jnp.clip(1.0 + 0.18 * jax.random.normal(key_of[3], (C,), jnp.float32), 0.1, 1.9),
        "norm_bias": normal_values(key_of[4], (C,), 0.5, 3.0, jnp.float32),
        "conv_weight": normal_values(key_of[5], (3, 3, 3, C, C), (27 * C) ** -0.5, 0.0546875),
        "conv_bias": normal_values(key_of[6], (C,), 0.3, 2.0, jnp.float32),
    }


def reference(feats, row_map, clip_ids, norm_gain, norm_bias, conv_weight, conv_bias):
    placed = jnp.zeros_like(feats).at[row_map].set(feats)
    features = placed.reshape(N_SRC, N_FRAME, N_TILE, FR_DEV, HR, WCOL, C)
    features = features.transpose(1, 3, 2, 4, 0, 5, 6).reshape(FRAMES, HEIGHT, WIDTH, C)
    group_width = C // GROUPS
    shaped = features.reshape(FRAMES, HEIGHT * WIDTH, GROUPS, group_width)
    onehot = (clip_ids[:, None] == jnp.arange(CLIPS, dtype=jnp.int32)[None, :]).astype(jnp.float32)
    counts = lax.optimization_barrier(jnp.sum(onehot, axis=0)) * (HEIGHT * WIDTH * group_width)
    frame_sum = lax.optimization_barrier(jnp.sum(shaped, axis=(1, 3)))
    clip_mean = jnp.dot(onehot.T, frame_sum, precision=lax.Precision.HIGHEST) / counts[:, None]
    frame_mean = jnp.dot(onehot, clip_mean, precision=lax.Precision.HIGHEST)
    centred = shaped - frame_mean[:, None, :, None]
    frame_sq = lax.optimization_barrier(jnp.sum(centred * centred, axis=(1, 3)))
    clip_var = jnp.dot(onehot.T, frame_sq, precision=lax.Precision.HIGHEST) / counts[:, None]
    inverse_std = 1.0 / jnp.sqrt(clip_var + 1e-06)
    frame_inv = jnp.dot(onehot, inverse_std, precision=lax.Precision.HIGHEST)
    normed = (centred * frame_inv[:, None, :, None]).reshape(FRAMES, HEIGHT, WIDTH, C)
    activated = jax.nn.silu(normed * norm_gain + norm_bias).astype(jnp.bfloat16)
    act_wide = activated.astype(jnp.float32)
    kernel = conv_weight.astype(jnp.float32)
    conv_sum = jnp.zeros((FRAMES, HEIGHT, WIDTH, C), jnp.float32)
    for tap_time in range(3):
        delay_steps = 2 - tap_time
        if delay_steps > 0:
            shifted = jnp.concatenate([jnp.zeros((delay_steps, HEIGHT, WIDTH, C), jnp.float32), act_wide[:FRAMES - delay_steps]], axis=0)
            validity = jnp.concatenate([jnp.zeros((delay_steps,), jnp.float32), (clip_ids[delay_steps:] == clip_ids[:FRAMES - delay_steps]).astype(jnp.float32)])
        else:
            shifted = act_wide
            validity = jnp.ones((FRAMES,), jnp.float32)
        partial_value = lax.conv_general_dilated(shifted, kernel[tap_time], (1, 1), ((1, 1), (1, 1)), dimension_numbers=('NHWC', 'HWIO', 'NHWC'), precision=lax.Precision.HIGHEST)
        conv_sum = conv_sum + partial_value * validity[:, None, None, None]
    return (features + conv_sum + conv_bias).astype(jnp.bfloat16)
```

```python
import jax
import jax.numpy as jnp
from jax import lax
from jax.sharding import PartitionSpec as P

GROUPS = 32
CLIPS = 4
FR_DEV = 6
HR = 8
WCOL = 32
HIGH = lax.Precision.HIGHEST


def passed_along(x, axis, by):
    peers = lax.axis_size(axis)
    pairs = [(i, i + by) for i in range(peers) if 0 <= i + by < peers]
    return lax.ppermute(x, axis, pairs)


def with_halo(x, sides, width):
    for axis, dim in sides:
        peers, length = (lax.axis_size(axis), x.shape[dim])
        up = [(i, (i + 1) % peers) for i in range(peers - 1)]
        down = [(j, i) for i, j in up]
        last = lax.slice_in_dim(x, length - width, length, axis=dim)
        leading = lax.slice_in_dim(x, 0, width, axis=dim)
        before = lax.ppermute(last, axis, up)
        after = lax.ppermute(leading, axis, down)
        x = jnp.concatenate([before, x, after], axis=dim)
    return x


def shards(feats, row_map, clip_ids, norm_gain, norm_bias, conv_weight, conv_bias):
    local_rows, channels = feats.shape
    n_src = lax.axis_size("src")
    n_frame = lax.axis_size("frame")
    n_tile = lax.axis_size("tile")
    devices = n_src * n_frame * n_tile
    per_pair = local_rows // devices
    group_width = channels // GROUPS
    per_frame = HR * WCOL

    owners = row_map // local_rows
    slot_ids = row_map % local_rows
    row_frame = (owners // n_tile) % n_frame * FR_DEV + slot_ids // per_frame
    row_clip = jnp.take(clip_ids, row_frame)
    row_onehot = (row_clip[:, None] == jnp.arange(CLIPS, dtype=jnp.int32)[None, :]).astype(
        jnp.float32
    )

    grouped = feats.reshape(local_rows, GROUPS, group_width)
    local_n = jnp.sum(row_onehot, axis=0) * group_width
    local_s = jnp.dot(row_onehot.T, jnp.sum(grouped, axis=2), precision=HIGH)
    local_m = local_s / jnp.maximum(local_n, 1.0)[:, None]
    row_m = jnp.dot(row_onehot, local_m, precision=HIGH)
    dev = grouped - row_m[:, :, None]
    local_m2 = jnp.dot(row_onehot.T, jnp.sum(dev * dev, axis=2), precision=HIGH)

    ordering = jnp.argsort(owners, stable=True)
    outgoing = feats[ordering].reshape(devices, per_pair, channels)
    sent_slots = slot_ids[ordering].astype(jnp.float32).reshape(devices, per_pair)
    stats = jnp.concatenate([local_n, local_s.reshape(-1), local_m2.reshape(-1)])
    tail = jnp.zeros((channels - per_pair - stats.shape[0],), jnp.float32)
    extra = jnp.concatenate(
        [sent_slots, jnp.broadcast_to(jnp.concatenate([stats, tail]), (devices, channels - per_pair))],
        axis=1,
    )
    payload = jnp.concatenate([outgoing, extra[:, None, :]], axis=1)
    arrived = lax.all_to_all(
        payload, ("src", "frame", "tile"), split_axis=0, concat_axis=0, tiled=True
    )

    rows = arrived[:, :per_pair, :].reshape(-1, channels)
    info = arrived[:, per_pair, :]
    targets = info[:, :per_pair].reshape(-1).astype(jnp.int32)
    part_n = info[:, per_pair : per_pair + CLIPS]
    base = per_pair + CLIPS
    part_s = info[:, base : base + CLIPS * GROUPS].reshape(devices, CLIPS, GROUPS)
    part_m2 = info[:, base + CLIPS * GROUPS : base + 2 * CLIPS * GROUPS].reshape(
        devices, CLIPS, GROUPS
    )
    total_n = jnp.sum(part_n, axis=0)
    clip_mean = jnp.sum(part_s, axis=0) / total_n[:, None]
    part_m = part_s / jnp.maximum(part_n, 1.0)[:, :, None]
    spread = part_m - clip_mean[None]
    clip_m2 = jnp.sum(part_m2, axis=0) + jnp.sum(part_n[:, :, None] * spread * spread, axis=0)
    clip_var = clip_m2 / total_n[:, None]

    inverse = jnp.argsort(targets)
    features = rows[inverse].reshape(FR_DEV, HR, WCOL, channels)

    first_frame = lax.axis_index("frame") * FR_DEV
    padded_ids = jnp.concatenate([jnp.full((2,), -1, jnp.int32), clip_ids])
    window_ids = lax.dynamic_slice_in_dim(padded_ids, first_frame, FR_DEV + 2)
    own_ids = window_ids[2:]
    onehot = (own_ids[:, None] == jnp.arange(CLIPS, dtype=jnp.int32)[None, :]).astype(jnp.float32)
    shaped = features.reshape(FR_DEV, per_frame, GROUPS, group_width)
    frame_mean = jnp.dot(onehot, clip_mean, precision=HIGH)
    centred = shaped - frame_mean[:, None, :, None]
    inverse_std = 1.0 / jnp.sqrt(clip_var + 1e-06)
    frame_inv = jnp.dot(onehot, inverse_std, precision=HIGH)
    normed = (centred * frame_inv[:, None, :, None]).reshape(FR_DEV, HR, WCOL, channels)
    activated = jax.nn.silu(normed * norm_gain + norm_bias).astype(jnp.bfloat16)
    previous = passed_along(activated[FR_DEV - 2 :], "frame", 1)
    extended = jnp.concatenate([previous, activated], axis=0)
    padded = with_halo(extended, (("tile", 1), ("src", 2)), 1)
    conv_sum = jnp.zeros((FR_DEV, HR, WCOL, channels), jnp.float32)
    for tap_time in range(3):
        validity = (window_ids[tap_time : tap_time + FR_DEV] == own_ids).astype(jnp.float32)
        partial_value = lax.conv_general_dilated(
            padded[tap_time : tap_time + FR_DEV],
            conv_weight[tap_time],
            (1, 1),
            "VALID",
            dimension_numbers=("NHWC", "HWIO", "NHWC"),
            preferred_element_type=jnp.float32,
        )
        conv_sum = conv_sum + partial_value * validity[:, None, None, None]
    decoded = features + conv_sum + conv_bias
    return decoded.astype(jnp.bfloat16)


def solution(mesh):
    placed = (
        P(("src", "frame", "tile"), None),
        P(("src", "frame", "tile")),
        P(),
        P(),
        P(),
        P(),
        P(),
    )
    return jax.shard_map(
        shards,
        mesh=mesh,
        in_specs=placed,
        out_specs=P("frame", "tile", "src", None),
        check_vma=False,
    )
```

```python
import jax
import jax.numpy as jnp
from jax import lax
from jax.experimental import pallas as pl
from jax.experimental.pallas import tpu as pltpu
from jax.sharding import PartitionSpec as P

GROUPS = 32
CLIPS = 4
FR_DEV = 6
HR = 8
WCOL = 32
HIGH = lax.Precision.HIGHEST


def passed_along(x, axis, by):
    peers = lax.axis_size(axis)
    pairs = [(i, i + by) for i in range(peers) if 0 <= i + by < peers]
    return lax.ppermute(x, axis, pairs)


def with_halo(x, sides, width):
    for axis, dim in sides:
        peers, length = (lax.axis_size(axis), x.shape[dim])
        up = [(i, (i + 1) % peers) for i in range(peers - 1)]
        down = [(j, i) for i, j in up]
        last = lax.slice_in_dim(x, length - width, length, axis=dim)
        leading = lax.slice_in_dim(x, 0, width, axis=dim)
        before = lax.ppermute(last, axis, up)
        after = lax.ppermute(leading, axis, down)
        x = jnp.concatenate([before, x, after], axis=dim)
    return x


def shards(feats, row_map, clip_ids, norm_gain, norm_bias, conv_weight, conv_bias):
    local_rows, channels = feats.shape
    n_src = lax.axis_size("src")
    n_frame = lax.axis_size("frame")
    n_tile = lax.axis_size("tile")
    devices = n_src * n_frame * n_tile
    per_pair = local_rows // devices
    group_width = channels // GROUPS
    per_frame = HR * WCOL

    owners = row_map // local_rows
    slot_ids = row_map % local_rows
    frames = clip_ids.shape[0]
    row_frame = (owners // n_tile) % n_frame * FR_DEV + slot_ids // per_frame
    frame_onehot = (row_frame[:, None] == jnp.arange(frames, dtype=jnp.int32)[None, :]).astype(
        jnp.float32
    )
    clip_onehot = (clip_ids[:, None] == jnp.arange(CLIPS, dtype=jnp.int32)[None, :]).astype(
        jnp.float32
    )
    row_onehot = jnp.dot(frame_onehot, clip_onehot)

    local_n = jnp.sum(row_onehot, axis=0) * group_width
    local_s = jnp.sum(
        jnp.dot(row_onehot.T, feats, precision=HIGH).reshape(CLIPS, GROUPS, group_width), axis=2
    )
    local_m = local_s / jnp.maximum(local_n, 1.0)[:, None]
    row_m = jnp.dot(row_onehot, jnp.repeat(local_m, group_width, axis=1), precision=HIGH)
    dev = feats - row_m
    local_m2 = jnp.sum(
        jnp.dot(row_onehot.T, dev * dev, precision=HIGH).reshape(CLIPS, GROUPS, group_width),
        axis=2,
    )

    block = 16
    iota = lax.iota(jnp.int32, local_rows)
    _, sent_slots, ordering = lax.sort((owners, slot_ids, iota), num_keys=1, is_stable=True)
    stats = jnp.concatenate([local_n, local_s.reshape(-1), local_m2.reshape(-1)])
    info = jnp.concatenate(
        [
            sent_slots.astype(jnp.float32).reshape(devices, per_pair),
            jnp.broadcast_to(stats, (devices, stats.shape[0])),
            jnp.zeros((devices, channels - per_pair - stats.shape[0]), jnp.float32),
        ],
        axis=1,
    )
    table = jnp.concatenate([feats, info, jnp.zeros((1, channels), jnp.float32)], axis=0)
    pick = jnp.concatenate(
        [
            ordering.reshape(devices, per_pair),
            local_rows + jnp.arange(devices, dtype=jnp.int32)[:, None],
            jnp.full((devices, block - per_pair - 1), local_rows + devices, jnp.int32),
        ],
        axis=1,
    )
    payload = table[pick.reshape(-1)].reshape(devices, block, channels)
    arrived = lax.all_to_all(
        payload, ("src", "frame", "tile"), split_axis=0, concat_axis=0, tiled=True
    )

    info = arrived[:, per_pair, :]
    targets = info[:, :per_pair].reshape(-1).astype(jnp.int32)
    part_n = info[:, per_pair : per_pair + CLIPS]
    base = per_pair + CLIPS
    part_s = info[:, base : base + CLIPS * GROUPS].reshape(devices, CLIPS, GROUPS)
    part_m2 = info[:, base + CLIPS * GROUPS : base + 2 * CLIPS * GROUPS].reshape(
        devices, CLIPS, GROUPS
    )
    total_n = jnp.sum(part_n, axis=0)
    clip_mean = jnp.sum(part_s, axis=0) / total_n[:, None]
    part_m = part_s / jnp.maximum(part_n, 1.0)[:, :, None]
    spread = part_m - clip_mean[None]
    clip_m2 = jnp.sum(part_m2, axis=0) + jnp.sum(part_n[:, :, None] * spread * spread, axis=0)
    clip_var = clip_m2 / total_n[:, None]

    arrival_row = (iota // per_pair) * block + iota % per_pair
    _, gather_rows = lax.sort((targets, arrival_row), num_keys=1)
    features = arrived.reshape(-1, channels)[gather_rows].reshape(FR_DEV, HR, WCOL, channels)

    first_frame = lax.axis_index("frame") * FR_DEV
    padded_ids = jnp.concatenate([jnp.full((2,), -1, jnp.int32), clip_ids])
    window_ids = lax.dynamic_slice_in_dim(padded_ids, first_frame, FR_DEV + 2)
    own_ids = window_ids[2:]
    onehot = (own_ids[:, None] == jnp.arange(CLIPS, dtype=jnp.int32)[None, :]).astype(jnp.float32)
    shaped = features.reshape(FR_DEV, per_frame, GROUPS, group_width)
    frame_mean = jnp.dot(onehot, clip_mean, precision=HIGH)
    centred = shaped - frame_mean[:, None, :, None]
    inverse_std = 1.0 / jnp.sqrt(clip_var + 1e-06)
    frame_inv = jnp.dot(onehot, inverse_std, precision=HIGH)
    normed = (centred * frame_inv[:, None, :, None]).reshape(FR_DEV, HR, WCOL, channels)
    activated = jax.nn.silu(normed * norm_gain + norm_bias).astype(jnp.bfloat16)
    previous = passed_along(activated[FR_DEV - 2 :], "frame", 1)
    extended = jnp.concatenate([previous, activated], axis=0)
    padded = with_halo(extended, (("tile", 1), ("src", 2)), 1)
    widened = jnp.concatenate([padded[:, :, e : e + WCOL] for e in range(3)], axis=-1)
    validity = jnp.stack(
        [(window_ids[a : a + FR_DEV] == own_ids).astype(jnp.int32) for a in range(3)]
    ).reshape(-1)
    weights = conv_weight.reshape(9, 3 * channels, channels)
    return causal_conv(validity, widened, weights, features, conv_bias.reshape(1, channels))


def conv_kernel(valid_ref, x_ref, w_ref, f_ref, b_ref, o_ref, acc_ref):
    tap_time = pl.program_id(0)
    tap_high = pl.program_id(1)

    @pl.when((tap_time == 0) & (tap_high == 0))
    def _():
        acc_ref[...] = jnp.zeros_like(acc_ref)

    for t in range(FR_DEV):

        @pl.when(valid_ref[tap_time * FR_DEV + t] != 0)
        def _():
            lhs = x_ref[tap_time + t, pl.ds(tap_high, HR)].reshape(HR * WCOL, -1)
            acc_ref[t] += jnp.dot(lhs, w_ref[0], preferred_element_type=jnp.float32)

    @pl.when((tap_time == 2) & (tap_high == 2))
    def _():
        conv_sum = acc_ref[...].reshape(o_ref.shape)
        o_ref[...] = ((f_ref[...] + conv_sum) + b_ref[...]).astype(o_ref.dtype)


def causal_conv(validity, widened, weights, features, bias):
    frames, high, wide, channels = features.shape
    whole = lambda *shape: pl.BlockSpec(
        shape, lambda a, b, v: (0,) * len(shape), pipeline_mode=pl.Buffered(1)
    )
    return pl.pallas_call(
        conv_kernel,
        grid_spec=pltpu.PrefetchScalarGridSpec(
            num_scalar_prefetch=1,
            grid=(3, 3),
            in_specs=[
                whole(*widened.shape),
                pl.BlockSpec((1,) + weights.shape[1:], lambda a, b, v: (a * 3 + b, 0, 0)),
                whole(*features.shape),
                whole(*bias.shape),
            ],
            out_specs=pl.BlockSpec(features.shape, lambda a, b, v: (0, 0, 0, 0)),
            scratch_shapes=[pltpu.VMEM((frames, high * wide, channels), jnp.float32)],
        ),
        out_shape=jax.ShapeDtypeStruct(features.shape, jnp.bfloat16),
        compiler_params=pltpu.CompilerParams(
            dimension_semantics=("arbitrary", "arbitrary"), vmem_limit_bytes=60 * 1024 * 1024
        ),
    )(validity, widened, weights, features, bias)


def solution(mesh):
    placed = (
        P(("src", "frame", "tile"), None),
        P(("src", "frame", "tile")),
        P(),
        P(),
        P(),
        P(),
        P(),
    )
    return jax.shard_map(
        shards,
        mesh=mesh,
        in_specs=placed,
        out_specs=P("frame", "tile", "src", None),
        check_vma=False,
    )
```

```python
import jax
import jax.numpy as jnp
from jax import lax
from jax.experimental import pallas as pl
from jax.experimental.pallas import tpu as pltpu
from jax.sharding import PartitionSpec as P

GROUPS = 32
CLIPS = 4
FR_DEV = 6
HR = 8
WCOL = 32
HIGH = lax.Precision.HIGHEST


def passed_along(x, axis, by):
    peers = lax.axis_size(axis)
    pairs = [(i, i + by) for i in range(peers) if 0 <= i + by < peers]
    return lax.ppermute(x, axis, pairs)


def with_halo(x, sides, width):
    for axis, dim in sides:
        peers, length = (lax.axis_size(axis), x.shape[dim])
        up = [(i, (i + 1) % peers) for i in range(peers - 1)]
        down = [(j, i) for i, j in up]
        last = lax.slice_in_dim(x, length - width, length, axis=dim)
        leading = lax.slice_in_dim(x, 0, width, axis=dim)
        before = lax.ppermute(last, axis, up)
        after = lax.ppermute(leading, axis, down)
        x = jnp.concatenate([before, x, after], axis=dim)
    return x


def shards(feats, row_map, clip_ids, norm_gain, norm_bias, conv_weight, conv_bias):
    local_rows, channels = feats.shape
    n_src = lax.axis_size("src")
    n_frame = lax.axis_size("frame")
    n_tile = lax.axis_size("tile")
    devices = n_src * n_frame * n_tile
    per_pair = local_rows // devices
    group_width = channels // GROUPS
    per_frame = HR * WCOL

    owners = row_map // local_rows
    slot_ids = row_map % local_rows
    frames = clip_ids.shape[0]
    row_frame = (owners // n_tile) % n_frame * FR_DEV + slot_ids // per_frame
    frame_onehot = (row_frame[:, None] == jnp.arange(frames, dtype=jnp.int32)[None, :]).astype(
        jnp.float32
    )
    clip_onehot = (clip_ids[:, None] == jnp.arange(CLIPS, dtype=jnp.int32)[None, :]).astype(
        jnp.float32
    )
    row_onehot = jnp.dot(frame_onehot, clip_onehot)

    clip_mask = row_onehot.T[:, :, None]
    local_n = jnp.sum(row_onehot, axis=0) * group_width
    local_s = jnp.sum(
        jnp.sum(feats[None] * clip_mask, axis=1).reshape(CLIPS, GROUPS, group_width), axis=2
    )
    local_m = local_s / jnp.maximum(local_n, 1.0)[:, None]
    wide_m = jnp.repeat(local_m, group_width, axis=1)
    row_m = jnp.sum(clip_mask * wide_m[:, None, :], axis=0)
    dev = feats - row_m
    local_m2 = jnp.sum(
        jnp.sum((dev * dev)[None] * clip_mask, axis=1).reshape(CLIPS, GROUPS, group_width),
        axis=2,
    )

    block = 16
    iota = lax.iota(jnp.int32, local_rows)
    _, sent_slots, ordering = lax.sort((owners, slot_ids, iota), num_keys=1, is_stable=True)
    stats = jnp.concatenate([local_n, local_s.reshape(-1), local_m2.reshape(-1)])
    info = jnp.concatenate(
        [
            sent_slots.astype(jnp.float32).reshape(devices, per_pair),
            jnp.broadcast_to(stats, (devices, stats.shape[0])),
            jnp.zeros((devices, channels - per_pair - stats.shape[0]), jnp.float32),
        ],
        axis=1,
    )
    pick = jnp.concatenate(
        [ordering.reshape(devices, per_pair), jnp.zeros((devices, block - per_pair), jnp.int32)],
        axis=1,
    )
    payload = feats[pick.reshape(-1)].reshape(devices, block, channels)
    payload = lax.dynamic_update_slice(payload, info[:, None, :], (0, per_pair, 0))
    arrived = lax.all_to_all(
        payload, ("src", "frame", "tile"), split_axis=0, concat_axis=0, tiled=True
    )

    info = arrived[:, per_pair, :]
    targets = info[:, :per_pair].reshape(-1).astype(jnp.int32)
    part_n = info[:, per_pair : per_pair + CLIPS]
    base = per_pair + CLIPS
    part_s = info[:, base : base + CLIPS * GROUPS].reshape(devices, CLIPS, GROUPS)
    part_m2 = info[:, base + CLIPS * GROUPS : base + 2 * CLIPS * GROUPS].reshape(
        devices, CLIPS, GROUPS
    )
    total_n = jnp.sum(part_n, axis=0)
    clip_mean = jnp.sum(part_s, axis=0) / total_n[:, None]
    part_m = part_s / jnp.maximum(part_n, 1.0)[:, :, None]
    spread = part_m - clip_mean[None]
    clip_m2 = jnp.sum(part_m2, axis=0) + jnp.sum(part_n[:, :, None] * spread * spread, axis=0)
    clip_var = clip_m2 / total_n[:, None]

    arrival_row = (iota // per_pair) * block + iota % per_pair
    _, gather_rows = lax.sort((targets, arrival_row), num_keys=1)
    features = arrived.reshape(-1, channels)[gather_rows].reshape(FR_DEV, HR, WCOL, channels)

    first_frame = lax.axis_index("frame") * FR_DEV
    padded_ids = jnp.concatenate([jnp.full((2,), -1, jnp.int32), clip_ids])
    window_ids = lax.dynamic_slice_in_dim(padded_ids, first_frame, FR_DEV + 2)
    own_ids = window_ids[2:]
    onehot = (own_ids[:, None] == jnp.arange(CLIPS, dtype=jnp.int32)[None, :]).astype(jnp.float32)
    shaped = features.reshape(FR_DEV, per_frame, GROUPS, group_width)
    frame_mean = jnp.dot(onehot, clip_mean, precision=HIGH)
    centred = shaped - frame_mean[:, None, :, None]
    inverse_std = 1.0 / jnp.sqrt(clip_var + 1e-06)
    frame_inv = jnp.dot(onehot, inverse_std, precision=HIGH)
    normed = (centred * frame_inv[:, None, :, None]).reshape(FR_DEV, HR, WCOL, channels)
    activated = jax.nn.silu(normed * norm_gain + norm_bias).astype(jnp.bfloat16)
    zero_col = jnp.zeros((FR_DEV, HR + 2, 1, channels), jnp.bfloat16)
    high_padded = with_halo(activated, (("tile", 1),), 1)
    n_wide = lax.axis_size("src")
    up = [(i, i + 1) for i in range(n_wide - 1)]
    left = lax.ppermute(high_padded[:, :, WCOL - 1 :], "src", up)
    right = lax.ppermute(high_padded[:, :, :1], "src", [(j, i) for i, j in up])
    own_wide = widen(high_padded, zero_col, left, right)
    sent_prev = jnp.concatenate(
        [high_padded[FR_DEV - 2 :], left[FR_DEV - 2 :], right[FR_DEV - 2 :]], axis=2
    )
    prev = passed_along(sent_prev, "frame", 1)
    prev_wide = widen(prev[:, :, :WCOL], zero_col[:2], prev[:, :, WCOL : WCOL + 1], prev[:, :, WCOL + 1 :])

    validity = jnp.stack(
        [(window_ids[a : a + FR_DEV] == own_ids).astype(jnp.int32) for a in range(3)]
    )
    reach = jnp.arange(3)[:, None] + jnp.arange(FR_DEV)[None, :]
    own_valid = jnp.where(reach >= 2, validity, 0).reshape(-1)
    prev_valid = jnp.where(reach < 2, validity, 0)[:2, :2].reshape(-1)
    weights = conv_weight.reshape(9, 3 * channels, channels)
    partial_sum = own_conv(own_valid, own_wide, weights)
    return prev_conv(
        prev_valid, prev_wide, weights, partial_sum, features, conv_bias.reshape(1, channels)
    )


def widen(block, zero_col, left, right):
    shifted_in = jnp.concatenate([zero_col, block[:, :, : WCOL - 1]], axis=2)
    shifted_out = jnp.concatenate([block[:, :, 1:], zero_col], axis=2)
    wide = jnp.concatenate([shifted_in, block, shifted_out], axis=-1)
    channels = block.shape[-1]
    wide = lax.dynamic_update_slice(wide, left, (0, 0, 0, 0))
    return lax.dynamic_update_slice(wide, right, (0, 0, WCOL - 1, 2 * channels))


def own_kernel(valid_ref, x_ref, w_ref, acc_ref):
    tap_time = pl.program_id(0)
    tap_high = pl.program_id(1)

    @pl.when((tap_time == 0) & (tap_high == 0))
    def _():
        acc_ref[...] = jnp.zeros_like(acc_ref)

    for t in range(FR_DEV):

        @pl.when(valid_ref[tap_time * FR_DEV + t] != 0)
        def _():
            frame = jnp.maximum(tap_time + t - 2, 0)
            lhs = x_ref[frame, pl.ds(tap_high, HR)].reshape(HR * WCOL, -1)
            acc_ref[t] += jnp.dot(lhs, w_ref[0], preferred_element_type=jnp.float32)


def own_conv(validity, wide, weights):
    frames = wide.shape[0]
    channels = weights.shape[-1]
    return pl.pallas_call(
        own_kernel,
        grid_spec=pltpu.PrefetchScalarGridSpec(
            num_scalar_prefetch=1,
            grid=(3, 3),
            in_specs=[
                pl.BlockSpec(wide.shape, lambda a, b, v: (0, 0, 0, 0), pipeline_mode=pl.Buffered(1)),
                pl.BlockSpec((1,) + weights.shape[1:], lambda a, b, v: (a * 3 + b, 0, 0)),
            ],
            out_specs=pl.BlockSpec((frames, HR * WCOL, channels), lambda a, b, v: (0, 0, 0)),
        ),
        out_shape=jax.ShapeDtypeStruct((frames, HR * WCOL, channels), jnp.float32),
        compiler_params=pltpu.CompilerParams(
            dimension_semantics=("arbitrary", "arbitrary"), vmem_limit_bytes=60 * 1024 * 1024
        ),
    )(validity, wide, weights)


def prev_kernel(valid_ref, x_ref, w_ref, part_ref, f_ref, b_ref, o_ref, acc_ref):
    tap_time = pl.program_id(0)
    tap_high = pl.program_id(1)

    @pl.when((tap_time == 0) & (tap_high == 0))
    def _():
        acc_ref[...] = part_ref[...]

    for t in range(2):

        @pl.when(valid_ref[tap_time * 2 + t] != 0)
        def _():
            frame = jnp.minimum(tap_time + t, 1)
            lhs = x_ref[frame, pl.ds(tap_high, HR)].reshape(HR * WCOL, -1)
            acc_ref[t] += jnp.dot(lhs, w_ref[0], preferred_element_type=jnp.float32)

    @pl.when((tap_time == 1) & (tap_high == 2))
    def _():
        conv_sum = acc_ref[...].reshape(o_ref.shape)
        o_ref[...] = ((f_ref[...] + conv_sum) + b_ref[...]).astype(o_ref.dtype)


def prev_conv(validity, wide, weights, partial_sum, features, bias):
    whole = lambda shape: pl.BlockSpec(
        shape, lambda a, b, v: (0,) * len(shape), pipeline_mode=pl.Buffered(1)
    )
    return pl.pallas_call(
        prev_kernel,
        grid_spec=pltpu.PrefetchScalarGridSpec(
            num_scalar_prefetch=1,
            grid=(2, 3),
            in_specs=[
                whole(wide.shape),
                pl.BlockSpec((1,) + weights.shape[1:], lambda a, b, v: (a * 3 + b, 0, 0)),
                whole(partial_sum.shape),
                whole(features.shape),
                whole(bias.shape),
            ],
            out_specs=pl.BlockSpec(features.shape, lambda a, b, v: (0, 0, 0, 0)),
            scratch_shapes=[pltpu.VMEM(partial_sum.shape, jnp.float32)],
        ),
        out_shape=jax.ShapeDtypeStruct(features.shape, jnp.bfloat16),
        compiler_params=pltpu.CompilerParams(
            dimension_semantics=("arbitrary", "arbitrary"), vmem_limit_bytes=60 * 1024 * 1024
        ),
    )(validity, wide, weights, partial_sum, features, bias)


def solution(mesh):
    placed = (
        P(("src", "frame", "tile"), None),
        P(("src", "frame", "tile")),
        P(),
        P(),
        P(),
        P(),
        P(),
    )
    return jax.shard_map(
        shards,
        mesh=mesh,
        in_specs=placed,
        out_specs=P("frame", "tile", "src", None),
        check_vma=False,
    )
```

```python
import jax
import jax.numpy as jnp
from jax import lax
from jax.experimental import pallas as pl
from jax.experimental.pallas import tpu as pltpu
from jax.sharding import PartitionSpec as P

GROUPS = 32
CLIPS = 4
FR_DEV = 6
HR = 8
WCOL = 32
HIGH = lax.Precision.HIGHEST


def passed_along(x, axis, by):
    peers = lax.axis_size(axis)
    pairs = [(i, i + by) for i in range(peers) if 0 <= i + by < peers]
    return lax.ppermute(x, axis, pairs)


def with_halo(x, sides, width):
    for axis, dim in sides:
        peers, length = (lax.axis_size(axis), x.shape[dim])
        up = [(i, (i + 1) % peers) for i in range(peers - 1)]
        down = [(j, i) for i, j in up]
        last = lax.slice_in_dim(x, length - width, length, axis=dim)
        leading = lax.slice_in_dim(x, 0, width, axis=dim)
        before = lax.ppermute(last, axis, up)
        after = lax.ppermute(leading, axis, down)
        x = jnp.concatenate([before, x, after], axis=dim)
    return x


def shards(feats, row_map, clip_ids, norm_gain, norm_bias, conv_weight, conv_bias):
    local_rows, channels = feats.shape
    n_src = lax.axis_size("src")
    n_frame = lax.axis_size("frame")
    n_tile = lax.axis_size("tile")
    devices = n_src * n_frame * n_tile
    per_pair = local_rows // devices
    group_width = channels // GROUPS
    per_frame = HR * WCOL

    owners = row_map // local_rows
    slot_ids = row_map % local_rows
    frames = clip_ids.shape[0]
    row_frame = (owners // n_tile) % n_frame * FR_DEV + slot_ids // per_frame
    frame_onehot = (row_frame[:, None] == jnp.arange(frames, dtype=jnp.int32)[None, :]).astype(
        jnp.float32
    )
    clip_onehot = (clip_ids[:, None] == jnp.arange(CLIPS, dtype=jnp.int32)[None, :]).astype(
        jnp.float32
    )
    row_onehot = jnp.dot(frame_onehot, clip_onehot)

    clip_mask = row_onehot.T[:, :, None]
    local_n = jnp.sum(row_onehot, axis=0) * group_width
    local_s = jnp.sum(
        jnp.sum(feats[None] * clip_mask, axis=1).reshape(CLIPS, GROUPS, group_width), axis=2
    )
    local_m = local_s / jnp.maximum(local_n, 1.0)[:, None]
    wide_m = jnp.repeat(local_m, group_width, axis=1)
    row_m = jnp.sum(clip_mask * wide_m[:, None, :], axis=0)
    dev = feats - row_m
    local_m2 = jnp.sum(
        jnp.sum((dev * dev)[None] * clip_mask, axis=1).reshape(CLIPS, GROUPS, group_width),
        axis=2,
    )

    block = 16
    iota = lax.iota(jnp.int32, local_rows)
    _, sent_slots, ordering = lax.sort((owners, slot_ids, iota), num_keys=1, is_stable=True)
    stats = jnp.concatenate([local_n, local_s.reshape(-1), local_m2.reshape(-1)])
    info = jnp.concatenate(
        [
            sent_slots.astype(jnp.float32).reshape(devices, per_pair),
            jnp.broadcast_to(stats, (devices, stats.shape[0])),
            jnp.zeros((devices, channels - per_pair - stats.shape[0]), jnp.float32),
        ],
        axis=1,
    )
    pick = jnp.concatenate(
        [ordering.reshape(devices, per_pair), jnp.zeros((devices, block - per_pair), jnp.int32)],
        axis=1,
    )
    payload = feats[pick.reshape(-1)].reshape(devices, block, channels)
    payload = lax.dynamic_update_slice(payload, info[:, None, :], (0, per_pair, 0))
    arrived = lax.all_to_all(
        payload, ("src", "frame", "tile"), split_axis=0, concat_axis=0, tiled=True
    )

    info = arrived[:, per_pair, :]
    targets = info[:, :per_pair].reshape(-1).astype(jnp.int32)
    part_n = info[:, per_pair : per_pair + CLIPS]
    base = per_pair + CLIPS
    part_s = info[:, base : base + CLIPS * GROUPS].reshape(devices, CLIPS, GROUPS)
    part_m2 = info[:, base + CLIPS * GROUPS : base + 2 * CLIPS * GROUPS].reshape(
        devices, CLIPS, GROUPS
    )
    total_n = jnp.sum(part_n, axis=0)
    clip_mean = jnp.sum(part_s, axis=0) / total_n[:, None]
    part_m = part_s / jnp.maximum(part_n, 1.0)[:, :, None]
    spread = part_m - clip_mean[None]
    clip_m2 = jnp.sum(part_m2, axis=0) + jnp.sum(part_n[:, :, None] * spread * spread, axis=0)
    clip_var = clip_m2 / total_n[:, None]

    arrival_row = (iota // per_pair) * block + iota % per_pair
    _, gather_rows = lax.sort((targets, arrival_row), num_keys=1)
    features = arrived.reshape(-1, channels)[gather_rows].reshape(FR_DEV, HR, WCOL, channels)

    first_frame = lax.axis_index("frame") * FR_DEV
    padded_ids = jnp.concatenate([jnp.full((2,), -1, jnp.int32), clip_ids])
    window_ids = lax.dynamic_slice_in_dim(padded_ids, first_frame, FR_DEV + 2)
    own_ids = window_ids[2:]
    onehot = (own_ids[:, None] == jnp.arange(CLIPS, dtype=jnp.int32)[None, :]).astype(jnp.float32)
    shaped = features.reshape(FR_DEV, per_frame, GROUPS, group_width)
    frame_mean = jnp.dot(onehot, clip_mean, precision=HIGH)
    centred = shaped - frame_mean[:, None, :, None]
    inverse_std = 1.0 / jnp.sqrt(clip_var + 1e-06)
    frame_inv = jnp.dot(onehot, inverse_std, precision=HIGH)
    normed = (centred * frame_inv[:, None, :, None]).reshape(FR_DEV, HR, WCOL, channels)
    activated = jax.nn.silu(normed * norm_gain + norm_bias).astype(jnp.bfloat16)
    high_padded = with_halo(activated, (("tile", 1),), 1)
    n_wide = lax.axis_size("src")
    up = [(i, i + 1) for i in range(n_wide - 1)]
    left = lax.ppermute(high_padded[:, :, WCOL - 1 :], "src", up)
    right = lax.ppermute(high_padded[:, :, :1], "src", [(j, i) for i, j in up])
    own_wide = widen(high_padded, left, right)
    sent_prev = jnp.concatenate(
        [high_padded[FR_DEV - 2 :], left[FR_DEV - 2 :], right[FR_DEV - 2 :]], axis=2
    )
    prev = passed_along(sent_prev, "frame", 1)
    prev_wide = widen(prev[:, :, :WCOL], prev[:, :, WCOL : WCOL + 1], prev[:, :, WCOL + 1 :])

    validity = jnp.stack(
        [(window_ids[a : a + FR_DEV] == own_ids).astype(jnp.int32) for a in range(3)]
    )
    reach = jnp.arange(3)[:, None] + jnp.arange(FR_DEV)[None, :]
    own_valid = jnp.where(reach >= 2, validity, 0).reshape(-1)
    prev_valid = jnp.where(reach < 2, validity, 0)[:2, :2].reshape(-1)
    weights = conv_weight.reshape(9, 3 * channels, channels)
    bias = conv_bias.reshape(1, channels)
    decoded, early = own_conv(own_valid, own_wide, weights, features, bias)
    return prev_conv(prev_valid, prev_wide, weights, early, decoded)


def widen(block, left, right):
    shifted_in = jnp.concatenate([left, block[:, :, : WCOL - 1]], axis=2)
    shifted_out = jnp.concatenate([block[:, :, 1:], right], axis=2)
    return jnp.concatenate([shifted_in, block, shifted_out], axis=-1)


def own_kernel(valid_ref, x_ref, w_ref, b_ref, f_hbm, o_ref, early_ref, f_ref, acc_ref, sem):
    tap_time = pl.program_id(0)
    tap_high = pl.program_id(1)
    fetch = pltpu.make_async_copy(f_hbm, f_ref, sem)

    @pl.when((tap_time == 0) & (tap_high == 0))
    def _():
        fetch.start()
        acc_ref[...] = jnp.zeros_like(acc_ref)

    for t in range(FR_DEV):

        @pl.when(valid_ref[tap_time * FR_DEV + t] != 0)
        def _():
            frame = jnp.maximum(tap_time + t - 2, 0)
            lhs = x_ref[frame, pl.ds(tap_high, HR)].reshape(HR * WCOL, -1)
            acc_ref[t] += jnp.dot(lhs, w_ref[0], preferred_element_type=jnp.float32)

    @pl.when((tap_time == 2) & (tap_high == 2))
    def _():
        fetch.wait()
        for t in range(FR_DEV):
            total = (f_ref[t] + acc_ref[t].reshape(HR, WCOL, -1)) + b_ref[...]
            if t < 2:
                early_ref[t] = total
            else:
                o_ref[t] = total.astype(o_ref.dtype)


def own_conv(validity, wide, weights, features, bias):
    return pl.pallas_call(
        own_kernel,
        grid_spec=pltpu.PrefetchScalarGridSpec(
            num_scalar_prefetch=1,
            grid=(3, 3),
            in_specs=[
                pl.BlockSpec(wide.shape, lambda a, b, v: (0, 0, 0, 0), pipeline_mode=pl.Buffered(1)),
                pl.BlockSpec((1,) + weights.shape[1:], lambda a, b, v: (a * 3 + b, 0, 0)),
                pl.BlockSpec(bias.shape, lambda a, b, v: (0, 0), pipeline_mode=pl.Buffered(1)),
                pl.BlockSpec(memory_space=pl.ANY),
            ],
            out_specs=[
                pl.BlockSpec(features.shape, lambda a, b, v: (0, 0, 0, 0)),
                pl.BlockSpec((2,) + features.shape[1:], lambda a, b, v: (0, 0, 0, 0)),
            ],
            scratch_shapes=[
                pltpu.VMEM(features.shape, jnp.float32),
                pltpu.VMEM((features.shape[0], HR * WCOL, features.shape[-1]), jnp.float32),
                pltpu.SemaphoreType.DMA(()),
            ],
        ),
        out_shape=[
            jax.ShapeDtypeStruct(features.shape, jnp.bfloat16),
            jax.ShapeDtypeStruct((2,) + features.shape[1:], jnp.float32),
        ],
        compiler_params=pltpu.CompilerParams(
            dimension_semantics=("arbitrary", "arbitrary"), vmem_limit_bytes=60 * 1024 * 1024
        ),
    )(validity, wide, weights, bias, features)


def prev_kernel(valid_ref, x_ref, w_ref, early_ref, whole_ref, o_ref, acc_ref):
    del whole_ref
    tap_time = pl.program_id(0)
    tap_high = pl.program_id(1)

    @pl.when((tap_time == 0) & (tap_high == 0))
    def _():
        acc_ref[...] = jnp.zeros_like(acc_ref)

    for t in range(2):

        @pl.when(valid_ref[tap_time * 2 + t] != 0)
        def _():
            frame = jnp.minimum(tap_time + t, 1)
            lhs = x_ref[frame, pl.ds(tap_high, HR)].reshape(HR * WCOL, -1)
            acc_ref[t] += jnp.dot(lhs, w_ref[0], preferred_element_type=jnp.float32)

    @pl.when((tap_time == 1) & (tap_high == 2))
    def _():
        for t in range(2):
            total = early_ref[t] + acc_ref[t].reshape(HR, WCOL, -1)
            o_ref[t] = total.astype(o_ref.dtype)


def prev_conv(validity, wide, weights, early, decoded):
    return pl.pallas_call(
        prev_kernel,
        grid_spec=pltpu.PrefetchScalarGridSpec(
            num_scalar_prefetch=1,
            grid=(2, 3),
            in_specs=[
                pl.BlockSpec(wide.shape, lambda a, b, v: (0, 0, 0, 0), pipeline_mode=pl.Buffered(1)),
                pl.BlockSpec((1,) + weights.shape[1:], lambda a, b, v: (a * 3 + b, 0, 0)),
                pl.BlockSpec(early.shape, lambda a, b, v: (0, 0, 0, 0), pipeline_mode=pl.Buffered(1)),
                pl.BlockSpec(memory_space=pl.ANY),
            ],
            out_specs=pl.BlockSpec(early.shape, lambda a, b, v: (0, 0, 0, 0)),
            scratch_shapes=[pltpu.VMEM((2, HR * WCOL, early.shape[-1]), jnp.float32)],
        ),
        out_shape=jax.ShapeDtypeStruct(decoded.shape, decoded.dtype),
        input_output_aliases={4: 0},
        compiler_params=pltpu.CompilerParams(
            dimension_semantics=("arbitrary", "arbitrary"), vmem_limit_bytes=60 * 1024 * 1024
        ),
    )(validity, wide, weights, early, decoded)


def solution(mesh):
    placed = (
        P(("src", "frame", "tile"), None),
        P(("src", "frame", "tile")),
        P(),
        P(),
        P(),
        P(),
        P(),
    )
    return jax.shard_map(
        shards,
        mesh=mesh,
        in_specs=placed,
        out_specs=P("frame", "tile", "src", None),
        check_vma=False,
    )
```

```python
import jax
import jax.numpy as jnp
from jax import lax
from jax.experimental import pallas as pl
from jax.experimental.pallas import tpu as pltpu
from jax.sharding import PartitionSpec as P

GROUPS = 32
CLIPS = 4
FR_DEV = 6
HR = 8
WCOL = 32
HIGH = lax.Precision.HIGHEST


def passed_along(x, axis, by):
    peers = lax.axis_size(axis)
    pairs = [(i, i + by) for i in range(peers) if 0 <= i + by < peers]
    return lax.ppermute(x, axis, pairs)


def with_halo(x, sides, width):
    for axis, dim in sides:
        peers, length = (lax.axis_size(axis), x.shape[dim])
        up = [(i, (i + 1) % peers) for i in range(peers - 1)]
        down = [(j, i) for i, j in up]
        last = lax.slice_in_dim(x, length - width, length, axis=dim)
        leading = lax.slice_in_dim(x, 0, width, axis=dim)
        before = lax.ppermute(last, axis, up)
        after = lax.ppermute(leading, axis, down)
        x = jnp.concatenate([before, x, after], axis=dim)
    return x


def shards(feats, row_map, clip_ids, norm_gain, norm_bias, conv_weight, conv_bias):
    local_rows, channels = feats.shape
    n_src = lax.axis_size("src")
    n_frame = lax.axis_size("frame")
    n_tile = lax.axis_size("tile")
    devices = n_src * n_frame * n_tile
    per_pair = local_rows // devices
    group_width = channels // GROUPS
    per_frame = HR * WCOL

    owners = row_map // local_rows
    slot_ids = row_map % local_rows
    frames = clip_ids.shape[0]
    row_frame = (owners // n_tile) % n_frame * FR_DEV + slot_ids // per_frame
    frame_onehot = (row_frame[:, None] == jnp.arange(frames, dtype=jnp.int32)[None, :]).astype(
        jnp.float32
    )
    clip_onehot = (clip_ids[:, None] == jnp.arange(CLIPS, dtype=jnp.int32)[None, :]).astype(
        jnp.float32
    )
    row_onehot = jnp.dot(frame_onehot, clip_onehot)

    clip_mask = row_onehot.T[:, :, None]
    local_n = jnp.sum(row_onehot, axis=0) * group_width
    local_s = jnp.sum(
        jnp.sum(feats[None] * clip_mask, axis=1).reshape(CLIPS, GROUPS, group_width), axis=2
    )
    local_m = local_s / jnp.maximum(local_n, 1.0)[:, None]
    wide_m = jnp.repeat(local_m, group_width, axis=1)
    row_m = jnp.sum(clip_mask * wide_m[:, None, :], axis=0)
    dev = feats - row_m
    local_m2 = jnp.sum(
        jnp.sum((dev * dev)[None] * clip_mask, axis=1).reshape(CLIPS, GROUPS, group_width),
        axis=2,
    )

    block = 16
    iota = lax.iota(jnp.int32, local_rows)
    _, sent_slots, ordering = lax.sort((owners, slot_ids, iota), num_keys=1, is_stable=True)
    stats = jnp.concatenate([local_n, local_s.reshape(-1), local_m2.reshape(-1)])
    info = jnp.concatenate(
        [
            sent_slots.astype(jnp.float32).reshape(devices, per_pair),
            jnp.broadcast_to(stats, (devices, stats.shape[0])),
            jnp.zeros((devices, channels - per_pair - stats.shape[0]), jnp.float32),
        ],
        axis=1,
    )
    pick = jnp.concatenate(
        [ordering.reshape(devices, per_pair), jnp.zeros((devices, block - per_pair), jnp.int32)],
        axis=1,
    )
    payload = feats[pick.reshape(-1)].reshape(devices, block, channels)
    payload = lax.dynamic_update_slice(payload, info[:, None, :], (0, per_pair, 0))
    arrived = lax.all_to_all(
        payload, ("src", "frame", "tile"), split_axis=0, concat_axis=0, tiled=True
    )

    info = arrived[:, per_pair, :]
    targets = info[:, :per_pair].reshape(-1).astype(jnp.int32)
    part_n = info[:, per_pair : per_pair + CLIPS]
    base = per_pair + CLIPS
    part_s = info[:, base : base + CLIPS * GROUPS].reshape(devices, CLIPS, GROUPS)
    part_m2 = info[:, base + CLIPS * GROUPS : base + 2 * CLIPS * GROUPS].reshape(
        devices, CLIPS, GROUPS
    )
    total_n = jnp.sum(part_n, axis=0)
    clip_mean = jnp.sum(part_s, axis=0) / total_n[:, None]
    part_m = part_s / jnp.maximum(part_n, 1.0)[:, :, None]
    spread = part_m - clip_mean[None]
    clip_m2 = jnp.sum(part_m2, axis=0) + jnp.sum(part_n[:, :, None] * spread * spread, axis=0)
    clip_var = clip_m2 / total_n[:, None]

    arrival_row = (iota // per_pair) * block + iota % per_pair
    _, gather_rows = lax.sort((targets, arrival_row), num_keys=1)
    features = arrived.reshape(-1, channels)[gather_rows].reshape(FR_DEV, HR, WCOL, channels)

    first_frame = lax.axis_index("frame") * FR_DEV
    padded_ids = jnp.concatenate([jnp.full((2,), -1, jnp.int32), clip_ids])
    window_ids = lax.dynamic_slice_in_dim(padded_ids, first_frame, FR_DEV + 2)
    own_ids = window_ids[2:]
    onehot = (own_ids[:, None] == jnp.arange(CLIPS, dtype=jnp.int32)[None, :]).astype(jnp.float32)
    shaped = features.reshape(FR_DEV, per_frame, GROUPS, group_width)
    frame_mean = jnp.dot(onehot, clip_mean, precision=HIGH)
    centred = shaped - frame_mean[:, None, :, None]
    inverse_std = 1.0 / jnp.sqrt(clip_var + 1e-06)
    frame_inv = jnp.dot(onehot, inverse_std, precision=HIGH)
    normed = (centred * frame_inv[:, None, :, None]).reshape(FR_DEV, HR, WCOL, channels)
    activated = jax.nn.silu(normed * norm_gain + norm_bias).astype(jnp.bfloat16)
    high_padded = with_halo(activated, (("tile", 1),), 1)
    n_wide = lax.axis_size("src")
    up = [(i, i + 1) for i in range(n_wide - 1)]
    left = lax.ppermute(high_padded[:, :, WCOL - 1 :], "src", up)
    right = lax.ppermute(high_padded[:, :, :1], "src", [(j, i) for i, j in up])
    own_wide = widen(high_padded, left, right)
    sent_prev = jnp.concatenate(
        [high_padded[FR_DEV - 2 :], left[FR_DEV - 2 :], right[FR_DEV - 2 :]], axis=2
    )
    prev = passed_along(sent_prev, "frame", 1)
    prev_wide = widen(prev[:, :, :WCOL], prev[:, :, WCOL : WCOL + 1], prev[:, :, WCOL + 1 :])

    validity = jnp.stack(
        [(window_ids[a : a + FR_DEV] == own_ids).astype(jnp.int32) for a in range(3)]
    )
    reach = jnp.arange(3)[:, None] + jnp.arange(FR_DEV)[None, :]
    own_valid = jnp.where(reach >= 2, validity, 0).reshape(-1)
    prev_valid = jnp.where(reach < 2, validity, 0)[:2, :2].reshape(-1)
    weights = conv_weight.reshape(9, 3 * channels, channels)
    bias = conv_bias.reshape(1, channels)
    decoded, early = own_conv(own_valid, own_wide, weights, features, bias)
    return prev_conv(prev_valid, prev_wide, weights, early, decoded)


def widen(block, left, right):
    shifted_in = jnp.concatenate([left, block[:, :, : WCOL - 1]], axis=2)
    shifted_out = jnp.concatenate([block[:, :, 1:], right], axis=2)
    return jnp.concatenate([shifted_in, block, shifted_out], axis=-1)


def own_kernel(valid_ref, x_ref, w_ref, b_ref, f_hbm, o_ref, early_ref, f_ref, acc_ref, sem):
    tap_time = pl.program_id(0)
    tap_high = pl.program_id(1)
    fetch = pltpu.make_async_copy(f_hbm, f_ref, sem)

    @pl.when((tap_time == 0) & (tap_high == 0))
    def _():
        fetch.start()
        acc_ref[...] = jnp.zeros_like(acc_ref)

    for a in range(3):

        @pl.when(tap_time == a)
        def _():
            reach = FR_DEV - 2 + a
            lhs = x_ref[:reach, pl.ds(tap_high, HR)].reshape(reach * HR * WCOL, -1)
            part = jnp.dot(lhs, w_ref[0], preferred_element_type=jnp.float32)
            for j in range(reach):
                t = j + 2 - a
                keep = valid_ref[a * FR_DEV + t].astype(jnp.float32)
                acc_ref[t] += part[j * HR * WCOL : (j + 1) * HR * WCOL] * keep

    @pl.when((tap_time == 2) & (tap_high == 2))
    def _():
        fetch.wait()
        for t in range(FR_DEV):
            total = (f_ref[t] + acc_ref[t].reshape(HR, WCOL, -1)) + b_ref[...]
            if t < 2:
                early_ref[t] = total
            else:
                o_ref[t] = total.astype(o_ref.dtype)


def own_conv(validity, wide, weights, features, bias):
    return pl.pallas_call(
        own_kernel,
        grid_spec=pltpu.PrefetchScalarGridSpec(
            num_scalar_prefetch=1,
            grid=(3, 3),
            in_specs=[
                pl.BlockSpec(wide.shape, lambda a, b, v: (0, 0, 0, 0), pipeline_mode=pl.Buffered(1)),
                pl.BlockSpec((1,) + weights.shape[1:], lambda a, b, v: (a * 3 + b, 0, 0)),
                pl.BlockSpec(bias.shape, lambda a, b, v: (0, 0), pipeline_mode=pl.Buffered(1)),
                pl.BlockSpec(memory_space=pl.ANY),
            ],
            out_specs=[
                pl.BlockSpec(features.shape, lambda a, b, v: (0, 0, 0, 0)),
                pl.BlockSpec((2,) + features.shape[1:], lambda a, b, v: (0, 0, 0, 0)),
            ],
            scratch_shapes=[
                pltpu.VMEM(features.shape, jnp.float32),
                pltpu.VMEM((features.shape[0], HR * WCOL, features.shape[-1]), jnp.float32),
                pltpu.SemaphoreType.DMA(()),
            ],
        ),
        out_shape=[
            jax.ShapeDtypeStruct(features.shape, jnp.bfloat16),
            jax.ShapeDtypeStruct((2,) + features.shape[1:], jnp.float32),
        ],
        compiler_params=pltpu.CompilerParams(
            dimension_semantics=("arbitrary", "arbitrary"), vmem_limit_bytes=60 * 1024 * 1024
        ),
    )(validity, wide, weights, bias, features)


def prev_kernel(valid_ref, x_ref, w_ref, early_ref, whole_ref, o_ref, acc_ref):
    del whole_ref
    tap_time = pl.program_id(0)
    tap_high = pl.program_id(1)

    @pl.when((tap_time == 0) & (tap_high == 0))
    def _():
        acc_ref[...] = jnp.zeros_like(acc_ref)

    for t in range(2):

        @pl.when(valid_ref[tap_time * 2 + t] != 0)
        def _():
            frame = jnp.minimum(tap_time + t, 1)
            lhs = x_ref[frame, pl.ds(tap_high, HR)].reshape(HR * WCOL, -1)
            acc_ref[t] += jnp.dot(lhs, w_ref[0], preferred_element_type=jnp.float32)

    @pl.when((tap_time == 1) & (tap_high == 2))
    def _():
        for t in range(2):
            total = early_ref[t] + acc_ref[t].reshape(HR, WCOL, -1)
            o_ref[t] = total.astype(o_ref.dtype)


def prev_conv(validity, wide, weights, early, decoded):
    return pl.pallas_call(
        prev_kernel,
        grid_spec=pltpu.PrefetchScalarGridSpec(
            num_scalar_prefetch=1,
            grid=(2, 3),
            in_specs=[
                pl.BlockSpec(wide.shape, lambda a, b, v: (0, 0, 0, 0), pipeline_mode=pl.Buffered(1)),
                pl.BlockSpec((1,) + weights.shape[1:], lambda a, b, v: (a * 3 + b, 0, 0)),
                pl.BlockSpec(early.shape, lambda a, b, v: (0, 0, 0, 0), pipeline_mode=pl.Buffered(1)),
                pl.BlockSpec(memory_space=pl.ANY),
            ],
            out_specs=pl.BlockSpec(early.shape, lambda a, b, v: (0, 0, 0, 0)),
            scratch_shapes=[pltpu.VMEM((2, HR * WCOL, early.shape[-1]), jnp.float32)],
        ),
        out_shape=jax.ShapeDtypeStruct(decoded.shape, decoded.dtype),
        input_output_aliases={4: 0},
        compiler_params=pltpu.CompilerParams(
            dimension_semantics=("arbitrary", "arbitrary"), vmem_limit_bytes=60 * 1024 * 1024
        ),
    )(validity, wide, weights, early, decoded)


def solution(mesh):
    placed = (
        P(("src", "frame", "tile"), None),
        P(("src", "frame", "tile")),
        P(),
        P(),
        P(),
        P(),
        P(),
    )
    return jax.shard_map(
        shards,
        mesh=mesh,
        in_specs=placed,
        out_specs=P("frame", "tile", "src", None),
        check_vma=False,
    )
```

```python
import jax
import jax.numpy as jnp
from jax import lax
from jax.experimental import pallas as pl
from jax.experimental.pallas import tpu as pltpu
from jax.sharding import PartitionSpec as P

GROUPS = 32
CLIPS = 4
FR_DEV = 6
HR = 8
WCOL = 32
HIGH = lax.Precision.HIGHEST


def passed_along(x, axis, by):
    peers = lax.axis_size(axis)
    pairs = [(i, i + by) for i in range(peers) if 0 <= i + by < peers]
    return lax.ppermute(x, axis, pairs)


def with_halo(x, sides, width):
    for axis, dim in sides:
        peers, length = (lax.axis_size(axis), x.shape[dim])
        up = [(i, (i + 1) % peers) for i in range(peers - 1)]
        down = [(j, i) for i, j in up]
        last = lax.slice_in_dim(x, length - width, length, axis=dim)
        leading = lax.slice_in_dim(x, 0, width, axis=dim)
        before = lax.ppermute(last, axis, up)
        after = lax.ppermute(leading, axis, down)
        x = jnp.concatenate([before, x, after], axis=dim)
    return x


def shards(feats, row_map, clip_ids, norm_gain, norm_bias, conv_weight, conv_bias):
    local_rows, channels = feats.shape
    n_src = lax.axis_size("src")
    n_frame = lax.axis_size("frame")
    n_tile = lax.axis_size("tile")
    devices = n_src * n_frame * n_tile
    per_pair = local_rows // devices
    group_width = channels // GROUPS
    per_frame = HR * WCOL

    owners = row_map // local_rows
    slot_ids = row_map % local_rows
    frames = clip_ids.shape[0]
    row_frame = (owners // n_tile) % n_frame * FR_DEV + slot_ids // per_frame
    frame_onehot = (row_frame[:, None] == jnp.arange(frames, dtype=jnp.int32)[None, :]).astype(
        jnp.float32
    )
    clip_onehot = (clip_ids[:, None] == jnp.arange(CLIPS, dtype=jnp.int32)[None, :]).astype(
        jnp.float32
    )
    row_onehot = jnp.dot(frame_onehot, clip_onehot)

    clip_mask = row_onehot.T[:, :, None]
    local_n = jnp.sum(row_onehot, axis=0) * group_width
    local_s = jnp.sum(
        jnp.sum(feats[None] * clip_mask, axis=1).reshape(CLIPS, GROUPS, group_width), axis=2
    )
    local_m = local_s / jnp.maximum(local_n, 1.0)[:, None]
    wide_m = jnp.repeat(local_m, group_width, axis=1)
    row_m = jnp.sum(clip_mask * wide_m[:, None, :], axis=0)
    dev = feats - row_m
    local_m2 = jnp.sum(
        jnp.sum((dev * dev)[None] * clip_mask, axis=1).reshape(CLIPS, GROUPS, group_width),
        axis=2,
    )

    iota = lax.iota(jnp.int32, local_rows)
    _, sent_slots, ordering = lax.sort((owners, slot_ids, iota), num_keys=1, is_stable=True)
    stats = jnp.concatenate([local_n, local_s.reshape(-1), local_m2.reshape(-1)])
    info = jnp.concatenate(
        [
            sent_slots.astype(jnp.float32).reshape(devices, per_pair),
            jnp.broadcast_to(stats, (devices, stats.shape[0])),
            jnp.zeros((devices, channels - per_pair - stats.shape[0]), jnp.float32),
        ],
        axis=1,
    )
    gathered = feats[ordering].reshape(devices, per_pair, channels)
    payload = jnp.concatenate([gathered, info[:, None, :]], axis=1).reshape(devices, -1)
    arrived = lax.all_to_all(
        payload, ("src", "frame", "tile"), split_axis=0, concat_axis=0, tiled=True
    )

    info = arrived[:, per_pair * channels :]
    targets = info[:, :per_pair].reshape(-1).astype(jnp.int32)
    part_n = info[:, per_pair : per_pair + CLIPS]
    base = per_pair + CLIPS
    part_s = info[:, base : base + CLIPS * GROUPS].reshape(devices, CLIPS, GROUPS)
    part_m2 = info[:, base + CLIPS * GROUPS : base + 2 * CLIPS * GROUPS].reshape(
        devices, CLIPS, GROUPS
    )
    total_n = jnp.sum(part_n, axis=0)
    clip_mean = jnp.sum(part_s, axis=0) / total_n[:, None]
    part_m = part_s / jnp.maximum(part_n, 1.0)[:, :, None]
    spread = part_m - clip_mean[None]
    clip_m2 = jnp.sum(part_m2, axis=0) + jnp.sum(part_n[:, :, None] * spread * spread, axis=0)
    clip_var = clip_m2 / total_n[:, None]

    _, gather_rows = lax.sort((targets, iota), num_keys=1)
    rows = arrived[:, : per_pair * channels].reshape(-1, channels)
    features = rows[gather_rows].reshape(FR_DEV, HR, WCOL, channels)

    first_frame = lax.axis_index("frame") * FR_DEV
    padded_ids = jnp.concatenate([jnp.full((2,), -1, jnp.int32), clip_ids])
    window_ids = lax.dynamic_slice_in_dim(padded_ids, first_frame, FR_DEV + 2)
    own_ids = window_ids[2:]
    onehot = (own_ids[:, None] == jnp.arange(CLIPS, dtype=jnp.int32)[None, :]).astype(jnp.float32)
    shaped = features.reshape(FR_DEV, per_frame, GROUPS, group_width)
    frame_mean = jnp.dot(onehot, clip_mean, precision=HIGH)
    centred = shaped - frame_mean[:, None, :, None]
    inverse_std = 1.0 / jnp.sqrt(clip_var + 1e-06)
    frame_inv = jnp.dot(onehot, inverse_std, precision=HIGH)
    normed = (centred * frame_inv[:, None, :, None]).reshape(FR_DEV, HR, WCOL, channels)
    activated = jax.nn.silu(normed * norm_gain + norm_bias).astype(jnp.bfloat16)
    high_padded = with_halo(activated, (("tile", 1),), 1)
    n_wide = lax.axis_size("src")
    up = [(i, i + 1) for i in range(n_wide - 1)]
    left = lax.ppermute(high_padded[:, :, WCOL - 1 :], "src", up)
    right = lax.ppermute(high_padded[:, :, :1], "src", [(j, i) for i, j in up])
    own_wide = widen(high_padded, left, right)
    sent_prev = jnp.concatenate(
        [high_padded[FR_DEV - 2 :], left[FR_DEV - 2 :], right[FR_DEV - 2 :]], axis=2
    )
    prev = passed_along(sent_prev, "frame", 1)
    prev_wide = widen(prev[:, :, :WCOL], prev[:, :, WCOL : WCOL + 1], prev[:, :, WCOL + 1 :])

    validity = jnp.stack(
        [(window_ids[a : a + FR_DEV] == own_ids).astype(jnp.int32) for a in range(3)]
    )
    reach = jnp.arange(3)[:, None] + jnp.arange(FR_DEV)[None, :]
    own_valid = jnp.where(reach >= 2, validity, 0).reshape(-1)
    prev_valid = jnp.where(reach < 2, validity, 0)[:2, :2].reshape(-1)
    weights = conv_weight.reshape(9, 3 * channels, channels)
    bias = conv_bias.reshape(1, channels)
    decoded, early = own_conv(own_valid, own_wide, weights, features, bias)
    return prev_conv(prev_valid, prev_wide, weights, early, decoded)


def widen(block, left, right):
    shifted_in = jnp.concatenate([left, block[:, :, : WCOL - 1]], axis=2)
    shifted_out = jnp.concatenate([block[:, :, 1:], right], axis=2)
    return jnp.concatenate([shifted_in, block, shifted_out], axis=-1)


def own_kernel(valid_ref, x_ref, w_ref, b_ref, f_hbm, o_ref, early_ref, f_ref, acc_ref, sem):
    tap_time = pl.program_id(0)
    tap_high = pl.program_id(1)
    fetch = pltpu.make_async_copy(f_hbm, f_ref, sem)

    @pl.when((tap_time == 0) & (tap_high == 0))
    def _():
        fetch.start()
        acc_ref[...] = jnp.zeros_like(acc_ref)

    for a in range(3):

        @pl.when(tap_time == a)
        def _():
            reach = FR_DEV - 2 + a
            lhs = x_ref[:reach, pl.ds(tap_high, HR)].reshape(reach * HR * WCOL, -1)
            part = jnp.dot(lhs, w_ref[0], preferred_element_type=jnp.float32)
            for j in range(reach):
                t = j + 2 - a
                keep = valid_ref[a * FR_DEV + t].astype(jnp.float32)
                acc_ref[t] += part[j * HR * WCOL : (j + 1) * HR * WCOL] * keep

    @pl.when((tap_time == 2) & (tap_high == 2))
    def _():
        fetch.wait()
        for t in range(FR_DEV):
            total = (f_ref[t] + acc_ref[t].reshape(HR, WCOL, -1)) + b_ref[...]
            if t < 2:
                early_ref[t] = total
            else:
                o_ref[t] = total.astype(o_ref.dtype)


def own_conv(validity, wide, weights, features, bias):
    return pl.pallas_call(
        own_kernel,
        grid_spec=pltpu.PrefetchScalarGridSpec(
            num_scalar_prefetch=1,
            grid=(3, 3),
            in_specs=[
                pl.BlockSpec(wide.shape, lambda a, b, v: (0, 0, 0, 0), pipeline_mode=pl.Buffered(1)),
                pl.BlockSpec((1,) + weights.shape[1:], lambda a, b, v: (a * 3 + b, 0, 0)),
                pl.BlockSpec(bias.shape, lambda a, b, v: (0, 0), pipeline_mode=pl.Buffered(1)),
                pl.BlockSpec(memory_space=pl.ANY),
            ],
            out_specs=[
                pl.BlockSpec(features.shape, lambda a, b, v: (0, 0, 0, 0)),
                pl.BlockSpec((2,) + features.shape[1:], lambda a, b, v: (0, 0, 0, 0)),
            ],
            scratch_shapes=[
                pltpu.VMEM(features.shape, jnp.float32),
                pltpu.VMEM((features.shape[0], HR * WCOL, features.shape[-1]), jnp.float32),
                pltpu.SemaphoreType.DMA(()),
            ],
        ),
        out_shape=[
            jax.ShapeDtypeStruct(features.shape, jnp.bfloat16),
            jax.ShapeDtypeStruct((2,) + features.shape[1:], jnp.float32),
        ],
        compiler_params=pltpu.CompilerParams(
            dimension_semantics=("arbitrary", "arbitrary"), vmem_limit_bytes=60 * 1024 * 1024
        ),
    )(validity, wide, weights, bias, features)


def prev_kernel(valid_ref, x_ref, w_ref, early_ref, whole_ref, o_ref, acc_ref):
    del whole_ref
    tap_time = pl.program_id(0)
    tap_high = pl.program_id(1)

    @pl.when((tap_time == 0) & (tap_high == 0))
    def _():
        acc_ref[...] = jnp.zeros_like(acc_ref)

    for t in range(2):

        @pl.when(valid_ref[tap_time * 2 + t] != 0)
        def _():
            frame = jnp.minimum(tap_time + t, 1)
            lhs = x_ref[frame, pl.ds(tap_high, HR)].reshape(HR * WCOL, -1)
            acc_ref[t] += jnp.dot(lhs, w_ref[0], preferred_element_type=jnp.float32)

    @pl.when((tap_time == 1) & (tap_high == 2))
    def _():
        for t in range(2):
            total = early_ref[t] + acc_ref[t].reshape(HR, WCOL, -1)
            o_ref[t] = total.astype(o_ref.dtype)


def prev_conv(validity, wide, weights, early, decoded):
    return pl.pallas_call(
        prev_kernel,
        grid_spec=pltpu.PrefetchScalarGridSpec(
            num_scalar_prefetch=1,
            grid=(2, 3),
            in_specs=[
                pl.BlockSpec(wide.shape, lambda a, b, v: (0, 0, 0, 0), pipeline_mode=pl.Buffered(1)),
                pl.BlockSpec((1,) + weights.shape[1:], lambda a, b, v: (a * 3 + b, 0, 0)),
                pl.BlockSpec(early.shape, lambda a, b, v: (0, 0, 0, 0), pipeline_mode=pl.Buffered(1)),
                pl.BlockSpec(memory_space=pl.ANY),
            ],
            out_specs=pl.BlockSpec(early.shape, lambda a, b, v: (0, 0, 0, 0)),
            scratch_shapes=[pltpu.VMEM((2, HR * WCOL, early.shape[-1]), jnp.float32)],
        ),
        out_shape=jax.ShapeDtypeStruct(decoded.shape, decoded.dtype),
        input_output_aliases={4: 0},
        compiler_params=pltpu.CompilerParams(
            dimension_semantics=("arbitrary", "arbitrary"), vmem_limit_bytes=60 * 1024 * 1024
        ),
    )(validity, wide, weights, early, decoded)


def solution(mesh):
    placed = (
        P(("src", "frame", "tile"), None),
        P(("src", "frame", "tile")),
        P(),
        P(),
        P(),
        P(),
        P(),
    )
    return jax.shard_map(
        shards,
        mesh=mesh,
        in_specs=placed,
        out_specs=P("frame", "tile", "src", None),
        check_vma=False,
    )
```

```python
import jax
import jax.numpy as jnp
from jax import lax
from jax.experimental import pallas as pl
from jax.experimental.pallas import tpu as pltpu
from jax.sharding import PartitionSpec as P

GROUPS = 32
CLIPS = 4
FR_DEV = 6
HR = 8
WCOL = 32
HIGH = lax.Precision.HIGHEST


def passed_along(x, axis, by):
    peers = lax.axis_size(axis)
    pairs = [(i, i + by) for i in range(peers) if 0 <= i + by < peers]
    return lax.ppermute(x, axis, pairs)


def with_halo(x, sides, width):
    for axis, dim in sides:
        peers, length = (lax.axis_size(axis), x.shape[dim])
        up = [(i, (i + 1) % peers) for i in range(peers - 1)]
        down = [(j, i) for i, j in up]
        last = lax.slice_in_dim(x, length - width, length, axis=dim)
        leading = lax.slice_in_dim(x, 0, width, axis=dim)
        before = lax.ppermute(last, axis, up)
        after = lax.ppermute(leading, axis, down)
        x = jnp.concatenate([before, x, after], axis=dim)
    return x


def shards(feats, row_map, clip_ids, norm_gain, norm_bias, conv_weight, conv_bias):
    local_rows, channels = feats.shape
    n_src = lax.axis_size("src")
    n_frame = lax.axis_size("frame")
    n_tile = lax.axis_size("tile")
    devices = n_src * n_frame * n_tile
    per_pair = local_rows // devices
    group_width = channels // GROUPS
    per_frame = HR * WCOL

    owners = row_map // local_rows
    slot_ids = row_map % local_rows
    frames = clip_ids.shape[0]
    row_frame = (owners // n_tile) % n_frame * FR_DEV + slot_ids // per_frame
    frame_onehot = (row_frame[:, None] == jnp.arange(frames, dtype=jnp.int32)[None, :]).astype(
        jnp.float32
    )
    clip_onehot = (clip_ids[:, None] == jnp.arange(CLIPS, dtype=jnp.int32)[None, :]).astype(
        jnp.float32
    )
    row_onehot = jnp.dot(frame_onehot, clip_onehot)

    clip_mask = row_onehot.T[:, :, None]
    local_n = jnp.sum(row_onehot, axis=0) * group_width
    local_s = jnp.sum(
        jnp.sum(feats[None] * clip_mask, axis=1).reshape(CLIPS, GROUPS, group_width), axis=2
    )
    local_m = local_s / jnp.maximum(local_n, 1.0)[:, None]
    wide_m = jnp.repeat(local_m, group_width, axis=1)
    row_m = jnp.sum(clip_mask * wide_m[:, None, :], axis=0)
    dev = feats - row_m
    local_m2 = jnp.sum(
        jnp.sum((dev * dev)[None] * clip_mask, axis=1).reshape(CLIPS, GROUPS, group_width),
        axis=2,
    )

    block = 16
    iota = lax.iota(jnp.int32, local_rows)
    _, sent_slots, ordering = lax.sort((owners, slot_ids, iota), num_keys=1, is_stable=True)
    stats = jnp.concatenate([local_n, local_s.reshape(-1), local_m2.reshape(-1)])
    info = jnp.concatenate(
        [
            sent_slots.astype(jnp.float32).reshape(devices, per_pair),
            jnp.broadcast_to(stats, (devices, stats.shape[0])),
            jnp.zeros((devices, channels - per_pair - stats.shape[0]), jnp.float32),
        ],
        axis=1,
    )
    payload = jnp.concatenate(
        [
            feats[ordering.reshape(devices, per_pair)],
            info[:, None, :],
            jnp.zeros((devices, block - per_pair - 1, channels), jnp.float32),
        ],
        axis=1,
    )
    arrived = lax.all_to_all(
        payload, ("src", "frame", "tile"), split_axis=0, concat_axis=0, tiled=True
    )

    info = arrived[:, per_pair, :]
    targets = info[:, :per_pair].reshape(-1).astype(jnp.int32)
    part_n = info[:, per_pair : per_pair + CLIPS]
    base = per_pair + CLIPS
    part_s = info[:, base : base + CLIPS * GROUPS].reshape(devices, CLIPS, GROUPS)
    part_m2 = info[:, base + CLIPS * GROUPS : base + 2 * CLIPS * GROUPS].reshape(
        devices, CLIPS, GROUPS
    )
    total_n = jnp.sum(part_n, axis=0)
    clip_mean = jnp.sum(part_s, axis=0) / total_n[:, None]
    part_m = part_s / jnp.maximum(part_n, 1.0)[:, :, None]
    spread = part_m - clip_mean[None]
    clip_m2 = jnp.sum(part_m2, axis=0) + jnp.sum(part_n[:, :, None] * spread * spread, axis=0)
    clip_var = clip_m2 / total_n[:, None]

    arrival_row = (iota // per_pair) * block + iota % per_pair
    digits = jnp.stack([arrival_row // 64, arrival_row % 64], axis=1).astype(jnp.bfloat16)
    chooser = (targets[None, :] == iota[:, None]).astype(jnp.bfloat16)
    found = jnp.dot(chooser, digits, preferred_element_type=jnp.float32).astype(jnp.int32)
    gather_rows = found[:, 0] * 64 + found[:, 1]
    features = arrived.reshape(-1, channels)[gather_rows].reshape(FR_DEV, HR, WCOL, channels)

    first_frame = lax.axis_index("frame") * FR_DEV
    padded_ids = jnp.concatenate([jnp.full((2,), -1, jnp.int32), clip_ids])
    window_ids = lax.dynamic_slice_in_dim(padded_ids, first_frame, FR_DEV + 2)
    own_ids = window_ids[2:]
    onehot = (own_ids[:, None] == jnp.arange(CLIPS, dtype=jnp.int32)[None, :]).astype(jnp.float32)
    shaped = features.reshape(FR_DEV, per_frame, GROUPS, group_width)
    frame_mean = jnp.dot(onehot, clip_mean, precision=HIGH)
    centred = shaped - frame_mean[:, None, :, None]
    inverse_std = 1.0 / jnp.sqrt(clip_var + 1e-06)
    frame_inv = jnp.dot(onehot, inverse_std, precision=HIGH)
    normed = (centred * frame_inv[:, None, :, None]).reshape(FR_DEV, HR, WCOL, channels)
    activated = jax.nn.silu(normed * norm_gain + norm_bias).astype(jnp.bfloat16)
    high_padded = with_halo(activated, (("tile", 1),), 1)
    n_wide = lax.axis_size("src")
    up = [(i, i + 1) for i in range(n_wide - 1)]
    left = lax.ppermute(high_padded[:, :, WCOL - 1 :], "src", up)
    right = lax.ppermute(high_padded[:, :, :1], "src", [(j, i) for i, j in up])
    own_wide = widen(high_padded, left, right)
    sent_prev = jnp.concatenate(
        [high_padded[FR_DEV - 2 :], left[FR_DEV - 2 :], right[FR_DEV - 2 :]], axis=2
    )
    prev = passed_along(sent_prev, "frame", 1)
    prev_wide = widen(prev[:, :, :WCOL], prev[:, :, WCOL : WCOL + 1], prev[:, :, WCOL + 1 :])

    validity = jnp.stack(
        [(window_ids[a : a + FR_DEV] == own_ids).astype(jnp.int32) for a in range(3)]
    )
    reach = jnp.arange(3)[:, None] + jnp.arange(FR_DEV)[None, :]
    own_valid = jnp.where(reach >= 2, validity, 0).reshape(-1)
    prev_valid = jnp.where(reach < 2, validity, 0)[:2, :2].reshape(-1)
    weights = conv_weight.reshape(9, 3 * channels, channels)
    bias = conv_bias.reshape(1, channels)
    decoded, early = own_conv(own_valid, own_wide, weights, features, bias)
    return prev_conv(prev_valid, prev_wide, weights, early, decoded)


def widen(block, left, right):
    shifted_in = jnp.concatenate([left, block[:, :, : WCOL - 1]], axis=2)
    shifted_out = jnp.concatenate([block[:, :, 1:], right], axis=2)
    return jnp.concatenate([shifted_in, block, shifted_out], axis=-1)


def own_kernel(valid_ref, x_ref, w_ref, b_ref, f_hbm, o_ref, early_ref, f_ref, acc_ref, sem):
    tap_time = pl.program_id(0)
    tap_high = pl.program_id(1)
    fetch = pltpu.make_async_copy(f_hbm, f_ref, sem)

    @pl.when((tap_time == 0) & (tap_high == 0))
    def _():
        fetch.start()
        acc_ref[...] = jnp.zeros_like(acc_ref)

    for a in range(3):

        @pl.when(tap_time == a)
        def _():
            reach = FR_DEV - 2 + a
            lhs = x_ref[:reach, pl.ds(tap_high, HR)].reshape(reach * HR * WCOL, -1)
            part = jnp.dot(lhs, w_ref[0], preferred_element_type=jnp.float32)
            for j in range(reach):
                t = j + 2 - a
                keep = valid_ref[a * FR_DEV + t].astype(jnp.float32)
                acc_ref[t] += part[j * HR * WCOL : (j + 1) * HR * WCOL] * keep

    @pl.when((tap_time == 2) & (tap_high == 2))
    def _():
        fetch.wait()
        for t in range(FR_DEV):
            total = (f_ref[t] + acc_ref[t].reshape(HR, WCOL, -1)) + b_ref[...]
            if t < 2:
                early_ref[t] = total
            else:
                o_ref[t] = total.astype(o_ref.dtype)


def own_conv(validity, wide, weights, features, bias):
    return pl.pallas_call(
        own_kernel,
        grid_spec=pltpu.PrefetchScalarGridSpec(
            num_scalar_prefetch=1,
            grid=(3, 3),
            in_specs=[
                pl.BlockSpec(wide.shape, lambda a, b, v: (0, 0, 0, 0), pipeline_mode=pl.Buffered(1)),
                pl.BlockSpec((1,) + weights.shape[1:], lambda a, b, v: (a * 3 + b, 0, 0)),
                pl.BlockSpec(bias.shape, lambda a, b, v: (0, 0), pipeline_mode=pl.Buffered(1)),
                pl.BlockSpec(memory_space=pl.ANY),
            ],
            out_specs=[
                pl.BlockSpec(features.shape, lambda a, b, v: (0, 0, 0, 0)),
                pl.BlockSpec((2,) + features.shape[1:], lambda a, b, v: (0, 0, 0, 0)),
            ],
            scratch_shapes=[
                pltpu.VMEM(features.shape, jnp.float32),
                pltpu.VMEM((features.shape[0], HR * WCOL, features.shape[-1]), jnp.float32),
                pltpu.SemaphoreType.DMA(()),
            ],
        ),
        out_shape=[
            jax.ShapeDtypeStruct(features.shape, jnp.bfloat16),
            jax.ShapeDtypeStruct((2,) + features.shape[1:], jnp.float32),
        ],
        compiler_params=pltpu.CompilerParams(
            dimension_semantics=("arbitrary", "arbitrary"), vmem_limit_bytes=60 * 1024 * 1024
        ),
    )(validity, wide, weights, bias, features)


def prev_kernel(valid_ref, x_ref, w_ref, early_ref, whole_ref, o_ref, acc_ref):
    del whole_ref
    tap_time = pl.program_id(0)
    tap_high = pl.program_id(1)

    @pl.when((tap_time == 0) & (tap_high == 0))
    def _():
        acc_ref[...] = jnp.zeros_like(acc_ref)

    for t in range(2):

        @pl.when(valid_ref[tap_time * 2 + t] != 0)
        def _():
            frame = jnp.minimum(tap_time + t, 1)
            lhs = x_ref[frame, pl.ds(tap_high, HR)].reshape(HR * WCOL, -1)
            acc_ref[t] += jnp.dot(lhs, w_ref[0], preferred_element_type=jnp.float32)

    @pl.when((tap_time == 1) & (tap_high == 2))
    def _():
        for t in range(2):
            total = early_ref[t] + acc_ref[t].reshape(HR, WCOL, -1)
            o_ref[t] = total.astype(o_ref.dtype)


def prev_conv(validity, wide, weights, early, decoded):
    return pl.pallas_call(
        prev_kernel,
        grid_spec=pltpu.PrefetchScalarGridSpec(
            num_scalar_prefetch=1,
            grid=(2, 3),
            in_specs=[
                pl.BlockSpec(wide.shape, lambda a, b, v: (0, 0, 0, 0), pipeline_mode=pl.Buffered(1)),
                pl.BlockSpec((1,) + weights.shape[1:], lambda a, b, v: (a * 3 + b, 0, 0)),
                pl.BlockSpec(early.shape, lambda a, b, v: (0, 0, 0, 0), pipeline_mode=pl.Buffered(1)),
                pl.BlockSpec(memory_space=pl.ANY),
            ],
            out_specs=pl.BlockSpec(early.shape, lambda a, b, v: (0, 0, 0, 0)),
            scratch_shapes=[pltpu.VMEM((2, HR * WCOL, early.shape[-1]), jnp.float32)],
        ),
        out_shape=jax.ShapeDtypeStruct(decoded.shape, decoded.dtype),
        input_output_aliases={4: 0},
        compiler_params=pltpu.CompilerParams(
            dimension_semantics=("arbitrary", "arbitrary"), vmem_limit_bytes=60 * 1024 * 1024
        ),
    )(validity, wide, weights, early, decoded)


def solution(mesh):
    placed = (
        P(("src", "frame", "tile"), None),
        P(("src", "frame", "tile")),
        P(),
        P(),
        P(),
        P(),
        P(),
    )
    return jax.shard_map(
        shards,
        mesh=mesh,
        in_specs=placed,
        out_specs=P("frame", "tile", "src", None),
        check_vma=False,
    )
```

```python
import jax
import jax.numpy as jnp
from jax import lax
from jax.experimental import pallas as pl
from jax.experimental.pallas import tpu as pltpu
from jax.sharding import PartitionSpec as P

GROUPS = 32
CLIPS = 4
FR_DEV = 6
HR = 8
WCOL = 32
HIGH = lax.Precision.HIGHEST


def passed_along(x, axis, by):
    peers = lax.axis_size(axis)
    pairs = [(i, i + by) for i in range(peers) if 0 <= i + by < peers]
    return lax.ppermute(x, axis, pairs)


def with_halo(x, sides, width):
    for axis, dim in sides:
        peers, length = (lax.axis_size(axis), x.shape[dim])
        up = [(i, (i + 1) % peers) for i in range(peers - 1)]
        down = [(j, i) for i, j in up]
        last = lax.slice_in_dim(x, length - width, length, axis=dim)
        leading = lax.slice_in_dim(x, 0, width, axis=dim)
        before = lax.ppermute(last, axis, up)
        after = lax.ppermute(leading, axis, down)
        x = jnp.concatenate([before, x, after], axis=dim)
    return x


def shards(feats, row_map, clip_ids, norm_gain, norm_bias, conv_weight, conv_bias):
    local_rows, channels = feats.shape
    n_src = lax.axis_size("src")
    n_frame = lax.axis_size("frame")
    n_tile = lax.axis_size("tile")
    devices = n_src * n_frame * n_tile
    per_pair = local_rows // devices
    group_width = channels // GROUPS
    per_frame = HR * WCOL

    owners = row_map // local_rows
    slot_ids = row_map % local_rows
    frames = clip_ids.shape[0]
    row_frame = (owners // n_tile) % n_frame * FR_DEV + slot_ids // per_frame
    frame_onehot = (row_frame[:, None] == jnp.arange(frames, dtype=jnp.int32)[None, :]).astype(
        jnp.float32
    )
    clip_onehot = (clip_ids[:, None] == jnp.arange(CLIPS, dtype=jnp.int32)[None, :]).astype(
        jnp.float32
    )
    row_onehot = jnp.dot(frame_onehot, clip_onehot)

    clip_mask = row_onehot.T[:, :, None]
    local_n = jnp.sum(row_onehot, axis=0) * group_width
    local_s = jnp.sum(
        jnp.sum(feats[None] * clip_mask, axis=1).reshape(CLIPS, GROUPS, group_width), axis=2
    )
    local_m = local_s / jnp.maximum(local_n, 1.0)[:, None]
    wide_m = jnp.repeat(local_m, group_width, axis=1)
    row_m = jnp.sum(clip_mask * wide_m[:, None, :], axis=0)
    dev = feats - row_m
    local_m2 = jnp.sum(
        jnp.sum((dev * dev)[None] * clip_mask, axis=1).reshape(CLIPS, GROUPS, group_width),
        axis=2,
    )

    block = 16
    iota = lax.iota(jnp.int32, local_rows)
    owner_onehot = (owners[:, None] == jnp.arange(devices, dtype=jnp.int32)[None, :]).astype(
        jnp.bfloat16
    )
    earlier = (iota[:, None] > iota[None, :]).astype(jnp.bfloat16)
    before = jnp.dot(earlier, owner_onehot, preferred_element_type=jnp.float32)
    rank = jnp.sum(before * owner_onehot.astype(jnp.float32), axis=1).astype(jnp.int32)
    position = owners * block + rank
    slots = lax.iota(jnp.int32, devices * block)
    placer = (position[None, :] == slots[:, None]).astype(jnp.bfloat16)

    high = lax.reduce_precision(feats, exponent_bits=8, mantissa_bits=7)
    rest = feats - high
    middle = lax.reduce_precision(rest, exponent_bits=8, mantissa_bits=7)
    low = rest - middle
    pieces = jnp.concatenate([high, middle, low], axis=1).astype(jnp.bfloat16)
    placed = jnp.dot(placer, pieces, preferred_element_type=jnp.float32)
    digits = jnp.stack([slot_ids // 64, slot_ids % 64], axis=1).astype(jnp.bfloat16)
    slot_digits = jnp.dot(placer, digits, preferred_element_type=jnp.float32)
    sent_slots = (slot_digits[:, 0] * 64 + slot_digits[:, 1]).reshape(devices, block)[:, :per_pair]

    stats = jnp.concatenate([local_n, local_s.reshape(-1), local_m2.reshape(-1)])
    info = jnp.concatenate(
        [
            sent_slots,
            jnp.broadcast_to(stats, (devices, stats.shape[0])),
            jnp.zeros((devices, channels - per_pair - stats.shape[0]), jnp.float32),
        ],
        axis=1,
    )
    rows = (placed[:, :channels] + placed[:, channels : 2 * channels]) + placed[:, 2 * channels :]
    rows = rows.reshape(devices, block, channels)
    is_info = (jnp.arange(block) == per_pair)[None, :, None]
    payload = jnp.where(is_info, info[:, None, :], rows)
    arrived = lax.all_to_all(
        payload, ("src", "frame", "tile"), split_axis=0, concat_axis=0, tiled=True
    )

    info = arrived[:, per_pair, :]
    targets = info[:, :per_pair].reshape(-1).astype(jnp.int32)
    part_n = info[:, per_pair : per_pair + CLIPS]
    base = per_pair + CLIPS
    part_s = info[:, base : base + CLIPS * GROUPS].reshape(devices, CLIPS, GROUPS)
    part_m2 = info[:, base + CLIPS * GROUPS : base + 2 * CLIPS * GROUPS].reshape(
        devices, CLIPS, GROUPS
    )
    total_n = jnp.sum(part_n, axis=0)
    clip_mean = jnp.sum(part_s, axis=0) / total_n[:, None]
    part_m = part_s / jnp.maximum(part_n, 1.0)[:, :, None]
    spread = part_m - clip_mean[None]
    clip_m2 = jnp.sum(part_m2, axis=0) + jnp.sum(part_n[:, :, None] * spread * spread, axis=0)
    clip_var = clip_m2 / total_n[:, None]

    arrival_row = (iota // per_pair) * block + iota % per_pair
    digits = jnp.stack([arrival_row // 64, arrival_row % 64], axis=1).astype(jnp.bfloat16)
    chooser = (targets[None, :] == iota[:, None]).astype(jnp.bfloat16)
    found = jnp.dot(chooser, digits, preferred_element_type=jnp.float32).astype(jnp.int32)
    gather_rows = found[:, 0] * 64 + found[:, 1]
    features = arrived.reshape(-1, channels)[gather_rows].reshape(FR_DEV, HR, WCOL, channels)

    first_frame = lax.axis_index("frame") * FR_DEV
    padded_ids = jnp.concatenate([jnp.full((2,), -1, jnp.int32), clip_ids])
    window_ids = lax.dynamic_slice_in_dim(padded_ids, first_frame, FR_DEV + 2)
    own_ids = window_ids[2:]
    onehot = (own_ids[:, None] == jnp.arange(CLIPS, dtype=jnp.int32)[None, :]).astype(jnp.float32)
    shaped = features.reshape(FR_DEV, per_frame, GROUPS, group_width)
    frame_mean = jnp.dot(onehot, clip_mean, precision=HIGH)
    centred = shaped - frame_mean[:, None, :, None]
    inverse_std = 1.0 / jnp.sqrt(clip_var + 1e-06)
    frame_inv = jnp.dot(onehot, inverse_std, precision=HIGH)
    normed = (centred * frame_inv[:, None, :, None]).reshape(FR_DEV, HR, WCOL, channels)
    activated = jax.nn.silu(normed * norm_gain + norm_bias).astype(jnp.bfloat16)
    high_padded = with_halo(activated, (("tile", 1),), 1)
    n_wide = lax.axis_size("src")
    up = [(i, i + 1) for i in range(n_wide - 1)]
    left = lax.ppermute(high_padded[:, :, WCOL - 1 :], "src", up)
    right = lax.ppermute(high_padded[:, :, :1], "src", [(j, i) for i, j in up])
    own_wide = widen(high_padded, left, right)
    sent_prev = jnp.concatenate(
        [high_padded[FR_DEV - 2 :], left[FR_DEV - 2 :], right[FR_DEV - 2 :]], axis=2
    )
    prev = passed_along(sent_prev, "frame", 1)
    prev_wide = widen(prev[:, :, :WCOL], prev[:, :, WCOL : WCOL + 1], prev[:, :, WCOL + 1 :])

    validity = jnp.stack(
        [(window_ids[a : a + FR_DEV] == own_ids).astype(jnp.int32) for a in range(3)]
    )
    reach = jnp.arange(3)[:, None] + jnp.arange(FR_DEV)[None, :]
    own_valid = jnp.where(reach >= 2, validity, 0).reshape(-1)
    prev_valid = jnp.where(reach < 2, validity, 0)[:2, :2].reshape(-1)
    weights = conv_weight.reshape(9, 3 * channels, channels)
    bias = conv_bias.reshape(1, channels)
    decoded, early = own_conv(own_valid, own_wide, weights, features, bias)
    return prev_conv(prev_valid, prev_wide, weights, early, decoded)


def widen(block, left, right):
    shifted_in = jnp.concatenate([left, block[:, :, : WCOL - 1]], axis=2)
    shifted_out = jnp.concatenate([block[:, :, 1:], right], axis=2)
    return jnp.concatenate([shifted_in, block, shifted_out], axis=-1)


def own_kernel(valid_ref, x_ref, w_ref, b_ref, f_hbm, o_ref, early_ref, f_ref, acc_ref, sem):
    tap_time = pl.program_id(0)
    tap_high = pl.program_id(1)
    fetch = pltpu.make_async_copy(f_hbm, f_ref, sem)

    @pl.when((tap_time == 0) & (tap_high == 0))
    def _():
        fetch.start()
        acc_ref[...] = jnp.zeros_like(acc_ref)

    for a in range(3):

        @pl.when(tap_time == a)
        def _():
            reach = FR_DEV - 2 + a
            lhs = x_ref[:reach, pl.ds(tap_high, HR)].reshape(reach * HR * WCOL, -1)
            part = jnp.dot(lhs, w_ref[0], preferred_element_type=jnp.float32)
            for j in range(reach):
                t = j + 2 - a
                keep = valid_ref[a * FR_DEV + t].astype(jnp.float32)
                acc_ref[t] += part[j * HR * WCOL : (j + 1) * HR * WCOL] * keep

    @pl.when((tap_time == 2) & (tap_high == 2))
    def _():
        fetch.wait()
        for t in range(FR_DEV):
            total = (f_ref[t] + acc_ref[t].reshape(HR, WCOL, -1)) + b_ref[...]
            if t < 2:
                early_ref[t] = total
            else:
                o_ref[t] = total.astype(o_ref.dtype)


def own_conv(validity, wide, weights, features, bias):
    return pl.pallas_call(
        own_kernel,
        grid_spec=pltpu.PrefetchScalarGridSpec(
            num_scalar_prefetch=1,
            grid=(3, 3),
            in_specs=[
                pl.BlockSpec(wide.shape, lambda a, b, v: (0, 0, 0, 0), pipeline_mode=pl.Buffered(1)),
                pl.BlockSpec((1,) + weights.shape[1:], lambda a, b, v: (a * 3 + b, 0, 0)),
                pl.BlockSpec(bias.shape, lambda a, b, v: (0, 0), pipeline_mode=pl.Buffered(1)),
                pl.BlockSpec(memory_space=pl.ANY),
            ],
            out_specs=[
                pl.BlockSpec(features.shape, lambda a, b, v: (0, 0, 0, 0)),
                pl.BlockSpec((2,) + features.shape[1:], lambda a, b, v: (0, 0, 0, 0)),
            ],
            scratch_shapes=[
                pltpu.VMEM(features.shape, jnp.float32),
                pltpu.VMEM((features.shape[0], HR * WCOL, features.shape[-1]), jnp.float32),
                pltpu.SemaphoreType.DMA(()),
            ],
        ),
        out_shape=[
            jax.ShapeDtypeStruct(features.shape, jnp.bfloat16),
            jax.ShapeDtypeStruct((2,) + features.shape[1:], jnp.float32),
        ],
        compiler_params=pltpu.CompilerParams(
            dimension_semantics=("arbitrary", "arbitrary"), vmem_limit_bytes=60 * 1024 * 1024
        ),
    )(validity, wide, weights, bias, features)


def prev_kernel(valid_ref, x_ref, w_ref, early_ref, whole_ref, o_ref, acc_ref):
    del whole_ref
    tap_time = pl.program_id(0)
    tap_high = pl.program_id(1)

    @pl.when((tap_time == 0) & (tap_high == 0))
    def _():
        acc_ref[...] = jnp.zeros_like(acc_ref)

    for t in range(2):

        @pl.when(valid_ref[tap_time * 2 + t] != 0)
        def _():
            frame = jnp.minimum(tap_time + t, 1)
            lhs = x_ref[frame, pl.ds(tap_high, HR)].reshape(HR * WCOL, -1)
            acc_ref[t] += jnp.dot(lhs, w_ref[0], preferred_element_type=jnp.float32)

    @pl.when((tap_time == 1) & (tap_high == 2))
    def _():
        for t in range(2):
            total = early_ref[t] + acc_ref[t].reshape(HR, WCOL, -1)
            o_ref[t] = total.astype(o_ref.dtype)


def prev_conv(validity, wide, weights, early, decoded):
    return pl.pallas_call(
        prev_kernel,
        grid_spec=pltpu.PrefetchScalarGridSpec(
            num_scalar_prefetch=1,
            grid=(2, 3),
            in_specs=[
                pl.BlockSpec(wide.shape, lambda a, b, v: (0, 0, 0, 0), pipeline_mode=pl.Buffered(1)),
                pl.BlockSpec((1,) + weights.shape[1:], lambda a, b, v: (a * 3 + b, 0, 0)),
                pl.BlockSpec(early.shape, lambda a, b, v: (0, 0, 0, 0), pipeline_mode=pl.Buffered(1)),
                pl.BlockSpec(memory_space=pl.ANY),
            ],
            out_specs=pl.BlockSpec(early.shape, lambda a, b, v: (0, 0, 0, 0)),
            scratch_shapes=[pltpu.VMEM((2, HR * WCOL, early.shape[-1]), jnp.float32)],
        ),
        out_shape=jax.ShapeDtypeStruct(decoded.shape, decoded.dtype),
        input_output_aliases={4: 0},
        compiler_params=pltpu.CompilerParams(
            dimension_semantics=("arbitrary", "arbitrary"), vmem_limit_bytes=60 * 1024 * 1024
        ),
    )(validity, wide, weights, early, decoded)


def solution(mesh):
    placed = (
        P(("src", "frame", "tile"), None),
        P(("src", "frame", "tile")),
        P(),
        P(),
        P(),
        P(),
        P(),
    )
    return jax.shard_map(
        shards,
        mesh=mesh,
        in_specs=placed,
        out_specs=P("frame", "tile", "src", None),
        check_vma=False,
    )
```

```python
import jax
import jax.numpy as jnp
from jax import lax
from jax.experimental import pallas as pl
from jax.experimental.pallas import tpu as pltpu
from jax.sharding import PartitionSpec as P

GROUPS = 32
CLIPS = 4
FR_DEV = 6
HR = 8
WCOL = 32
HIGH = lax.Precision.HIGHEST


def passed_along(x, axis, by):
    peers = lax.axis_size(axis)
    pairs = [(i, i + by) for i in range(peers) if 0 <= i + by < peers]
    return lax.ppermute(x, axis, pairs)


def with_halo(x, sides, width):
    for axis, dim in sides:
        peers, length = (lax.axis_size(axis), x.shape[dim])
        up = [(i, (i + 1) % peers) for i in range(peers - 1)]
        down = [(j, i) for i, j in up]
        last = lax.slice_in_dim(x, length - width, length, axis=dim)
        leading = lax.slice_in_dim(x, 0, width, axis=dim)
        before = lax.ppermute(last, axis, up)
        after = lax.ppermute(leading, axis, down)
        x = jnp.concatenate([before, x, after], axis=dim)
    return x


def shards(feats, row_map, clip_ids, norm_gain, norm_bias, conv_weight, conv_bias):
    local_rows, channels = feats.shape
    n_src = lax.axis_size("src")
    n_frame = lax.axis_size("frame")
    n_tile = lax.axis_size("tile")
    devices = n_src * n_frame * n_tile
    per_pair = local_rows // devices
    group_width = channels // GROUPS
    per_frame = HR * WCOL

    owners = row_map // local_rows
    slot_ids = row_map % local_rows
    frames = clip_ids.shape[0]
    row_frame = (owners // n_tile) % n_frame * FR_DEV + slot_ids // per_frame
    frame_onehot = (row_frame[:, None] == jnp.arange(frames, dtype=jnp.int32)[None, :]).astype(
        jnp.float32
    )
    clip_onehot = (clip_ids[:, None] == jnp.arange(CLIPS, dtype=jnp.int32)[None, :]).astype(
        jnp.float32
    )
    row_onehot = jnp.dot(frame_onehot, clip_onehot)

    clip_mask = row_onehot.T[:, :, None]
    local_n = jnp.sum(row_onehot, axis=0) * group_width
    local_s = jnp.sum(
        jnp.sum(feats[None] * clip_mask, axis=1).reshape(CLIPS, GROUPS, group_width), axis=2
    )
    local_m = local_s / jnp.maximum(local_n, 1.0)[:, None]
    wide_m = jnp.repeat(local_m, group_width, axis=1)
    row_m = jnp.sum(clip_mask * wide_m[:, None, :], axis=0)
    dev = feats - row_m
    local_m2 = jnp.sum(
        jnp.sum((dev * dev)[None] * clip_mask, axis=1).reshape(CLIPS, GROUPS, group_width),
        axis=2,
    )

    block = 16
    iota = lax.iota(jnp.int32, local_rows)
    _, sent_slots, ordering = lax.sort((owners, slot_ids, iota), num_keys=1, is_stable=True)
    info = jnp.concatenate(
        [
            sent_slots.astype(jnp.float32).reshape(devices, per_pair),
            jnp.zeros((devices, channels - per_pair), jnp.float32),
        ],
        axis=1,
    )
    payload = jnp.concatenate(
        [
            feats[ordering.reshape(devices, per_pair)],
            info[:, None, :],
            jnp.zeros((devices, block - per_pair - 1, channels), jnp.float32),
        ],
        axis=1,
    )
    arrived = lax.all_to_all(
        payload, ("src", "frame", "tile"), split_axis=0, concat_axis=0, tiled=True
    )

    info = arrived[:, per_pair, :]
    targets = info[:, :per_pair].reshape(-1).astype(jnp.int32)
    stats = jnp.concatenate([local_n, local_s.reshape(-1), local_m2.reshape(-1)])
    everyone = lax.all_gather(stats, ("src", "frame", "tile"))
    part_n = everyone[:, :CLIPS]
    part_s = everyone[:, CLIPS : CLIPS + CLIPS * GROUPS].reshape(devices, CLIPS, GROUPS)
    part_m2 = everyone[:, CLIPS + CLIPS * GROUPS :].reshape(devices, CLIPS, GROUPS)
    total_n = jnp.sum(part_n, axis=0)
    clip_mean = jnp.sum(part_s, axis=0) / total_n[:, None]
    part_m = part_s / jnp.maximum(part_n, 1.0)[:, :, None]
    spread = part_m - clip_mean[None]
    clip_m2 = jnp.sum(part_m2, axis=0) + jnp.sum(part_n[:, :, None] * spread * spread, axis=0)
    clip_var = clip_m2 / total_n[:, None]

    arrival_row = (iota // per_pair) * block + iota % per_pair
    digits = jnp.stack([arrival_row // 64, arrival_row % 64], axis=1).astype(jnp.bfloat16)
    chooser = (targets[None, :] == iota[:, None]).astype(jnp.bfloat16)
    found = jnp.dot(chooser, digits, preferred_element_type=jnp.float32).astype(jnp.int32)
    gather_rows = found[:, 0] * 64 + found[:, 1]
    features = arrived.reshape(-1, channels)[gather_rows].reshape(FR_DEV, HR, WCOL, channels)

    first_frame = lax.axis_index("frame") * FR_DEV
    padded_ids = jnp.concatenate([jnp.full((2,), -1, jnp.int32), clip_ids])
    window_ids = lax.dynamic_slice_in_dim(padded_ids, first_frame, FR_DEV + 2)
    own_ids = window_ids[2:]
    onehot = (own_ids[:, None] == jnp.arange(CLIPS, dtype=jnp.int32)[None, :]).astype(jnp.float32)
    shaped = features.reshape(FR_DEV, per_frame, GROUPS, group_width)
    frame_mean = jnp.dot(onehot, clip_mean, precision=HIGH)
    centred = shaped - frame_mean[:, None, :, None]
    inverse_std = 1.0 / jnp.sqrt(clip_var + 1e-06)
    frame_inv = jnp.dot(onehot, inverse_std, precision=HIGH)
    normed = (centred * frame_inv[:, None, :, None]).reshape(FR_DEV, HR, WCOL, channels)
    activated = jax.nn.silu(normed * norm_gain + norm_bias).astype(jnp.bfloat16)
    high_padded = with_halo(activated, (("tile", 1),), 1)
    n_wide = lax.axis_size("src")
    up = [(i, i + 1) for i in range(n_wide - 1)]
    left = lax.ppermute(high_padded[:, :, WCOL - 1 :], "src", up)
    right = lax.ppermute(high_padded[:, :, :1], "src", [(j, i) for i, j in up])
    own_wide = widen(high_padded, left, right)
    sent_prev = jnp.concatenate(
        [high_padded[FR_DEV - 2 :], left[FR_DEV - 2 :], right[FR_DEV - 2 :]], axis=2
    )
    prev = passed_along(sent_prev, "frame", 1)
    prev_wide = widen(prev[:, :, :WCOL], prev[:, :, WCOL : WCOL + 1], prev[:, :, WCOL + 1 :])

    validity = jnp.stack(
        [(window_ids[a : a + FR_DEV] == own_ids).astype(jnp.int32) for a in range(3)]
    )
    reach = jnp.arange(3)[:, None] + jnp.arange(FR_DEV)[None, :]
    own_valid = jnp.where(reach >= 2, validity, 0).reshape(-1)
    prev_valid = jnp.where(reach < 2, validity, 0)[:2, :2].reshape(-1)
    weights = conv_weight.reshape(9, 3 * channels, channels)
    bias = conv_bias.reshape(1, channels)
    decoded, early = own_conv(own_valid, own_wide, weights, features, bias)
    return prev_conv(prev_valid, prev_wide, weights, early, decoded)


def widen(block, left, right):
    shifted_in = jnp.concatenate([left, block[:, :, : WCOL - 1]], axis=2)
    shifted_out = jnp.concatenate([block[:, :, 1:], right], axis=2)
    return jnp.concatenate([shifted_in, block, shifted_out], axis=-1)


def own_kernel(valid_ref, x_ref, w_ref, b_ref, f_hbm, o_ref, early_ref, f_ref, acc_ref, sem):
    tap_time = pl.program_id(0)
    tap_high = pl.program_id(1)
    fetch = pltpu.make_async_copy(f_hbm, f_ref, sem)

    @pl.when((tap_time == 0) & (tap_high == 0))
    def _():
        fetch.start()
        acc_ref[...] = jnp.zeros_like(acc_ref)

    for a in range(3):

        @pl.when(tap_time == a)
        def _():
            reach = FR_DEV - 2 + a
            lhs = x_ref[:reach, pl.ds(tap_high, HR)].reshape(reach * HR * WCOL, -1)
            part = jnp.dot(lhs, w_ref[0], preferred_element_type=jnp.float32)
            for j in range(reach):
                t = j + 2 - a
                keep = valid_ref[a * FR_DEV + t].astype(jnp.float32)
                acc_ref[t] += part[j * HR * WCOL : (j + 1) * HR * WCOL] * keep

    @pl.when((tap_time == 2) & (tap_high == 2))
    def _():
        fetch.wait()
        for t in range(FR_DEV):
            total = (f_ref[t] + acc_ref[t].reshape(HR, WCOL, -1)) + b_ref[...]
            if t < 2:
                early_ref[t] = total
            else:
                o_ref[t] = total.astype(o_ref.dtype)


def own_conv(validity, wide, weights, features, bias):
    return pl.pallas_call(
        own_kernel,
        grid_spec=pltpu.PrefetchScalarGridSpec(
            num_scalar_prefetch=1,
            grid=(3, 3),
            in_specs=[
                pl.BlockSpec(wide.shape, lambda a, b, v: (0, 0, 0, 0), pipeline_mode=pl.Buffered(1)),
                pl.BlockSpec((1,) + weights.shape[1:], lambda a, b, v: (a * 3 + b, 0, 0)),
                pl.BlockSpec(bias.shape, lambda a, b, v: (0, 0), pipeline_mode=pl.Buffered(1)),
                pl.BlockSpec(memory_space=pl.ANY),
            ],
            out_specs=[
                pl.BlockSpec(features.shape, lambda a, b, v: (0, 0, 0, 0)),
                pl.BlockSpec((2,) + features.shape[1:], lambda a, b, v: (0, 0, 0, 0)),
            ],
            scratch_shapes=[
                pltpu.VMEM(features.shape, jnp.float32),
                pltpu.VMEM((features.shape[0], HR * WCOL, features.shape[-1]), jnp.float32),
                pltpu.SemaphoreType.DMA(()),
            ],
        ),
        out_shape=[
            jax.ShapeDtypeStruct(features.shape, jnp.bfloat16),
            jax.ShapeDtypeStruct((2,) + features.shape[1:], jnp.float32),
        ],
        compiler_params=pltpu.CompilerParams(
            dimension_semantics=("arbitrary", "arbitrary"), vmem_limit_bytes=60 * 1024 * 1024
        ),
    )(validity, wide, weights, bias, features)


def prev_kernel(valid_ref, x_ref, w_ref, early_ref, whole_ref, o_ref, acc_ref):
    del whole_ref
    tap_time = pl.program_id(0)
    tap_high = pl.program_id(1)

    @pl.when((tap_time == 0) & (tap_high == 0))
    def _():
        acc_ref[...] = jnp.zeros_like(acc_ref)

    for t in range(2):

        @pl.when(valid_ref[tap_time * 2 + t] != 0)
        def _():
            frame = jnp.minimum(tap_time + t, 1)
            lhs = x_ref[frame, pl.ds(tap_high, HR)].reshape(HR * WCOL, -1)
            acc_ref[t] += jnp.dot(lhs, w_ref[0], preferred_element_type=jnp.float32)

    @pl.when((tap_time == 1) & (tap_high == 2))
    def _():
        for t in range(2):
            total = early_ref[t] + acc_ref[t].reshape(HR, WCOL, -1)
            o_ref[t] = total.astype(o_ref.dtype)


def prev_conv(validity, wide, weights, early, decoded):
    return pl.pallas_call(
        prev_kernel,
        grid_spec=pltpu.PrefetchScalarGridSpec(
            num_scalar_prefetch=1,
            grid=(2, 3),
            in_specs=[
                pl.BlockSpec(wide.shape, lambda a, b, v: (0, 0, 0, 0), pipeline_mode=pl.Buffered(1)),
                pl.BlockSpec((1,) + weights.shape[1:], lambda a, b, v: (a * 3 + b, 0, 0)),
                pl.BlockSpec(early.shape, lambda a, b, v: (0, 0, 0, 0), pipeline_mode=pl.Buffered(1)),
                pl.BlockSpec(memory_space=pl.ANY),
            ],
            out_specs=pl.BlockSpec(early.shape, lambda a, b, v: (0, 0, 0, 0)),
            scratch_shapes=[pltpu.VMEM((2, HR * WCOL, early.shape[-1]), jnp.float32)],
        ),
        out_shape=jax.ShapeDtypeStruct(decoded.shape, decoded.dtype),
        input_output_aliases={4: 0},
        compiler_params=pltpu.CompilerParams(
            dimension_semantics=("arbitrary", "arbitrary"), vmem_limit_bytes=60 * 1024 * 1024
        ),
    )(validity, wide, weights, early, decoded)


def solution(mesh):
    placed = (
        P(("src", "frame", "tile"), None),
        P(("src", "frame", "tile")),
        P(),
        P(),
        P(),
        P(),
        P(),
    )
    return jax.shard_map(
        shards,
        mesh=mesh,
        in_specs=placed,
        out_specs=P("frame", "tile", "src", None),
        check_vma=False,
    )
```

```python
import jax
import jax.numpy as jnp
from jax import lax
from jax.experimental import pallas as pl
from jax.experimental.pallas import tpu as pltpu
from jax.sharding import PartitionSpec as P

GROUPS = 32
CLIPS = 4
FR_DEV = 6
HR = 8
WCOL = 32
HIGH = lax.Precision.HIGHEST


def passed_along(x, axis, by):
    peers = lax.axis_size(axis)
    pairs = [(i, i + by) for i in range(peers) if 0 <= i + by < peers]
    return lax.ppermute(x, axis, pairs)


def with_halo(x, sides, width):
    for axis, dim in sides:
        peers, length = (lax.axis_size(axis), x.shape[dim])
        up = [(i, (i + 1) % peers) for i in range(peers - 1)]
        down = [(j, i) for i, j in up]
        last = lax.slice_in_dim(x, length - width, length, axis=dim)
        leading = lax.slice_in_dim(x, 0, width, axis=dim)
        before = lax.ppermute(last, axis, up)
        after = lax.ppermute(leading, axis, down)
        x = jnp.concatenate([before, x, after], axis=dim)
    return x


def shards(feats, row_map, clip_ids, norm_gain, norm_bias, conv_weight, conv_bias):
    local_rows, channels = feats.shape
    n_src = lax.axis_size("src")
    n_frame = lax.axis_size("frame")
    n_tile = lax.axis_size("tile")
    devices = n_src * n_frame * n_tile
    per_pair = local_rows // devices
    group_width = channels // GROUPS
    per_frame = HR * WCOL

    owners = row_map // local_rows
    slot_ids = row_map % local_rows
    frames = clip_ids.shape[0]
    row_frame = (owners // n_tile) % n_frame * FR_DEV + slot_ids // per_frame
    frame_onehot = (row_frame[:, None] == jnp.arange(frames, dtype=jnp.int32)[None, :]).astype(
        jnp.float32
    )
    clip_onehot = (clip_ids[:, None] == jnp.arange(CLIPS, dtype=jnp.int32)[None, :]).astype(
        jnp.float32
    )
    row_onehot = jnp.dot(frame_onehot, clip_onehot)

    clip_mask = row_onehot.T[:, :, None]
    local_n = jnp.sum(row_onehot, axis=0) * group_width
    local_s = jnp.sum(
        jnp.sum(feats[None] * clip_mask, axis=1).reshape(CLIPS, GROUPS, group_width), axis=2
    )
    local_m = local_s / jnp.maximum(local_n, 1.0)[:, None]
    wide_m = jnp.repeat(local_m, group_width, axis=1)
    row_m = jnp.sum(clip_mask * wide_m[:, None, :], axis=0)
    dev = feats - row_m
    local_m2 = jnp.sum(
        jnp.sum((dev * dev)[None] * clip_mask, axis=1).reshape(CLIPS, GROUPS, group_width),
        axis=2,
    )

    block = 16
    iota = lax.iota(jnp.int32, local_rows)
    _, sent_slots, ordering = lax.sort((owners, slot_ids, iota), num_keys=1, is_stable=True)
    stats = jnp.concatenate([local_n, local_s.reshape(-1), local_m2.reshape(-1)])
    info = jnp.concatenate(
        [
            sent_slots.astype(jnp.float32).reshape(devices, per_pair),
            jnp.broadcast_to(stats, (devices, stats.shape[0])),
            jnp.zeros((devices, channels - per_pair - stats.shape[0]), jnp.float32),
        ],
        axis=1,
    )
    payload = jnp.concatenate(
        [
            feats[ordering.reshape(devices, per_pair)],
            info[:, None, :],
            jnp.zeros((devices, block - per_pair - 1, channels), jnp.float32),
        ],
        axis=1,
    )
    arrived = lax.all_to_all(
        payload, ("src", "frame", "tile"), split_axis=0, concat_axis=0, tiled=True
    )

    info = arrived[:, per_pair, :]
    targets = info[:, :per_pair].reshape(-1).astype(jnp.int32)
    part_n = info[:, per_pair : per_pair + CLIPS]
    base = per_pair + CLIPS
    part_s = info[:, base : base + CLIPS * GROUPS].reshape(devices, CLIPS, GROUPS)
    part_m2 = info[:, base + CLIPS * GROUPS : base + 2 * CLIPS * GROUPS].reshape(
        devices, CLIPS, GROUPS
    )
    total_n = jnp.sum(part_n, axis=0)
    clip_mean = jnp.sum(part_s, axis=0) / total_n[:, None]
    part_m = part_s / jnp.maximum(part_n, 1.0)[:, :, None]
    spread = part_m - clip_mean[None]
    clip_m2 = jnp.sum(part_m2, axis=0) + jnp.sum(part_n[:, :, None] * spread * spread, axis=0)
    clip_var = clip_m2 / total_n[:, None]

    arrival_row = (iota // per_pair) * block + iota % per_pair
    digits = jnp.stack([arrival_row // 64, arrival_row % 64], axis=1).astype(jnp.bfloat16)
    chooser = (targets[None, :] == iota[:, None]).astype(jnp.bfloat16)
    found = jnp.dot(chooser, digits, preferred_element_type=jnp.float32).astype(jnp.int32)
    gather_rows = found[:, 0] * 64 + found[:, 1]
    features = arrived.reshape(-1, channels)[gather_rows].reshape(FR_DEV, HR, WCOL, channels)

    first_frame = lax.axis_index("frame") * FR_DEV
    padded_ids = jnp.concatenate([jnp.full((2,), -1, jnp.int32), clip_ids])
    window_ids = lax.dynamic_slice_in_dim(padded_ids, first_frame, FR_DEV + 2)
    own_ids = window_ids[2:]
    onehot = (own_ids[:, None] == jnp.arange(CLIPS, dtype=jnp.int32)[None, :]).astype(jnp.float32)
    frame_mean = jnp.dot(onehot, clip_mean, precision=HIGH)
    inverse_std = 1.0 / jnp.sqrt(clip_var + 1e-06)
    frame_inv = jnp.dot(onehot, inverse_std, precision=HIGH)

    def activate(x):
        grouped = x.reshape(FR_DEV, -1, GROUPS, group_width)
        centred = grouped - frame_mean[:, None, :, None]
        normed = (centred * frame_inv[:, None, :, None]).reshape(x.shape)
        return jax.nn.silu(normed * norm_gain + norm_bias).astype(jnp.bfloat16)

    grid_rows = gather_rows.reshape(FR_DEV, HR, WCOL)
    edge_rows = jnp.concatenate(
        [grid_rows[:, 0], grid_rows[:, HR - 1], grid_rows[:, :, 0], grid_rows[:, :, WCOL - 1]],
        axis=1,
    )
    edges = activate(arrived.reshape(-1, channels)[edge_rows])
    top_own = edges[:, :WCOL]
    bottom_own = edges[:, WCOL : 2 * WCOL]
    first_col = edges[:, 2 * WCOL : 2 * WCOL + HR]
    last_col = edges[:, 2 * WCOL + HR :]
    top_halo = passed_along(bottom_own, "tile", 1)
    bottom_halo = passed_along(top_own, "tile", -1)
    left = passed_along(
        jnp.concatenate([top_halo[:, WCOL - 1 :], last_col, bottom_halo[:, WCOL - 1 :]], axis=1),
        "src",
        1,
    )[:, :, None]
    right = passed_along(
        jnp.concatenate([top_halo[:, :1], first_col, bottom_halo[:, :1]], axis=1), "src", -1
    )[:, :, None]

    activated = activate(features)
    high_padded = jnp.concatenate([top_halo[:, None], activated, bottom_halo[:, None]], axis=1)
    own_wide = widen(high_padded, left, right)
    sent_prev = jnp.concatenate(
        [high_padded[FR_DEV - 2 :], left[FR_DEV - 2 :], right[FR_DEV - 2 :]], axis=2
    )
    prev = passed_along(sent_prev, "frame", 1)
    prev_wide = widen(prev[:, :, :WCOL], prev[:, :, WCOL : WCOL + 1], prev[:, :, WCOL + 1 :])

    validity = jnp.stack(
        [(window_ids[a : a + FR_DEV] == own_ids).astype(jnp.int32) for a in range(3)]
    )
    reach = jnp.arange(3)[:, None] + jnp.arange(FR_DEV)[None, :]
    own_valid = jnp.where(reach >= 2, validity, 0).reshape(-1)
    prev_valid = jnp.where(reach < 2, validity, 0)[:2, :2].reshape(-1)
    weights = conv_weight.reshape(9, 3 * channels, channels)
    bias = conv_bias.reshape(1, channels)
    decoded, early = own_conv(own_valid, own_wide, weights, features, bias)
    return prev_conv(prev_valid, prev_wide, weights, early, decoded)


def widen(block, left, right):
    shifted_in = jnp.concatenate([left, block[:, :, : WCOL - 1]], axis=2)
    shifted_out = jnp.concatenate([block[:, :, 1:], right], axis=2)
    return jnp.concatenate([shifted_in, block, shifted_out], axis=-1)


def own_kernel(valid_ref, x_ref, w_ref, b_ref, f_hbm, o_ref, early_ref, f_ref, acc_ref, sem):
    tap_time = pl.program_id(0)
    tap_high = pl.program_id(1)
    fetch = pltpu.make_async_copy(f_hbm, f_ref, sem)

    @pl.when((tap_time == 0) & (tap_high == 0))
    def _():
        fetch.start()
        acc_ref[...] = jnp.zeros_like(acc_ref)

    for a in range(3):

        @pl.when(tap_time == a)
        def _():
            reach = FR_DEV - 2 + a
            lhs = x_ref[:reach, pl.ds(tap_high, HR)].reshape(reach * HR * WCOL, -1)
            part = jnp.dot(lhs, w_ref[0], preferred_element_type=jnp.float32)
            for j in range(reach):
                t = j + 2 - a
                keep = valid_ref[a * FR_DEV + t].astype(jnp.float32)
                acc_ref[t] += part[j * HR * WCOL : (j + 1) * HR * WCOL] * keep

    @pl.when((tap_time == 2) & (tap_high == 2))
    def _():
        fetch.wait()
        for t in range(FR_DEV):
            total = (f_ref[t] + acc_ref[t].reshape(HR, WCOL, -1)) + b_ref[...]
            if t < 2:
                early_ref[t] = total
            else:
                o_ref[t] = total.astype(o_ref.dtype)


def own_conv(validity, wide, weights, features, bias):
    return pl.pallas_call(
        own_kernel,
        grid_spec=pltpu.PrefetchScalarGridSpec(
            num_scalar_prefetch=1,
            grid=(3, 3),
            in_specs=[
                pl.BlockSpec(wide.shape, lambda a, b, v: (0, 0, 0, 0), pipeline_mode=pl.Buffered(1)),
                pl.BlockSpec((1,) + weights.shape[1:], lambda a, b, v: (a * 3 + b, 0, 0)),
                pl.BlockSpec(bias.shape, lambda a, b, v: (0, 0), pipeline_mode=pl.Buffered(1)),
                pl.BlockSpec(memory_space=pl.ANY),
            ],
            out_specs=[
                pl.BlockSpec(features.shape, lambda a, b, v: (0, 0, 0, 0)),
                pl.BlockSpec((2,) + features.shape[1:], lambda a, b, v: (0, 0, 0, 0)),
            ],
            scratch_shapes=[
                pltpu.VMEM(features.shape, jnp.float32),
                pltpu.VMEM((features.shape[0], HR * WCOL, features.shape[-1]), jnp.float32),
                pltpu.SemaphoreType.DMA(()),
            ],
        ),
        out_shape=[
            jax.ShapeDtypeStruct(features.shape, jnp.bfloat16),
            jax.ShapeDtypeStruct((2,) + features.shape[1:], jnp.float32),
        ],
        compiler_params=pltpu.CompilerParams(
            dimension_semantics=("arbitrary", "arbitrary"), vmem_limit_bytes=60 * 1024 * 1024
        ),
    )(validity, wide, weights, bias, features)


def prev_kernel(valid_ref, x_ref, w_ref, early_ref, whole_ref, o_ref, acc_ref):
    del whole_ref
    tap_time = pl.program_id(0)
    tap_high = pl.program_id(1)

    @pl.when((tap_time == 0) & (tap_high == 0))
    def _():
        acc_ref[...] = jnp.zeros_like(acc_ref)

    for t in range(2):

        @pl.when(valid_ref[tap_time * 2 + t] != 0)
        def _():
            frame = jnp.minimum(tap_time + t, 1)
            lhs = x_ref[frame, pl.ds(tap_high, HR)].reshape(HR * WCOL, -1)
            acc_ref[t] += jnp.dot(lhs, w_ref[0], preferred_element_type=jnp.float32)

    @pl.when((tap_time == 1) & (tap_high == 2))
    def _():
        for t in range(2):
            total = early_ref[t] + acc_ref[t].reshape(HR, WCOL, -1)
            o_ref[t] = total.astype(o_ref.dtype)


def prev_conv(validity, wide, weights, early, decoded):
    return pl.pallas_call(
        prev_kernel,
        grid_spec=pltpu.PrefetchScalarGridSpec(
            num_scalar_prefetch=1,
            grid=(2, 3),
            in_specs=[
                pl.BlockSpec(wide.shape, lambda a, b, v: (0, 0, 0, 0), pipeline_mode=pl.Buffered(1)),
                pl.BlockSpec((1,) + weights.shape[1:], lambda a, b, v: (a * 3 + b, 0, 0)),
                pl.BlockSpec(early.shape, lambda a, b, v: (0, 0, 0, 0), pipeline_mode=pl.Buffered(1)),
                pl.BlockSpec(memory_space=pl.ANY),
            ],
            out_specs=pl.BlockSpec(early.shape, lambda a, b, v: (0, 0, 0, 0)),
            scratch_shapes=[pltpu.VMEM((2, HR * WCOL, early.shape[-1]), jnp.float32)],
        ),
        out_shape=jax.ShapeDtypeStruct(decoded.shape, decoded.dtype),
        input_output_aliases={4: 0},
        compiler_params=pltpu.CompilerParams(
            dimension_semantics=("arbitrary", "arbitrary"), vmem_limit_bytes=60 * 1024 * 1024
        ),
    )(validity, wide, weights, early, decoded)


def solution(mesh):
    placed = (
        P(("src", "frame", "tile"), None),
        P(("src", "frame", "tile")),
        P(),
        P(),
        P(),
        P(),
        P(),
    )
    return jax.shard_map(
        shards,
        mesh=mesh,
        in_specs=placed,
        out_specs=P("frame", "tile", "src", None),
        check_vma=False,
    )
```

```python
import jax
import jax.numpy as jnp
from jax import lax
from jax.experimental import pallas as pl
from jax.experimental.pallas import tpu as pltpu
from jax.sharding import PartitionSpec as P

GROUPS = 32
CLIPS = 4
FR_DEV = 6
HR = 8
WCOL = 32
HIGH = lax.Precision.HIGHEST


def passed_along(x, axis, by):
    peers = lax.axis_size(axis)
    pairs = [(i, i + by) for i in range(peers) if 0 <= i + by < peers]
    return lax.ppermute(x, axis, pairs)


def with_halo(x, sides, width):
    for axis, dim in sides:
        peers, length = (lax.axis_size(axis), x.shape[dim])
        up = [(i, (i + 1) % peers) for i in range(peers - 1)]
        down = [(j, i) for i, j in up]
        last = lax.slice_in_dim(x, length - width, length, axis=dim)
        leading = lax.slice_in_dim(x, 0, width, axis=dim)
        before = lax.ppermute(last, axis, up)
        after = lax.ppermute(leading, axis, down)
        x = jnp.concatenate([before, x, after], axis=dim)
    return x


def shards(feats, row_map, clip_ids, norm_gain, norm_bias, conv_weight, conv_bias):
    local_rows, channels = feats.shape
    n_src = lax.axis_size("src")
    n_frame = lax.axis_size("frame")
    n_tile = lax.axis_size("tile")
    devices = n_src * n_frame * n_tile
    per_pair = local_rows // devices
    group_width = channels // GROUPS
    per_frame = HR * WCOL

    owners = row_map // local_rows
    slot_ids = row_map % local_rows
    frames = clip_ids.shape[0]
    row_frame = (owners // n_tile) % n_frame * FR_DEV + slot_ids // per_frame
    frame_onehot = (row_frame[:, None] == jnp.arange(frames, dtype=jnp.int32)[None, :]).astype(
        jnp.float32
    )
    clip_onehot = (clip_ids[:, None] == jnp.arange(CLIPS, dtype=jnp.int32)[None, :]).astype(
        jnp.float32
    )
    row_onehot = jnp.dot(frame_onehot, clip_onehot)

    clip_mask = row_onehot.T[:, :, None]
    local_n = jnp.sum(row_onehot, axis=0) * group_width
    local_s = jnp.sum(
        jnp.sum(feats[None] * clip_mask, axis=1).reshape(CLIPS, GROUPS, group_width), axis=2
    )
    local_m = local_s / jnp.maximum(local_n, 1.0)[:, None]
    wide_m = jnp.repeat(local_m, group_width, axis=1)
    row_m = jnp.sum(clip_mask * wide_m[:, None, :], axis=0)
    dev = feats - row_m
    local_m2 = jnp.sum(
        jnp.sum((dev * dev)[None] * clip_mask, axis=1).reshape(CLIPS, GROUPS, group_width),
        axis=2,
    )

    block = 16
    iota = lax.iota(jnp.int32, local_rows)
    _, sent_slots, ordering = lax.sort((owners, slot_ids, iota), num_keys=1, is_stable=True)
    stats = jnp.concatenate([local_n, local_s.reshape(-1), local_m2.reshape(-1)])
    info = jnp.concatenate(
        [
            sent_slots.astype(jnp.float32).reshape(devices, per_pair),
            jnp.broadcast_to(stats, (devices, stats.shape[0])),
            jnp.zeros((devices, channels - per_pair - stats.shape[0]), jnp.float32),
        ],
        axis=1,
    )
    payload = jnp.concatenate(
        [
            feats[ordering.reshape(devices, per_pair)],
            info[:, None, :],
            jnp.zeros((devices, block - per_pair - 1, channels), jnp.float32),
        ],
        axis=1,
    )
    arrived = lax.all_to_all(
        payload, ("src", "frame", "tile"), split_axis=0, concat_axis=0, tiled=True
    )

    info = arrived[:, per_pair, :]
    targets = info[:, :per_pair].reshape(-1).astype(jnp.int32)
    part_n = info[:, per_pair : per_pair + CLIPS]
    base = per_pair + CLIPS
    part_s = info[:, base : base + CLIPS * GROUPS].reshape(devices, CLIPS, GROUPS)
    part_m2 = info[:, base + CLIPS * GROUPS : base + 2 * CLIPS * GROUPS].reshape(
        devices, CLIPS, GROUPS
    )
    total_n = jnp.sum(part_n, axis=0)
    clip_mean = jnp.sum(part_s, axis=0) / total_n[:, None]
    part_m = part_s / jnp.maximum(part_n, 1.0)[:, :, None]
    spread = part_m - clip_mean[None]
    clip_m2 = jnp.sum(part_m2, axis=0) + jnp.sum(part_n[:, :, None] * spread * spread, axis=0)
    clip_var = clip_m2 / total_n[:, None]

    arrival_row = (iota // per_pair) * block + iota % per_pair
    digits = jnp.stack([arrival_row // 64, arrival_row % 64], axis=1).astype(jnp.bfloat16)
    chooser = (targets[None, :] == iota[:, None]).astype(jnp.bfloat16)
    found = jnp.dot(chooser, digits, preferred_element_type=jnp.float32).astype(jnp.int32)
    gather_rows = found[:, 0] * 64 + found[:, 1]
    features = arrived.reshape(-1, channels)[gather_rows].reshape(FR_DEV, HR, WCOL, channels)

    first_frame = lax.axis_index("frame") * FR_DEV
    padded_ids = jnp.concatenate([jnp.full((2,), -1, jnp.int32), clip_ids])
    window_ids = lax.dynamic_slice_in_dim(padded_ids, first_frame, FR_DEV + 2)
    own_ids = window_ids[2:]
    onehot = (own_ids[:, None] == jnp.arange(CLIPS, dtype=jnp.int32)[None, :]).astype(jnp.float32)
    shaped = features.reshape(FR_DEV, per_frame, GROUPS, group_width)
    frame_mean = jnp.dot(onehot, clip_mean, precision=HIGH)
    centred = shaped - frame_mean[:, None, :, None]
    inverse_std = 1.0 / jnp.sqrt(clip_var + 1e-06)
    frame_inv = jnp.dot(onehot, inverse_std, precision=HIGH)
    normed = (centred * frame_inv[:, None, :, None]).reshape(FR_DEV, HR, WCOL, channels)
    activated = jax.nn.silu(normed * norm_gain + norm_bias).astype(jnp.bfloat16)
    high_padded = with_halo(activated, (("tile", 1),), 1)
    n_wide = lax.axis_size("src")
    up = [(i, i + 1) for i in range(n_wide - 1)]
    left = lax.ppermute(high_padded[:, :, WCOL - 1 :], "src", up)
    right = lax.ppermute(high_padded[:, :, :1], "src", [(j, i) for i, j in up])
    own_wide = widen(high_padded, left, right)
    prev_wide = passed_along(own_wide[FR_DEV - 2 :], "frame", 1)

    validity = jnp.stack(
        [(window_ids[a : a + FR_DEV] == own_ids).astype(jnp.int32) for a in range(3)]
    )
    reach = jnp.arange(3)[:, None] + jnp.arange(FR_DEV)[None, :]
    own_valid = jnp.where(reach >= 2, validity, 0).reshape(-1)
    prev_valid = jnp.where(reach < 2, validity, 0)[:2, :2].reshape(-1)
    weights = conv_weight.reshape(9, 3 * channels, channels)
    bias = conv_bias.reshape(1, channels)
    decoded, early = own_conv(own_valid, own_wide, weights, features, bias)
    return prev_conv(prev_valid, prev_wide, weights, early, decoded)


def widen(block, left, right):
    shifted_in = jnp.concatenate([left, block[:, :, : WCOL - 1]], axis=2)
    shifted_out = jnp.concatenate([block[:, :, 1:], right], axis=2)
    return jnp.concatenate([shifted_in, block, shifted_out], axis=-1)


def own_kernel(valid_ref, x_ref, w_ref, b_ref, f_hbm, o_ref, early_ref, f_ref, acc_ref, sem):
    tap_time = pl.program_id(0)
    tap_high = pl.program_id(1)
    fetch = pltpu.make_async_copy(f_hbm, f_ref, sem)

    @pl.when((tap_time == 0) & (tap_high == 0))
    def _():
        fetch.start()
        acc_ref[...] = jnp.zeros_like(acc_ref)

    for a in range(3):

        @pl.when(tap_time == a)
        def _():
            reach = FR_DEV - 2 + a
            lhs = x_ref[:reach, pl.ds(tap_high, HR)].reshape(reach * HR * WCOL, -1)
            part = jnp.dot(lhs, w_ref[0], preferred_element_type=jnp.float32)
            for j in range(reach):
                t = j + 2 - a
                keep = valid_ref[a * FR_DEV + t].astype(jnp.float32)
                acc_ref[t] += part[j * HR * WCOL : (j + 1) * HR * WCOL] * keep

    @pl.when((tap_time == 2) & (tap_high == 2))
    def _():
        fetch.wait()
        for t in range(FR_DEV):
            total = (f_ref[t] + acc_ref[t].reshape(HR, WCOL, -1)) + b_ref[...]
            if t < 2:
                early_ref[t] = total
            else:
                o_ref[t] = total.astype(o_ref.dtype)


def own_conv(validity, wide, weights, features, bias):
    return pl.pallas_call(
        own_kernel,
        grid_spec=pltpu.PrefetchScalarGridSpec(
            num_scalar_prefetch=1,
            grid=(3, 3),
            in_specs=[
                pl.BlockSpec(wide.shape, lambda a, b, v: (0, 0, 0, 0), pipeline_mode=pl.Buffered(1)),
                pl.BlockSpec((1,) + weights.shape[1:], lambda a, b, v: (a * 3 + b, 0, 0)),
                pl.BlockSpec(bias.shape, lambda a, b, v: (0, 0), pipeline_mode=pl.Buffered(1)),
                pl.BlockSpec(memory_space=pl.ANY),
            ],
            out_specs=[
                pl.BlockSpec(features.shape, lambda a, b, v: (0, 0, 0, 0)),
                pl.BlockSpec((2,) + features.shape[1:], lambda a, b, v: (0, 0, 0, 0)),
            ],
            scratch_shapes=[
                pltpu.VMEM(features.shape, jnp.float32),
                pltpu.VMEM((features.shape[0], HR * WCOL, features.shape[-1]), jnp.float32),
                pltpu.SemaphoreType.DMA(()),
            ],
        ),
        out_shape=[
            jax.ShapeDtypeStruct(features.shape, jnp.bfloat16),
            jax.ShapeDtypeStruct((2,) + features.shape[1:], jnp.float32),
        ],
        compiler_params=pltpu.CompilerParams(
            dimension_semantics=("arbitrary", "arbitrary"), vmem_limit_bytes=60 * 1024 * 1024
        ),
    )(validity, wide, weights, bias, features)


def prev_kernel(valid_ref, x_ref, w_ref, early_ref, whole_ref, o_ref, acc_ref):
    del whole_ref
    tap_time = pl.program_id(0)
    tap_high = pl.program_id(1)

    @pl.when((tap_time == 0) & (tap_high == 0))
    def _():
        acc_ref[...] = jnp.zeros_like(acc_ref)

    for t in range(2):

        @pl.when(valid_ref[tap_time * 2 + t] != 0)
        def _():
            frame = jnp.minimum(tap_time + t, 1)
            lhs = x_ref[frame, pl.ds(tap_high, HR)].reshape(HR * WCOL, -1)
            acc_ref[t] += jnp.dot(lhs, w_ref[0], preferred_element_type=jnp.float32)

    @pl.when((tap_time == 1) & (tap_high == 2))
    def _():
        for t in range(2):
            total = early_ref[t] + acc_ref[t].reshape(HR, WCOL, -1)
            o_ref[t] = total.astype(o_ref.dtype)


def prev_conv(validity, wide, weights, early, decoded):
    return pl.pallas_call(
        prev_kernel,
        grid_spec=pltpu.PrefetchScalarGridSpec(
            num_scalar_prefetch=1,
            grid=(2, 3),
            in_specs=[
                pl.BlockSpec(wide.shape, lambda a, b, v: (0, 0, 0, 0), pipeline_mode=pl.Buffered(1)),
                pl.BlockSpec((1,) + weights.shape[1:], lambda a, b, v: (a * 3 + b, 0, 0)),
                pl.BlockSpec(early.shape, lambda a, b, v: (0, 0, 0, 0), pipeline_mode=pl.Buffered(1)),
                pl.BlockSpec(memory_space=pl.ANY),
            ],
            out_specs=pl.BlockSpec(early.shape, lambda a, b, v: (0, 0, 0, 0)),
            scratch_shapes=[pltpu.VMEM((2, HR * WCOL, early.shape[-1]), jnp.float32)],
        ),
        out_shape=jax.ShapeDtypeStruct(decoded.shape, decoded.dtype),
        input_output_aliases={4: 0},
        compiler_params=pltpu.CompilerParams(
            dimension_semantics=("arbitrary", "arbitrary"), vmem_limit_bytes=60 * 1024 * 1024
        ),
    )(validity, wide, weights, early, decoded)


def solution(mesh):
    placed = (
        P(("src", "frame", "tile"), None),
        P(("src", "frame", "tile")),
        P(),
        P(),
        P(),
        P(),
        P(),
    )
    return jax.shard_map(
        shards,
        mesh=mesh,
        in_specs=placed,
        out_specs=P("frame", "tile", "src", None),
        check_vma=False,
    )
```

```python
import jax
import jax.numpy as jnp
from jax import lax
from jax.experimental import pallas as pl
from jax.experimental.pallas import tpu as pltpu
from jax.sharding import PartitionSpec as P

GROUPS = 32
CLIPS = 4
FR_DEV = 6
HR = 8
WCOL = 32
HIGH = lax.Precision.HIGHEST


def passed_along(x, axis, by):
    peers = lax.axis_size(axis)
    pairs = [(i, i + by) for i in range(peers) if 0 <= i + by < peers]
    return lax.ppermute(x, axis, pairs)


def with_halo(x, sides, width):
    for axis, dim in sides:
        peers, length = (lax.axis_size(axis), x.shape[dim])
        up = [(i, (i + 1) % peers) for i in range(peers - 1)]
        down = [(j, i) for i, j in up]
        last = lax.slice_in_dim(x, length - width, length, axis=dim)
        leading = lax.slice_in_dim(x, 0, width, axis=dim)
        before = lax.ppermute(last, axis, up)
        after = lax.ppermute(leading, axis, down)
        x = jnp.concatenate([before, x, after], axis=dim)
    return x


def shards(feats, row_map, clip_ids, norm_gain, norm_bias, conv_weight, conv_bias):
    local_rows, channels = feats.shape
    n_src = lax.axis_size("src")
    n_frame = lax.axis_size("frame")
    n_tile = lax.axis_size("tile")
    devices = n_src * n_frame * n_tile
    per_pair = local_rows // devices
    group_width = channels // GROUPS
    per_frame = HR * WCOL

    owners = row_map // local_rows
    slot_ids = row_map % local_rows
    frames = clip_ids.shape[0]
    row_frame = (owners // n_tile) % n_frame * FR_DEV + slot_ids // per_frame
    frame_onehot = (row_frame[:, None] == jnp.arange(frames, dtype=jnp.int32)[None, :]).astype(
        jnp.float32
    )
    clip_onehot = (clip_ids[:, None] == jnp.arange(CLIPS, dtype=jnp.int32)[None, :]).astype(
        jnp.float32
    )
    row_onehot = jnp.dot(frame_onehot, clip_onehot)

    clip_mask = row_onehot.T[:, :, None]
    local_n = jnp.sum(row_onehot, axis=0) * group_width
    local_s = jnp.sum(
        jnp.sum(feats[None] * clip_mask, axis=1).reshape(CLIPS, GROUPS, group_width), axis=2
    )
    local_m = local_s / jnp.maximum(local_n, 1.0)[:, None]
    wide_m = jnp.repeat(local_m, group_width, axis=1)
    row_m = jnp.sum(clip_mask * wide_m[:, None, :], axis=0)
    dev = feats - row_m
    local_m2 = jnp.sum(
        jnp.sum((dev * dev)[None] * clip_mask, axis=1).reshape(CLIPS, GROUPS, group_width),
        axis=2,
    )

    block = 16
    iota = lax.iota(jnp.int32, local_rows)
    _, sent_slots, ordering = lax.sort((owners, slot_ids, iota), num_keys=1, is_stable=True)
    stats = jnp.concatenate([local_n, local_s.reshape(-1), local_m2.reshape(-1)])
    info = jnp.concatenate(
        [
            sent_slots.astype(jnp.float32).reshape(devices, per_pair),
            jnp.broadcast_to(stats, (devices, stats.shape[0])),
            jnp.zeros((devices, channels - per_pair - stats.shape[0]), jnp.float32),
        ],
        axis=1,
    )
    pick = jnp.concatenate(
        [ordering.reshape(devices, per_pair), jnp.zeros((devices, block - per_pair), jnp.int32)],
        axis=1,
    )
    is_info = (jnp.arange(block) == per_pair)[None, :, None]
    payload = jnp.where(
        is_info, info[:, None, :], feats[pick.reshape(-1)].reshape(devices, block, channels)
    )
    arrived = lax.all_to_all(
        payload, ("src", "frame", "tile"), split_axis=0, concat_axis=0, tiled=True
    )

    info = arrived[:, per_pair, :]
    targets = info[:, :per_pair].reshape(-1).astype(jnp.int32)
    part_n = info[:, per_pair : per_pair + CLIPS]
    base = per_pair + CLIPS
    part_s = info[:, base : base + CLIPS * GROUPS].reshape(devices, CLIPS, GROUPS)
    part_m2 = info[:, base + CLIPS * GROUPS : base + 2 * CLIPS * GROUPS].reshape(
        devices, CLIPS, GROUPS
    )
    total_n = jnp.sum(part_n, axis=0)
    clip_mean = jnp.sum(part_s, axis=0) / total_n[:, None]
    part_m = part_s / jnp.maximum(part_n, 1.0)[:, :, None]
    spread = part_m - clip_mean[None]
    clip_m2 = jnp.sum(part_m2, axis=0) + jnp.sum(part_n[:, :, None] * spread * spread, axis=0)
    clip_var = clip_m2 / total_n[:, None]

    arrival_row = (iota // per_pair) * block + iota % per_pair
    digits = jnp.stack([arrival_row // 64, arrival_row % 64], axis=1).astype(jnp.bfloat16)
    chooser = (targets[None, :] == iota[:, None]).astype(jnp.bfloat16)
    found = jnp.dot(chooser, digits, preferred_element_type=jnp.float32).astype(jnp.int32)
    gather_rows = found[:, 0] * 64 + found[:, 1]
    features = arrived.reshape(-1, channels)[gather_rows].reshape(FR_DEV, HR, WCOL, channels)

    first_frame = lax.axis_index("frame") * FR_DEV
    padded_ids = jnp.concatenate([jnp.full((2,), -1, jnp.int32), clip_ids])
    window_ids = lax.dynamic_slice_in_dim(padded_ids, first_frame, FR_DEV + 2)
    own_ids = window_ids[2:]
    onehot = (own_ids[:, None] == jnp.arange(CLIPS, dtype=jnp.int32)[None, :]).astype(jnp.float32)
    shaped = features.reshape(FR_DEV, per_frame, GROUPS, group_width)
    frame_mean = jnp.dot(onehot, clip_mean, precision=HIGH)
    centred = shaped - frame_mean[:, None, :, None]
    inverse_std = 1.0 / jnp.sqrt(clip_var + 1e-06)
    frame_inv = jnp.dot(onehot, inverse_std, precision=HIGH)
    normed = (centred * frame_inv[:, None, :, None]).reshape(FR_DEV, HR, WCOL, channels)
    activated = jax.nn.silu(normed * norm_gain + norm_bias).astype(jnp.bfloat16)
    high_padded = with_halo(activated, (("tile", 1),), 1)
    n_wide = lax.axis_size("src")
    up = [(i, i + 1) for i in range(n_wide - 1)]
    left = lax.ppermute(high_padded[:, :, WCOL - 1 :], "src", up)
    right = lax.ppermute(high_padded[:, :, :1], "src", [(j, i) for i, j in up])
    own_wide = widen(high_padded, left, right)
    sent_prev = jnp.concatenate(
        [high_padded[FR_DEV - 2 :], left[FR_DEV - 2 :], right[FR_DEV - 2 :]], axis=2
    )
    prev = passed_along(sent_prev, "frame", 1)
    prev_wide = widen(prev[:, :, :WCOL], prev[:, :, WCOL : WCOL + 1], prev[:, :, WCOL + 1 :])

    validity = jnp.stack(
        [(window_ids[a : a + FR_DEV] == own_ids).astype(jnp.int32) for a in range(3)]
    )
    reach = jnp.arange(3)[:, None] + jnp.arange(FR_DEV)[None, :]
    own_valid = jnp.where(reach >= 2, validity, 0).reshape(-1)
    prev_valid = jnp.where(reach < 2, validity, 0)[:2, :2].reshape(-1)
    weights = conv_weight.reshape(9, 3 * channels, channels)
    bias = conv_bias.reshape(1, channels)
    decoded, early = own_conv(own_valid, own_wide, weights, features, bias)
    return prev_conv(prev_valid, prev_wide, weights, early, decoded)


def widen(block, left, right):
    shifted_in = jnp.concatenate([left, block[:, :, : WCOL - 1]], axis=2)
    shifted_out = jnp.concatenate([block[:, :, 1:], right], axis=2)
    return jnp.concatenate([shifted_in, block, shifted_out], axis=-1)


def own_kernel(valid_ref, x_ref, w_ref, b_ref, f_hbm, o_ref, early_ref, f_ref, acc_ref, sem):
    tap_time = pl.program_id(0)
    tap_high = pl.program_id(1)
    fetch = pltpu.make_async_copy(f_hbm, f_ref, sem)

    @pl.when((tap_time == 0) & (tap_high == 0))
    def _():
        fetch.start()
        acc_ref[...] = jnp.zeros_like(acc_ref)

    for a in range(3):

        @pl.when(tap_time == a)
        def _():
            reach = FR_DEV - 2 + a
            lhs = x_ref[:reach, pl.ds(tap_high, HR)].reshape(reach * HR * WCOL, -1)
            part = jnp.dot(lhs, w_ref[0], preferred_element_type=jnp.float32)
            for j in range(reach):
                t = j + 2 - a
                keep = valid_ref[a * FR_DEV + t].astype(jnp.float32)
                acc_ref[t] += part[j * HR * WCOL : (j + 1) * HR * WCOL] * keep

    @pl.when((tap_time == 2) & (tap_high == 2))
    def _():
        fetch.wait()
        for t in range(FR_DEV):
            total = (f_ref[t] + acc_ref[t].reshape(HR, WCOL, -1)) + b_ref[...]
            if t < 2:
                early_ref[t] = total
            else:
                o_ref[t] = total.astype(o_ref.dtype)


def own_conv(validity, wide, weights, features, bias):
    return pl.pallas_call(
        own_kernel,
        grid_spec=pltpu.PrefetchScalarGridSpec(
            num_scalar_prefetch=1,
            grid=(3, 3),
            in_specs=[
                pl.BlockSpec(wide.shape, lambda a, b, v: (0, 0, 0, 0), pipeline_mode=pl.Buffered(1)),
                pl.BlockSpec((1,) + weights.shape[1:], lambda a, b, v: (a * 3 + b, 0, 0)),
                pl.BlockSpec(bias.shape, lambda a, b, v: (0, 0), pipeline_mode=pl.Buffered(1)),
                pl.BlockSpec(memory_space=pl.ANY),
            ],
            out_specs=[
                pl.BlockSpec(features.shape, lambda a, b, v: (0, 0, 0, 0)),
                pl.BlockSpec((2,) + features.shape[1:], lambda a, b, v: (0, 0, 0, 0)),
            ],
            scratch_shapes=[
                pltpu.VMEM(features.shape, jnp.float32),
                pltpu.VMEM((features.shape[0], HR * WCOL, features.shape[-1]), jnp.float32),
                pltpu.SemaphoreType.DMA(()),
            ],
        ),
        out_shape=[
            jax.ShapeDtypeStruct(features.shape, jnp.bfloat16),
            jax.ShapeDtypeStruct((2,) + features.shape[1:], jnp.float32),
        ],
        compiler_params=pltpu.CompilerParams(
            dimension_semantics=("arbitrary", "arbitrary"), vmem_limit_bytes=60 * 1024 * 1024
        ),
    )(validity, wide, weights, bias, features)


def prev_kernel(valid_ref, x_ref, w_ref, early_ref, whole_ref, o_ref, acc_ref):
    del whole_ref
    tap_time = pl.program_id(0)
    tap_high = pl.program_id(1)

    @pl.when((tap_time == 0) & (tap_high == 0))
    def _():
        acc_ref[...] = jnp.zeros_like(acc_ref)

    for t in range(2):

        @pl.when(valid_ref[tap_time * 2 + t] != 0)
        def _():
            frame = jnp.minimum(tap_time + t, 1)
            lhs = x_ref[frame, pl.ds(tap_high, HR)].reshape(HR * WCOL, -1)
            acc_ref[t] += jnp.dot(lhs, w_ref[0], preferred_element_type=jnp.float32)

    @pl.when((tap_time == 1) & (tap_high == 2))
    def _():
        for t in range(2):
            total = early_ref[t] + acc_ref[t].reshape(HR, WCOL, -1)
            o_ref[t] = total.astype(o_ref.dtype)


def prev_conv(validity, wide, weights, early, decoded):
    return pl.pallas_call(
        prev_kernel,
        grid_spec=pltpu.PrefetchScalarGridSpec(
            num_scalar_prefetch=1,
            grid=(2, 3),
            in_specs=[
                pl.BlockSpec(wide.shape, lambda a, b, v: (0, 0, 0, 0), pipeline_mode=pl.Buffered(1)),
                pl.BlockSpec((1,) + weights.shape[1:], lambda a, b, v: (a * 3 + b, 0, 0)),
                pl.BlockSpec(early.shape, lambda a, b, v: (0, 0, 0, 0), pipeline_mode=pl.Buffered(1)),
                pl.BlockSpec(memory_space=pl.ANY),
            ],
            out_specs=pl.BlockSpec(early.shape, lambda a, b, v: (0, 0, 0, 0)),
            scratch_shapes=[pltpu.VMEM((2, HR * WCOL, early.shape[-1]), jnp.float32)],
        ),
        out_shape=jax.ShapeDtypeStruct(decoded.shape, decoded.dtype),
        input_output_aliases={4: 0},
        compiler_params=pltpu.CompilerParams(
            dimension_semantics=("arbitrary", "arbitrary"), vmem_limit_bytes=60 * 1024 * 1024
        ),
    )(validity, wide, weights, early, decoded)


def solution(mesh):
    placed = (
        P(("src", "frame", "tile"), None),
        P(("src", "frame", "tile")),
        P(),
        P(),
        P(),
        P(),
        P(),
    )
    return jax.shard_map(
        shards,
        mesh=mesh,
        in_specs=placed,
        out_specs=P("frame", "tile", "src", None),
        check_vma=False,
    )
```

```python
import jax
import jax.numpy as jnp
from jax import lax
from jax.experimental import pallas as pl
from jax.experimental.pallas import tpu as pltpu
from jax.sharding import PartitionSpec as P

GROUPS = 32
CLIPS = 4
FR_DEV = 6
HR = 8
WCOL = 32
HIGH = lax.Precision.HIGHEST


def passed_along(x, axis, by):
    peers = lax.axis_size(axis)
    pairs = [(i, i + by) for i in range(peers) if 0 <= i + by < peers]
    return lax.ppermute(x, axis, pairs)


def with_halo(x, sides, width):
    for axis, dim in sides:
        peers, length = (lax.axis_size(axis), x.shape[dim])
        up = [(i, (i + 1) % peers) for i in range(peers - 1)]
        down = [(j, i) for i, j in up]
        last = lax.slice_in_dim(x, length - width, length, axis=dim)
        leading = lax.slice_in_dim(x, 0, width, axis=dim)
        before = lax.ppermute(last, axis, up)
        after = lax.ppermute(leading, axis, down)
        x = jnp.concatenate([before, x, after], axis=dim)
    return x


def shards(feats, row_map, clip_ids, norm_gain, norm_bias, conv_weight, conv_bias):
    local_rows, channels = feats.shape
    n_src = lax.axis_size("src")
    n_frame = lax.axis_size("frame")
    n_tile = lax.axis_size("tile")
    devices = n_src * n_frame * n_tile
    per_pair = local_rows // devices
    group_width = channels // GROUPS
    per_frame = HR * WCOL

    owners = row_map // local_rows
    slot_ids = row_map % local_rows
    frames = clip_ids.shape[0]
    row_frame = (owners // n_tile) % n_frame * FR_DEV + slot_ids // per_frame
    frame_onehot = (row_frame[:, None] == jnp.arange(frames, dtype=jnp.int32)[None, :]).astype(
        jnp.float32
    )
    clip_onehot = (clip_ids[:, None] == jnp.arange(CLIPS, dtype=jnp.int32)[None, :]).astype(
        jnp.float32
    )
    row_onehot = jnp.dot(frame_onehot, clip_onehot)

    clip_mask = row_onehot.T[:, :, None]
    local_n = jnp.sum(row_onehot, axis=0) * group_width
    local_s = jnp.sum(
        jnp.sum(feats[None] * clip_mask, axis=1).reshape(CLIPS, GROUPS, group_width), axis=2
    )
    local_m = local_s / jnp.maximum(local_n, 1.0)[:, None]
    wide_m = jnp.repeat(local_m, group_width, axis=1)
    row_m = jnp.sum(clip_mask * wide_m[:, None, :], axis=0)
    dev = feats - row_m
    local_m2 = jnp.sum(
        jnp.sum((dev * dev)[None] * clip_mask, axis=1).reshape(CLIPS, GROUPS, group_width),
        axis=2,
    )

    block = 16
    iota = lax.iota(jnp.int32, local_rows)
    _, sent_slots, ordering = lax.sort((owners, slot_ids, iota), num_keys=1, is_stable=True)
    stats = jnp.concatenate([local_n, local_s.reshape(-1), local_m2.reshape(-1)])
    info = jnp.concatenate(
        [
            sent_slots.astype(jnp.float32).reshape(devices, per_pair),
            jnp.broadcast_to(stats, (devices, stats.shape[0])),
            jnp.zeros((devices, channels - per_pair - stats.shape[0]), jnp.float32),
        ],
        axis=1,
    )
    pick = jnp.concatenate(
        [ordering.reshape(devices, per_pair), jnp.zeros((devices, block - per_pair), jnp.int32)],
        axis=1,
    )
    is_info = (jnp.arange(block) == per_pair)[None, :, None]
    payload = jnp.where(
        is_info, info[:, None, :], feats[pick.reshape(-1)].reshape(devices, block, channels)
    )
    arrived = lax.all_to_all(
        payload, ("src", "frame", "tile"), split_axis=0, concat_axis=0, tiled=True
    )

    info = arrived[:, per_pair, :]
    targets = info[:, :per_pair].reshape(-1).astype(jnp.int32)
    part_n = info[:, per_pair : per_pair + CLIPS]
    base = per_pair + CLIPS
    part_s = info[:, base : base + CLIPS * GROUPS].reshape(devices, CLIPS, GROUPS)
    part_m2 = info[:, base + CLIPS * GROUPS : base + 2 * CLIPS * GROUPS].reshape(
        devices, CLIPS, GROUPS
    )
    total_n = jnp.sum(part_n, axis=0)
    clip_mean = jnp.sum(part_s, axis=0) / total_n[:, None]
    part_m = part_s / jnp.maximum(part_n, 1.0)[:, :, None]
    spread = part_m - clip_mean[None]
    clip_m2 = jnp.sum(part_m2, axis=0) + jnp.sum(part_n[:, :, None] * spread * spread, axis=0)
    clip_var = clip_m2 / total_n[:, None]

    arrival_row = (iota // per_pair) * block + iota % per_pair
    digits = jnp.stack([arrival_row // 64, arrival_row % 64], axis=1).astype(jnp.bfloat16)
    chooser = (targets[None, :] == iota[:, None]).astype(jnp.bfloat16)
    found = jnp.dot(chooser, digits, preferred_element_type=jnp.float32).astype(jnp.int32)
    gather_rows = found[:, 0] * 64 + found[:, 1]
    features = arrived.reshape(-1, channels)[gather_rows].reshape(FR_DEV, HR, WCOL, channels)

    first_frame = lax.axis_index("frame") * FR_DEV
    padded_ids = jnp.concatenate([jnp.full((2,), -1, jnp.int32), clip_ids])
    window_ids = lax.dynamic_slice_in_dim(padded_ids, first_frame, FR_DEV + 2)
    own_ids = window_ids[2:]
    onehot = (own_ids[:, None] == jnp.arange(CLIPS, dtype=jnp.int32)[None, :]).astype(jnp.float32)
    shaped = features.reshape(FR_DEV, per_frame, GROUPS, group_width)
    frame_mean = jnp.dot(onehot, clip_mean, precision=HIGH)
    centred = shaped - frame_mean[:, None, :, None]
    inverse_std = 1.0 / jnp.sqrt(clip_var + 1e-06)
    frame_inv = jnp.dot(onehot, inverse_std, precision=HIGH)
    normed = (centred * frame_inv[:, None, :, None]).reshape(FR_DEV, HR, WCOL, channels)
    activated = jax.nn.silu(normed * norm_gain + norm_bias).astype(jnp.bfloat16)
    high_padded = with_halo(activated, (("tile", 1),), 1)
    n_wide = lax.axis_size("src")
    up = [(i, i + 1) for i in range(n_wide - 1)]
    left = lax.ppermute(high_padded[:, :, WCOL - 1 :], "src", up)
    right = lax.ppermute(high_padded[:, :, :1], "src", [(j, i) for i, j in up])
    own_wide = widen(high_padded, left, right)
    sent_prev = jnp.concatenate(
        [high_padded[FR_DEV - 2 :], left[FR_DEV - 2 :], right[FR_DEV - 2 :]], axis=2
    )
    prev = passed_along(sent_prev, "frame", 1)
    prev_wide = widen(prev[:, :, :WCOL], prev[:, :, WCOL : WCOL + 1], prev[:, :, WCOL + 1 :])

    validity = jnp.stack(
        [(window_ids[a : a + FR_DEV] == own_ids).astype(jnp.int32) for a in range(3)]
    )
    reach = jnp.arange(3)[:, None] + jnp.arange(FR_DEV)[None, :]
    own_valid = jnp.where(reach >= 2, validity, 0).reshape(-1)
    prev_valid = jnp.where(reach < 2, validity, 0)[:2, :2].reshape(-1)
    weights = conv_weight.reshape(9, 3 * channels, channels)
    bias = conv_bias.reshape(1, channels)
    decoded, early = own_conv(own_valid, own_wide, weights, features, bias)
    return prev_conv(prev_valid, prev_wide, weights, early, decoded)


def widen(block, left, right):
    shifted_in = jnp.concatenate([left, block[:, :, : WCOL - 1]], axis=2)
    shifted_out = jnp.concatenate([block[:, :, 1:], right], axis=2)
    return jnp.concatenate([shifted_in, block, shifted_out], axis=-1)


def own_kernel(valid_ref, x_ref, w_ref, b_ref, f_hbm, o_ref, early_ref, f_ref, acc_ref, sem):
    tap_time = pl.program_id(0)
    tap_high = pl.program_id(1)
    fetch = pltpu.make_async_copy(f_hbm, f_ref, sem)

    @pl.when((tap_time == 0) & (tap_high == 0))
    def _():
        fetch.start()
        acc_ref[...] = jnp.zeros_like(acc_ref)

    for a in range(3):

        @pl.when(tap_time == a)
        def _():
            reach = FR_DEV - 2 + a
            lhs = x_ref[:reach, pl.ds(tap_high, HR)].reshape(reach * HR * WCOL, -1)
            part = jnp.dot(lhs, w_ref[0], preferred_element_type=jnp.float32)
            for j in range(reach):
                t = j + 2 - a
                keep = valid_ref[a * FR_DEV + t].astype(jnp.float32)
                acc_ref[t] += part[j * HR * WCOL : (j + 1) * HR * WCOL] * keep

    @pl.when((tap_time == 2) & (tap_high == 2))
    def _():
        fetch.wait()
        for t in range(FR_DEV):
            total = (f_ref[t] + acc_ref[t].reshape(HR, WCOL, -1)) + b_ref[...]
            if t < 2:
                early_ref[t] = total
            else:
                o_ref[t] = total.astype(o_ref.dtype)


def own_conv(validity, wide, weights, features, bias):
    return pl.pallas_call(
        own_kernel,
        grid_spec=pltpu.PrefetchScalarGridSpec(
            num_scalar_prefetch=1,
            grid=(3, 3),
            in_specs=[
                pl.BlockSpec(wide.shape, lambda a, b, v: (0, 0, 0, 0), pipeline_mode=pl.Buffered(1)),
                pl.BlockSpec((1,) + weights.shape[1:], lambda a, b, v: (a * 3 + b, 0, 0)),
                pl.BlockSpec(bias.shape, lambda a, b, v: (0, 0), pipeline_mode=pl.Buffered(1)),
                pl.BlockSpec(memory_space=pl.ANY),
            ],
            out_specs=[
                pl.BlockSpec(features.shape, lambda a, b, v: (0, 0, 0, 0)),
                pl.BlockSpec((2,) + features.shape[1:], lambda a, b, v: (0, 0, 0, 0)),
            ],
            scratch_shapes=[
                pltpu.VMEM(features.shape, jnp.float32),
                pltpu.VMEM((features.shape[0], HR * WCOL, features.shape[-1]), jnp.float32),
                pltpu.SemaphoreType.DMA(()),
            ],
        ),
        out_shape=[
            jax.ShapeDtypeStruct(features.shape, jnp.bfloat16),
            jax.ShapeDtypeStruct((2,) + features.shape[1:], jnp.float32),
        ],
        compiler_params=pltpu.CompilerParams(
            dimension_semantics=("arbitrary", "arbitrary"), vmem_limit_bytes=60 * 1024 * 1024
        ),
    )(validity, wide, weights, bias, features)


def prev_kernel(valid_ref, x_ref, w_ref, early_ref, whole_ref, o_ref, acc_ref):
    del whole_ref
    tap_time = pl.program_id(0)
    tap_high = pl.program_id(1)

    @pl.when((tap_time == 0) & (tap_high == 0))
    def _():
        acc_ref[...] = jnp.zeros_like(acc_ref)

    for a in range(2):

        @pl.when(tap_time == a)
        def _():
            reach = 2 - a
            lhs = x_ref[a : a + reach, pl.ds(tap_high, HR)].reshape(reach * HR * WCOL, -1)
            part = jnp.dot(lhs, w_ref[0], preferred_element_type=jnp.float32)
            for t in range(reach):
                keep = valid_ref[a * 2 + t].astype(jnp.float32)
                acc_ref[t] += part[t * HR * WCOL : (t + 1) * HR * WCOL] * keep

    @pl.when((tap_time == 1) & (tap_high == 2))
    def _():
        for t in range(2):
            total = early_ref[t] + acc_ref[t].reshape(HR, WCOL, -1)
            o_ref[t] = total.astype(o_ref.dtype)


def prev_conv(validity, wide, weights, early, decoded):
    return pl.pallas_call(
        prev_kernel,
        grid_spec=pltpu.PrefetchScalarGridSpec(
            num_scalar_prefetch=1,
            grid=(2, 3),
            in_specs=[
                pl.BlockSpec(wide.shape, lambda a, b, v: (0, 0, 0, 0), pipeline_mode=pl.Buffered(1)),
                pl.BlockSpec((1,) + weights.shape[1:], lambda a, b, v: (a * 3 + b, 0, 0)),
                pl.BlockSpec(early.shape, lambda a, b, v: (0, 0, 0, 0), pipeline_mode=pl.Buffered(1)),
                pl.BlockSpec(memory_space=pl.ANY),
            ],
            out_specs=pl.BlockSpec(early.shape, lambda a, b, v: (0, 0, 0, 0)),
            scratch_shapes=[pltpu.VMEM((2, HR * WCOL, early.shape[-1]), jnp.float32)],
        ),
        out_shape=jax.ShapeDtypeStruct(decoded.shape, decoded.dtype),
        input_output_aliases={4: 0},
        compiler_params=pltpu.CompilerParams(
            dimension_semantics=("arbitrary", "arbitrary"), vmem_limit_bytes=60 * 1024 * 1024
        ),
    )(validity, wide, weights, early, decoded)


def solution(mesh):
    placed = (
        P(("src", "frame", "tile"), None),
        P(("src", "frame", "tile")),
        P(),
        P(),
        P(),
        P(),
        P(),
    )
    return jax.shard_map(
        shards,
        mesh=mesh,
        in_specs=placed,
        out_specs=P("frame", "tile", "src", None),
        check_vma=False,
    )
```

```python
import jax
import jax.numpy as jnp
from jax import lax
from jax.experimental import pallas as pl
from jax.experimental.pallas import tpu as pltpu
from jax.sharding import PartitionSpec as P

GROUPS = 32
CLIPS = 4
FR_DEV = 6
HR = 8
WCOL = 32
HIGH = lax.Precision.HIGHEST


def passed_along(x, axis, by):
    peers = lax.axis_size(axis)
    pairs = [(i, i + by) for i in range(peers) if 0 <= i + by < peers]
    return lax.ppermute(x, axis, pairs)


def with_halo(x, sides, width):
    for axis, dim in sides:
        peers, length = (lax.axis_size(axis), x.shape[dim])
        up = [(i, (i + 1) % peers) for i in range(peers - 1)]
        down = [(j, i) for i, j in up]
        last = lax.slice_in_dim(x, length - width, length, axis=dim)
        leading = lax.slice_in_dim(x, 0, width, axis=dim)
        before = lax.ppermute(last, axis, up)
        after = lax.ppermute(leading, axis, down)
        x = jnp.concatenate([before, x, after], axis=dim)
    return x


def shards(feats, row_map, clip_ids, norm_gain, norm_bias, conv_weight, conv_bias):
    local_rows, channels = feats.shape
    n_src = lax.axis_size("src")
    n_frame = lax.axis_size("frame")
    n_tile = lax.axis_size("tile")
    devices = n_src * n_frame * n_tile
    per_pair = local_rows // devices
    group_width = channels // GROUPS
    per_frame = HR * WCOL

    owners = row_map // local_rows
    slot_ids = row_map % local_rows
    frames = clip_ids.shape[0]
    row_frame = (owners // n_tile) % n_frame * FR_DEV + slot_ids // per_frame
    frame_onehot = (row_frame[:, None] == jnp.arange(frames, dtype=jnp.int32)[None, :]).astype(
        jnp.float32
    )
    clip_onehot = (clip_ids[:, None] == jnp.arange(CLIPS, dtype=jnp.int32)[None, :]).astype(
        jnp.float32
    )
    row_onehot = jnp.dot(frame_onehot, clip_onehot)

    clip_mask = row_onehot.T[:, :, None]
    local_n = jnp.sum(row_onehot, axis=0) * group_width
    local_s = jnp.sum(
        jnp.sum(feats[None] * clip_mask, axis=1).reshape(CLIPS, GROUPS, group_width), axis=2
    )
    local_m = local_s / jnp.maximum(local_n, 1.0)[:, None]
    wide_m = jnp.repeat(local_m, group_width, axis=1)
    row_m = jnp.sum(clip_mask * wide_m[:, None, :], axis=0)
    dev = feats - row_m
    local_m2 = jnp.sum(
        jnp.sum((dev * dev)[None] * clip_mask, axis=1).reshape(CLIPS, GROUPS, group_width),
        axis=2,
    )

    block = 16
    iota = lax.iota(jnp.int32, local_rows)
    _, sent_slots, ordering = lax.sort((owners, slot_ids, iota), num_keys=1, is_stable=True)
    stats = jnp.concatenate([local_n, local_s.reshape(-1), local_m2.reshape(-1)])
    info = jnp.concatenate(
        [
            sent_slots.astype(jnp.float32).reshape(devices, per_pair),
            jnp.broadcast_to(stats, (devices, stats.shape[0])),
            jnp.zeros((devices, channels - per_pair - stats.shape[0]), jnp.float32),
        ],
        axis=1,
    )
    pick = jnp.concatenate(
        [ordering.reshape(devices, per_pair), jnp.zeros((devices, block - per_pair), jnp.int32)],
        axis=1,
    )
    is_info = (jnp.arange(block) == per_pair)[None, :, None]
    payload = jnp.where(
        is_info, info[:, None, :], feats[pick.reshape(-1)].reshape(devices, block, channels)
    )
    arrived = lax.all_to_all(
        payload, ("src", "frame", "tile"), split_axis=0, concat_axis=0, tiled=True
    )

    info = arrived[:, per_pair, :]
    targets = info[:, :per_pair].reshape(-1).astype(jnp.int32)
    part_n = info[:, per_pair : per_pair + CLIPS]
    base = per_pair + CLIPS
    part_s = info[:, base : base + CLIPS * GROUPS].reshape(devices, CLIPS, GROUPS)
    part_m2 = info[:, base + CLIPS * GROUPS : base + 2 * CLIPS * GROUPS].reshape(
        devices, CLIPS, GROUPS
    )
    total_n = jnp.sum(part_n, axis=0)
    clip_mean = jnp.sum(part_s, axis=0) / total_n[:, None]
    part_m = part_s / jnp.maximum(part_n, 1.0)[:, :, None]
    spread = part_m - clip_mean[None]
    clip_m2 = jnp.sum(part_m2, axis=0) + jnp.sum(part_n[:, :, None] * spread * spread, axis=0)
    clip_var = clip_m2 / total_n[:, None]

    arrival_row = (iota // per_pair) * block + iota % per_pair
    digits = jnp.stack([arrival_row // 64, arrival_row % 64], axis=1).astype(jnp.bfloat16)
    chooser = (targets[None, :] == iota[:, None]).astype(jnp.bfloat16)
    found = jnp.dot(chooser, digits, preferred_element_type=jnp.float32).astype(jnp.int32)
    gather_rows = found[:, 0] * 64 + found[:, 1]
    features = arrived.reshape(-1, channels)[gather_rows].reshape(FR_DEV, HR, WCOL, channels)

    first_frame = lax.axis_index("frame") * FR_DEV
    padded_ids = jnp.concatenate([jnp.full((2,), -1, jnp.int32), clip_ids])
    window_ids = lax.dynamic_slice_in_dim(padded_ids, first_frame, FR_DEV + 2)
    own_ids = window_ids[2:]
    onehot = (own_ids[:, None] == jnp.arange(CLIPS, dtype=jnp.int32)[None, :]).astype(jnp.float32)
    shaped = features.reshape(FR_DEV, per_frame, GROUPS, group_width)
    frame_mean = jnp.dot(onehot, clip_mean, precision=HIGH)
    centred = shaped - frame_mean[:, None, :, None]
    inverse_std = 1.0 / jnp.sqrt(clip_var + 1e-06)
    frame_inv = jnp.dot(onehot, inverse_std, precision=HIGH)
    normed = (centred * frame_inv[:, None, :, None]).reshape(FR_DEV, HR, WCOL, channels)
    activated = jax.nn.silu(normed * norm_gain + norm_bias).astype(jnp.bfloat16)
    high_padded = with_halo(activated, (("tile", 1),), 1)
    n_wide = lax.axis_size("src")
    up = [(i, i + 1) for i in range(n_wide - 1)]
    left = lax.ppermute(high_padded[:, :, WCOL - 1 :], "src", up)
    right = lax.ppermute(high_padded[:, :, :1], "src", [(j, i) for i, j in up])
    own_wide = widen(high_padded, left, right)
    sent_prev = jnp.concatenate(
        [high_padded[FR_DEV - 2 :], left[FR_DEV - 2 :], right[FR_DEV - 2 :]], axis=2
    )
    prev = passed_along(sent_prev, "frame", 1)
    prev_wide = widen(prev[:, :, :WCOL], prev[:, :, WCOL : WCOL + 1], prev[:, :, WCOL + 1 :])

    validity = jnp.stack(
        [(window_ids[a : a + FR_DEV] == own_ids).astype(jnp.int32) for a in range(3)]
    )
    reach = jnp.arange(3)[:, None] + jnp.arange(FR_DEV)[None, :]
    own_valid = jnp.where(reach >= 2, validity, 0)
    prev_valid = jnp.where(reach < 2, validity, 0)[:2, :2].reshape(-1)
    late_valid = jnp.concatenate([prev_valid, own_valid[2]])
    weights = conv_weight.reshape(9, 3 * channels, channels)
    bias = conv_bias.reshape(1, channels)
    early = early_conv(own_valid[:2].reshape(-1), own_wide, weights)
    return late_conv(late_valid, prev_wide, weights, bias, own_wide, early, features)


def widen(block, left, right):
    shifted_in = jnp.concatenate([left, block[:, :, : WCOL - 1]], axis=2)
    shifted_out = jnp.concatenate([block[:, :, 1:], right], axis=2)
    return jnp.concatenate([shifted_in, block, shifted_out], axis=-1)


def early_kernel(valid_ref, x_ref, w_ref, acc_ref):
    tap_time = pl.program_id(0)
    tap_high = pl.program_id(1)

    @pl.when((tap_time == 0) & (tap_high == 0))
    def _():
        acc_ref[...] = jnp.zeros_like(acc_ref)

    for a in range(2):

        @pl.when(tap_time == a)
        def _():
            reach = FR_DEV - 2 + a
            lhs = x_ref[:reach, pl.ds(tap_high, HR)].reshape(reach * HR * WCOL, -1)
            part = jnp.dot(lhs, w_ref[0], preferred_element_type=jnp.float32)
            for j in range(reach):
                t = j + 2 - a
                keep = valid_ref[a * FR_DEV + t].astype(jnp.float32)
                acc_ref[t] += part[j * HR * WCOL : (j + 1) * HR * WCOL] * keep


def early_conv(validity, wide, weights):
    frames = wide.shape[0]
    channels = weights.shape[-1]
    return pl.pallas_call(
        early_kernel,
        grid_spec=pltpu.PrefetchScalarGridSpec(
            num_scalar_prefetch=1,
            grid=(2, 3),
            in_specs=[
                pl.BlockSpec(wide.shape, lambda a, b, v: (0, 0, 0, 0), pipeline_mode=pl.Buffered(1)),
                pl.BlockSpec((1,) + weights.shape[1:], lambda a, b, v: (a * 3 + b, 0, 0)),
            ],
            out_specs=pl.BlockSpec((frames, HR * WCOL, channels), lambda a, b, v: (0, 0, 0)),
        ),
        out_shape=jax.ShapeDtypeStruct((frames, HR * WCOL, channels), jnp.float32),
        compiler_params=pltpu.CompilerParams(
            dimension_semantics=("arbitrary", "arbitrary"), vmem_limit_bytes=60 * 1024 * 1024
        ),
    )(validity, wide, weights)


def late_kernel(
    valid_ref, xp_ref, w_ref, b_ref, xo_hbm, early_hbm, f_hbm, o_ref,
    xo_ref, early_ref, f_ref, acc_ref, sems,
):
    tap_time = pl.program_id(0)
    tap_high = pl.program_id(1)
    own_copy = pltpu.make_async_copy(xo_hbm, xo_ref, sems.at[0])
    early_copy = pltpu.make_async_copy(early_hbm, early_ref, sems.at[1])
    feature_copy = pltpu.make_async_copy(f_hbm, f_ref, sems.at[2])

    @pl.when((tap_time == 0) & (tap_high == 0))
    def _():
        own_copy.start()
        early_copy.start()
        feature_copy.start()
        acc_ref[...] = jnp.zeros_like(acc_ref)

    for a in range(2):

        @pl.when(tap_time == a)
        def _():
            reach = 2 - a
            lhs = xp_ref[a : a + reach, pl.ds(tap_high, HR)].reshape(reach * HR * WCOL, -1)
            part = jnp.dot(lhs, w_ref[0], preferred_element_type=jnp.float32)
            for t in range(reach):
                keep = valid_ref[a * 2 + t].astype(jnp.float32)
                acc_ref[t] += part[t * HR * WCOL : (t + 1) * HR * WCOL] * keep

    @pl.when((tap_time == 2) & (tap_high == 0))
    def _():
        own_copy.wait()

    @pl.when(tap_time == 2)
    def _():
        lhs = xo_ref[:, pl.ds(tap_high, HR)].reshape(FR_DEV * HR * WCOL, -1)
        part = jnp.dot(lhs, w_ref[0], preferred_element_type=jnp.float32)
        for t in range(FR_DEV):
            keep = valid_ref[4 + t].astype(jnp.float32)
            acc_ref[t] += part[t * HR * WCOL : (t + 1) * HR * WCOL] * keep

    @pl.when((tap_time == 2) & (tap_high == 2))
    def _():
        early_copy.wait()
        feature_copy.wait()
        for t in range(FR_DEV):
            conv_sum = (early_ref[t] + acc_ref[t]).reshape(HR, WCOL, -1)
            o_ref[t] = ((f_ref[t] + conv_sum) + b_ref[...]).astype(o_ref.dtype)


def late_conv(validity, prev_wide, weights, bias, own_wide, early, features):
    return pl.pallas_call(
        late_kernel,
        grid_spec=pltpu.PrefetchScalarGridSpec(
            num_scalar_prefetch=1,
            grid=(3, 3),
            in_specs=[
                pl.BlockSpec(
                    prev_wide.shape, lambda a, b, v: (0, 0, 0, 0), pipeline_mode=pl.Buffered(1)
                ),
                pl.BlockSpec((1,) + weights.shape[1:], lambda a, b, v: (a * 3 + b, 0, 0)),
                pl.BlockSpec(bias.shape, lambda a, b, v: (0, 0), pipeline_mode=pl.Buffered(1)),
                pl.BlockSpec(memory_space=pl.ANY),
                pl.BlockSpec(memory_space=pl.ANY),
                pl.BlockSpec(memory_space=pl.ANY),
            ],
            out_specs=pl.BlockSpec(features.shape, lambda a, b, v: (0, 0, 0, 0)),
            scratch_shapes=[
                pltpu.VMEM(own_wide.shape, own_wide.dtype),
                pltpu.VMEM(early.shape, jnp.float32),
                pltpu.VMEM(features.shape, jnp.float32),
                pltpu.VMEM(early.shape, jnp.float32),
                pltpu.SemaphoreType.DMA((3,)),
            ],
        ),
        out_shape=jax.ShapeDtypeStruct(features.shape, jnp.bfloat16),
        compiler_params=pltpu.CompilerParams(
            dimension_semantics=("arbitrary", "arbitrary"), vmem_limit_bytes=60 * 1024 * 1024
        ),
    )(validity, prev_wide, weights, bias, own_wide, early, features)


def solution(mesh):
    placed = (
        P(("src", "frame", "tile"), None),
        P(("src", "frame", "tile")),
        P(),
        P(),
        P(),
        P(),
        P(),
    )
    return jax.shard_map(
        shards,
        mesh=mesh,
        in_specs=placed,
        out_specs=P("frame", "tile", "src", None),
        check_vma=False,
    )
```

```python
import jax
import jax.numpy as jnp
from jax import lax
from jax.experimental import pallas as pl
from jax.experimental.pallas import tpu as pltpu
from jax.sharding import PartitionSpec as P

GROUPS = 32
CLIPS = 4
FR_DEV = 6
HR = 8
WCOL = 32
HIGH = lax.Precision.HIGHEST


def passed_along(x, axis, by):
    peers = lax.axis_size(axis)
    pairs = [(i, i + by) for i in range(peers) if 0 <= i + by < peers]
    return lax.ppermute(x, axis, pairs)


def with_halo(x, sides, width):
    for axis, dim in sides:
        peers, length = (lax.axis_size(axis), x.shape[dim])
        up = [(i, (i + 1) % peers) for i in range(peers - 1)]
        down = [(j, i) for i, j in up]
        last = lax.slice_in_dim(x, length - width, length, axis=dim)
        leading = lax.slice_in_dim(x, 0, width, axis=dim)
        before = lax.ppermute(last, axis, up)
        after = lax.ppermute(leading, axis, down)
        x = jnp.concatenate([before, x, after], axis=dim)
    return x


def shards(feats, row_map, clip_ids, norm_gain, norm_bias, conv_weight, conv_bias):
    local_rows, channels = feats.shape
    n_src = lax.axis_size("src")
    n_frame = lax.axis_size("frame")
    n_tile = lax.axis_size("tile")
    devices = n_src * n_frame * n_tile
    per_pair = local_rows // devices
    group_width = channels // GROUPS
    per_frame = HR * WCOL

    owners = row_map // local_rows
    slot_ids = row_map % local_rows
    frames = clip_ids.shape[0]
    row_frame = (owners // n_tile) % n_frame * FR_DEV + slot_ids // per_frame
    frame_onehot = (row_frame[:, None] == jnp.arange(frames, dtype=jnp.int32)[None, :]).astype(
        jnp.float32
    )
    clip_onehot = (clip_ids[:, None] == jnp.arange(CLIPS, dtype=jnp.int32)[None, :]).astype(
        jnp.float32
    )
    row_onehot = jnp.dot(frame_onehot, clip_onehot)

    clip_mask = row_onehot.T[:, :, None]
    local_n = jnp.sum(row_onehot, axis=0) * group_width
    local_s = jnp.sum(
        jnp.sum(feats[None] * clip_mask, axis=1).reshape(CLIPS, GROUPS, group_width), axis=2
    )
    local_m = local_s / jnp.maximum(local_n, 1.0)[:, None]
    wide_m = jnp.repeat(local_m, group_width, axis=1)
    row_m = jnp.sum(clip_mask * wide_m[:, None, :], axis=0)
    dev = feats - row_m
    local_m2 = jnp.sum(
        jnp.sum((dev * dev)[None] * clip_mask, axis=1).reshape(CLIPS, GROUPS, group_width),
        axis=2,
    )

    block = 16
    iota = lax.iota(jnp.int32, local_rows)
    _, sent_slots, ordering = lax.sort((owners, slot_ids, iota), num_keys=1, is_stable=True)
    stats = jnp.concatenate([local_n, local_s.reshape(-1), local_m2.reshape(-1)])
    info = jnp.concatenate(
        [
            sent_slots.astype(jnp.float32).reshape(devices, per_pair),
            jnp.broadcast_to(stats, (devices, stats.shape[0])),
            jnp.zeros((devices, channels - per_pair - stats.shape[0]), jnp.float32),
        ],
        axis=1,
    )
    pick = jnp.concatenate(
        [ordering.reshape(devices, per_pair), jnp.zeros((devices, block - per_pair), jnp.int32)],
        axis=1,
    )
    is_info = (jnp.arange(block) == per_pair)[None, :, None]
    payload = jnp.where(
        is_info, info[:, None, :], feats[pick.reshape(-1)].reshape(devices, block, channels)
    )
    arrived = lax.all_to_all(
        payload, ("src", "frame", "tile"), split_axis=0, concat_axis=0, tiled=True
    )

    info = arrived[:, per_pair, :]
    targets = info[:, :per_pair].reshape(-1).astype(jnp.int32)
    part_n = info[:, per_pair : per_pair + CLIPS]
    base = per_pair + CLIPS
    part_s = info[:, base : base + CLIPS * GROUPS].reshape(devices, CLIPS, GROUPS)
    part_m2 = info[:, base + CLIPS * GROUPS : base + 2 * CLIPS * GROUPS].reshape(
        devices, CLIPS, GROUPS
    )
    total_n = jnp.sum(part_n, axis=0)
    clip_mean = jnp.sum(part_s, axis=0) / total_n[:, None]
    part_m = part_s / jnp.maximum(part_n, 1.0)[:, :, None]
    spread = part_m - clip_mean[None]
    clip_m2 = jnp.sum(part_m2, axis=0) + jnp.sum(part_n[:, :, None] * spread * spread, axis=0)
    clip_var = clip_m2 / total_n[:, None]

    arrival_row = (iota // per_pair) * block + iota % per_pair
    digits = jnp.stack([arrival_row // 64, arrival_row % 64], axis=1).astype(jnp.bfloat16)
    chooser = (targets[None, :] == iota[:, None]).astype(jnp.bfloat16)
    found = jnp.dot(chooser, digits, preferred_element_type=jnp.float32).astype(jnp.int32)
    gather_rows = found[:, 0] * 64 + found[:, 1]
    features = arrived.reshape(-1, channels)[gather_rows].reshape(FR_DEV, HR, WCOL, channels)

    first_frame = lax.axis_index("frame") * FR_DEV
    padded_ids = jnp.concatenate([jnp.full((2,), -1, jnp.int32), clip_ids])
    window_ids = lax.dynamic_slice_in_dim(padded_ids, first_frame, FR_DEV + 2)
    own_ids = window_ids[2:]
    onehot = (own_ids[:, None] == jnp.arange(CLIPS, dtype=jnp.int32)[None, :]).astype(jnp.float32)
    shaped = features.reshape(FR_DEV, per_frame, GROUPS, group_width)
    frame_mean = jnp.dot(onehot, clip_mean, precision=HIGH)
    centred = shaped - frame_mean[:, None, :, None]
    inverse_std = 1.0 / jnp.sqrt(clip_var + 1e-06)
    frame_inv = jnp.dot(onehot, inverse_std, precision=HIGH)
    normed = (centred * frame_inv[:, None, :, None]).reshape(FR_DEV, HR, WCOL, channels)
    activated = jax.nn.silu(normed * norm_gain + norm_bias).astype(jnp.bfloat16)
    high_padded = with_halo(activated, (("tile", 1),), 1)
    n_wide = lax.axis_size("src")
    up = [(i, i + 1) for i in range(n_wide - 1)]
    left = lax.ppermute(high_padded[:, :, WCOL - 1 :], "src", up)
    right = lax.ppermute(high_padded[:, :, :1], "src", [(j, i) for i, j in up])
    own_wide = widen(high_padded, left, right)
    sent_prev = jnp.concatenate(
        [high_padded[FR_DEV - 2 :], left[FR_DEV - 2 :], right[FR_DEV - 2 :]], axis=2
    )
    prev = passed_along(sent_prev, "frame", 1)
    prev_wide = widen(prev[:, :, :WCOL], prev[:, :, WCOL : WCOL + 1], prev[:, :, WCOL + 1 :])

    validity = jnp.stack(
        [(window_ids[a : a + FR_DEV] == own_ids).astype(jnp.int32) for a in range(3)]
    )
    reach = jnp.arange(3)[:, None] + jnp.arange(FR_DEV)[None, :]
    own_valid = jnp.where(reach >= 2, validity, 0).reshape(-1)
    prev_valid = jnp.where(reach < 2, validity, 0)[:2, :2].reshape(-1)
    weights = conv_weight.reshape(9, 3 * channels, channels)
    bias = conv_bias.reshape(1, channels)
    decoded, early = own_conv(own_valid, own_wide, weights, features, bias)
    return prev_conv(prev_valid, prev_wide, weights, early, decoded)


def widen(block, left, right):
    shifted_in = jnp.concatenate([left, block[:, :, : WCOL - 1]], axis=2)
    shifted_out = jnp.concatenate([block[:, :, 1:], right], axis=2)
    return jnp.concatenate([shifted_in, block, shifted_out], axis=-1)


def own_kernel(valid_ref, x_ref, w_ref, b_ref, f_hbm, o_ref, early_ref, f_ref, acc_ref, sem):
    tap_time = pl.program_id(0)
    tap_high = pl.program_id(1)
    fetch = pltpu.make_async_copy(f_hbm, f_ref, sem)

    @pl.when((tap_time == 0) & (tap_high == 0))
    def _():
        fetch.start()
        acc_ref[...] = jnp.zeros_like(acc_ref)

    for a in range(3):

        @pl.when(tap_time == a)
        def _():
            reach = FR_DEV - 2 + a
            lhs = x_ref[:reach, pl.ds(tap_high, HR)].reshape(reach * HR * WCOL, -1)
            part = jnp.dot(lhs, w_ref[0], preferred_element_type=jnp.float32)
            for j in range(reach):
                t = j + 2 - a
                keep = valid_ref[a * FR_DEV + t].astype(jnp.float32)
                acc_ref[t] += part[j * HR * WCOL : (j + 1) * HR * WCOL] * keep

    @pl.when((tap_time == 2) & (tap_high == 2))
    def _():
        fetch.wait()
        for t in range(FR_DEV):
            total = (f_ref[t] + acc_ref[t].reshape(HR, WCOL, -1)) + b_ref[...]
            if t < 2:
                early_ref[t] = total
            else:
                o_ref[t] = total.astype(o_ref.dtype)


def own_conv(validity, wide, weights, features, bias):
    return pl.pallas_call(
        own_kernel,
        grid_spec=pltpu.PrefetchScalarGridSpec(
            num_scalar_prefetch=1,
            grid=(3, 3),
            in_specs=[
                pl.BlockSpec(wide.shape, lambda a, b, v: (0, 0, 0, 0), pipeline_mode=pl.Buffered(1)),
                pl.BlockSpec((1,) + weights.shape[1:], lambda a, b, v: (a * 3 + b, 0, 0)),
                pl.BlockSpec(bias.shape, lambda a, b, v: (0, 0), pipeline_mode=pl.Buffered(1)),
                pl.BlockSpec(memory_space=pl.ANY),
            ],
            out_specs=[
                pl.BlockSpec(features.shape, lambda a, b, v: (0, 0, 0, 0)),
                pl.BlockSpec((2,) + features.shape[1:], lambda a, b, v: (0, 0, 0, 0)),
            ],
            scratch_shapes=[
                pltpu.VMEM(features.shape, jnp.float32),
                pltpu.VMEM((features.shape[0], HR * WCOL, features.shape[-1]), jnp.float32),
                pltpu.SemaphoreType.DMA(()),
            ],
        ),
        out_shape=[
            jax.ShapeDtypeStruct(features.shape, jnp.bfloat16),
            jax.ShapeDtypeStruct((2,) + features.shape[1:], jnp.float32),
        ],
        compiler_params=pltpu.CompilerParams(
            dimension_semantics=("arbitrary", "arbitrary"), vmem_limit_bytes=60 * 1024 * 1024
        ),
    )(validity, wide, weights, bias, features)


def prev_kernel(valid_ref, x_ref, w_ref, early_ref, whole_ref, o_ref, acc_ref):
    del whole_ref
    tap_time = pl.program_id(0)

    @pl.when(tap_time == 0)
    def _():
        acc_ref[...] = jnp.zeros_like(acc_ref)

    for a in range(2):

        @pl.when(tap_time == a)
        def _():
            reach = 2 - a
            for b in range(3):
                lhs = x_ref[a : a + reach, b : b + HR].reshape(reach * HR * WCOL, -1)
                part = jnp.dot(lhs, w_ref[0, b], preferred_element_type=jnp.float32)
                for t in range(reach):
                    keep = valid_ref[a * 2 + t].astype(jnp.float32)
                    acc_ref[t] += part[t * HR * WCOL : (t + 1) * HR * WCOL] * keep

    @pl.when(tap_time == 1)
    def _():
        for t in range(2):
            total = early_ref[t] + acc_ref[t].reshape(HR, WCOL, -1)
            o_ref[t] = total.astype(o_ref.dtype)


def prev_conv(validity, wide, weights, early, decoded):
    taps = weights.reshape(3, 3, *weights.shape[1:])
    return pl.pallas_call(
        prev_kernel,
        grid_spec=pltpu.PrefetchScalarGridSpec(
            num_scalar_prefetch=1,
            grid=(2,),
            in_specs=[
                pl.BlockSpec(wide.shape, lambda a, v: (0, 0, 0, 0), pipeline_mode=pl.Buffered(1)),
                pl.BlockSpec((1,) + taps.shape[1:], lambda a, v: (a, 0, 0, 0)),
                pl.BlockSpec(early.shape, lambda a, v: (0, 0, 0, 0), pipeline_mode=pl.Buffered(1)),
                pl.BlockSpec(memory_space=pl.ANY),
            ],
            out_specs=pl.BlockSpec(early.shape, lambda a, v: (0, 0, 0, 0)),
            scratch_shapes=[pltpu.VMEM((2, HR * WCOL, early.shape[-1]), jnp.float32)],
        ),
        out_shape=jax.ShapeDtypeStruct(decoded.shape, decoded.dtype),
        input_output_aliases={4: 0},
        compiler_params=pltpu.CompilerParams(
            dimension_semantics=("arbitrary",), vmem_limit_bytes=60 * 1024 * 1024
        ),
    )(validity, wide, taps, early, decoded)


def solution(mesh):
    placed = (
        P(("src", "frame", "tile"), None),
        P(("src", "frame", "tile")),
        P(),
        P(),
        P(),
        P(),
        P(),
    )
    return jax.shard_map(
        shards,
        mesh=mesh,
        in_specs=placed,
        out_specs=P("frame", "tile", "src", None),
        check_vma=False,
    )
```

```python
import jax
import jax.numpy as jnp
from jax import lax
from jax.experimental import pallas as pl
from jax.experimental.pallas import tpu as pltpu
from jax.sharding import PartitionSpec as P

GROUPS = 32
CLIPS = 4
FR_DEV = 6
HR = 8
WCOL = 32
HIGH = lax.Precision.HIGHEST


def passed_along(x, axis, by):
    peers = lax.axis_size(axis)
    pairs = [(i, i + by) for i in range(peers) if 0 <= i + by < peers]
    return lax.ppermute(x, axis, pairs)


def with_halo(x, sides, width):
    for axis, dim in sides:
        peers, length = (lax.axis_size(axis), x.shape[dim])
        up = [(i, (i + 1) % peers) for i in range(peers - 1)]
        down = [(j, i) for i, j in up]
        last = lax.slice_in_dim(x, length - width, length, axis=dim)
        leading = lax.slice_in_dim(x, 0, width, axis=dim)
        before = lax.ppermute(last, axis, up)
        after = lax.ppermute(leading, axis, down)
        x = jnp.concatenate([before, x, after], axis=dim)
    return x


def shards(feats, row_map, clip_ids, norm_gain, norm_bias, conv_weight, conv_bias):
    local_rows, channels = feats.shape
    n_src = lax.axis_size("src")
    n_frame = lax.axis_size("frame")
    n_tile = lax.axis_size("tile")
    devices = n_src * n_frame * n_tile
    per_pair = local_rows // devices
    group_width = channels // GROUPS
    per_frame = HR * WCOL

    owners = row_map // local_rows
    slot_ids = row_map % local_rows
    frames = clip_ids.shape[0]
    row_frame = (owners // n_tile) % n_frame * FR_DEV + slot_ids // per_frame
    frame_onehot = (row_frame[:, None] == jnp.arange(frames, dtype=jnp.int32)[None, :]).astype(
        jnp.float32
    )
    clip_onehot = (clip_ids[:, None] == jnp.arange(CLIPS, dtype=jnp.int32)[None, :]).astype(
        jnp.float32
    )
    row_onehot = jnp.dot(frame_onehot, clip_onehot)

    clip_mask = row_onehot.T[:, :, None]
    local_n = jnp.sum(row_onehot, axis=0) * group_width
    local_s = jnp.sum(
        jnp.sum(feats[None] * clip_mask, axis=1).reshape(CLIPS, GROUPS, group_width), axis=2
    )
    local_m = local_s / jnp.maximum(local_n, 1.0)[:, None]
    wide_m = jnp.repeat(local_m, group_width, axis=1)
    row_m = jnp.sum(clip_mask * wide_m[:, None, :], axis=0)
    dev = feats - row_m
    local_m2 = jnp.sum(
        jnp.sum((dev * dev)[None] * clip_mask, axis=1).reshape(CLIPS, GROUPS, group_width),
        axis=2,
    )

    block = 16
    iota = lax.iota(jnp.int32, local_rows)
    _, sent_slots, ordering = lax.sort((owners, slot_ids, iota), num_keys=1, is_stable=True)
    stats = jnp.concatenate([local_n, local_s.reshape(-1), local_m2.reshape(-1)])
    info = jnp.concatenate(
        [
            sent_slots.astype(jnp.float32).reshape(devices, per_pair),
            jnp.broadcast_to(stats, (devices, stats.shape[0])),
            jnp.zeros((devices, channels - per_pair - stats.shape[0]), jnp.float32),
        ],
        axis=1,
    )
    pick = jnp.concatenate(
        [ordering.reshape(devices, per_pair), jnp.zeros((devices, block - per_pair), jnp.int32)],
        axis=1,
    )
    is_info = (jnp.arange(block) == per_pair)[None, :, None]
    payload = jnp.where(
        is_info, info[:, None, :], feats[pick.reshape(-1)].reshape(devices, block, channels)
    )
    arrived = lax.all_to_all(
        payload, ("src", "frame", "tile"), split_axis=0, concat_axis=0, tiled=True
    )

    info = arrived[:, per_pair, :]
    targets = info[:, :per_pair].reshape(-1).astype(jnp.int32)
    part_n = info[:, per_pair : per_pair + CLIPS]
    base = per_pair + CLIPS
    part_s = info[:, base : base + CLIPS * GROUPS].reshape(devices, CLIPS, GROUPS)
    part_m2 = info[:, base + CLIPS * GROUPS : base + 2 * CLIPS * GROUPS].reshape(
        devices, CLIPS, GROUPS
    )
    total_n = jnp.sum(part_n, axis=0)
    clip_mean = jnp.sum(part_s, axis=0) / total_n[:, None]
    part_m = part_s / jnp.maximum(part_n, 1.0)[:, :, None]
    spread = part_m - clip_mean[None]
    clip_m2 = jnp.sum(part_m2, axis=0) + jnp.sum(part_n[:, :, None] * spread * spread, axis=0)
    clip_var = clip_m2 / total_n[:, None]

    arrival_row = (iota // per_pair) * block + iota % per_pair
    digits = jnp.stack([arrival_row // 64, arrival_row % 64], axis=1).astype(jnp.bfloat16)
    chooser = (targets[None, :] == iota[:, None]).astype(jnp.bfloat16)
    found = jnp.dot(chooser, digits, preferred_element_type=jnp.float32).astype(jnp.int32)
    gather_rows = found[:, 0] * 64 + found[:, 1]
    features = arrived.reshape(-1, channels)[gather_rows].reshape(FR_DEV, HR, WCOL, channels)

    first_frame = lax.axis_index("frame") * FR_DEV
    padded_ids = jnp.concatenate([jnp.full((2,), -1, jnp.int32), clip_ids])
    window_ids = lax.dynamic_slice_in_dim(padded_ids, first_frame, FR_DEV + 2)
    own_ids = window_ids[2:]
    onehot = (own_ids[:, None] == jnp.arange(CLIPS, dtype=jnp.int32)[None, :]).astype(jnp.float32)
    shaped = features.reshape(FR_DEV, per_frame, GROUPS, group_width)
    frame_mean = jnp.dot(onehot, clip_mean, precision=HIGH)
    centred = shaped - frame_mean[:, None, :, None]
    inverse_std = 1.0 / jnp.sqrt(clip_var + 1e-06)
    frame_inv = jnp.dot(onehot, inverse_std, precision=HIGH)
    normed = (centred * frame_inv[:, None, :, None]).reshape(FR_DEV, HR, WCOL, channels)
    activated = jax.nn.silu(normed * norm_gain + norm_bias).astype(jnp.bfloat16)
    high_padded = with_halo(activated, (("tile", 1),), 1)
    n_wide = lax.axis_size("src")
    up = [(i, i + 1) for i in range(n_wide - 1)]
    left = lax.ppermute(high_padded[:, :, WCOL - 1 :], "src", up)
    right = lax.ppermute(high_padded[:, :, :1], "src", [(j, i) for i, j in up])
    own_wide = widen(high_padded, left, right)
    cols = jnp.concatenate([left[FR_DEV - 2 :], right[FR_DEV - 2 :]], axis=2)
    prev_high, prev_cols = passed_along((high_padded[FR_DEV - 2 :], cols), "frame", 1)
    prev_wide = widen(prev_high, prev_cols[:, :, :1], prev_cols[:, :, 1:])

    validity = jnp.stack(
        [(window_ids[a : a + FR_DEV] == own_ids).astype(jnp.int32) for a in range(3)]
    )
    reach = jnp.arange(3)[:, None] + jnp.arange(FR_DEV)[None, :]
    own_valid = jnp.where(reach >= 2, validity, 0).reshape(-1)
    prev_valid = jnp.where(reach < 2, validity, 0)[:2, :2].reshape(-1)
    weights = conv_weight.reshape(9, 3 * channels, channels)
    bias = conv_bias.reshape(1, channels)
    decoded, early = own_conv(own_valid, own_wide, weights, features, bias)
    return prev_conv(prev_valid, prev_wide, weights, early, decoded)


def widen(block, left, right):
    shifted_in = jnp.concatenate([left, block[:, :, : WCOL - 1]], axis=2)
    shifted_out = jnp.concatenate([block[:, :, 1:], right], axis=2)
    return jnp.concatenate([shifted_in, block, shifted_out], axis=-1)


def own_kernel(valid_ref, x_ref, w_ref, b_ref, f_hbm, o_ref, early_ref, f_ref, acc_ref, sem):
    tap_time = pl.program_id(0)
    tap_high = pl.program_id(1)
    fetch = pltpu.make_async_copy(f_hbm, f_ref, sem)

    @pl.when((tap_time == 0) & (tap_high == 0))
    def _():
        fetch.start()
        acc_ref[...] = jnp.zeros_like(acc_ref)

    for a in range(3):

        @pl.when(tap_time == a)
        def _():
            reach = FR_DEV - 2 + a
            lhs = x_ref[:reach, pl.ds(tap_high, HR)].reshape(reach * HR * WCOL, -1)
            part = jnp.dot(lhs, w_ref[0], preferred_element_type=jnp.float32)
            for j in range(reach):
                t = j + 2 - a
                keep = valid_ref[a * FR_DEV + t].astype(jnp.float32)
                acc_ref[t] += part[j * HR * WCOL : (j + 1) * HR * WCOL] * keep

    @pl.when((tap_time == 2) & (tap_high == 2))
    def _():
        fetch.wait()
        for t in range(FR_DEV):
            total = (f_ref[t] + acc_ref[t].reshape(HR, WCOL, -1)) + b_ref[...]
            if t < 2:
                early_ref[t] = total
            else:
                o_ref[t] = total.astype(o_ref.dtype)


def own_conv(validity, wide, weights, features, bias):
    return pl.pallas_call(
        own_kernel,
        grid_spec=pltpu.PrefetchScalarGridSpec(
            num_scalar_prefetch=1,
            grid=(3, 3),
            in_specs=[
                pl.BlockSpec(wide.shape, lambda a, b, v: (0, 0, 0, 0), pipeline_mode=pl.Buffered(1)),
                pl.BlockSpec((1,) + weights.shape[1:], lambda a, b, v: (a * 3 + b, 0, 0)),
                pl.BlockSpec(bias.shape, lambda a, b, v: (0, 0), pipeline_mode=pl.Buffered(1)),
                pl.BlockSpec(memory_space=pl.ANY),
            ],
            out_specs=[
                pl.BlockSpec(features.shape, lambda a, b, v: (0, 0, 0, 0)),
                pl.BlockSpec((2,) + features.shape[1:], lambda a, b, v: (0, 0, 0, 0)),
            ],
            scratch_shapes=[
                pltpu.VMEM(features.shape, jnp.float32),
                pltpu.VMEM((features.shape[0], HR * WCOL, features.shape[-1]), jnp.float32),
                pltpu.SemaphoreType.DMA(()),
            ],
        ),
        out_shape=[
            jax.ShapeDtypeStruct(features.shape, jnp.bfloat16),
            jax.ShapeDtypeStruct((2,) + features.shape[1:], jnp.float32),
        ],
        compiler_params=pltpu.CompilerParams(
            dimension_semantics=("arbitrary", "arbitrary"), vmem_limit_bytes=60 * 1024 * 1024
        ),
    )(validity, wide, weights, bias, features)


def prev_kernel(valid_ref, x_ref, w_ref, early_ref, whole_ref, o_ref, acc_ref):
    del whole_ref
    tap_time = pl.program_id(0)
    tap_high = pl.program_id(1)

    @pl.when((tap_time == 0) & (tap_high == 0))
    def _():
        acc_ref[...] = jnp.zeros_like(acc_ref)

    for t in range(2):

        @pl.when(valid_ref[tap_time * 2 + t] != 0)
        def _():
            frame = jnp.minimum(tap_time + t, 1)
            lhs = x_ref[frame, pl.ds(tap_high, HR)].reshape(HR * WCOL, -1)
            acc_ref[t] += jnp.dot(lhs, w_ref[0], preferred_element_type=jnp.float32)

    @pl.when((tap_time == 1) & (tap_high == 2))
    def _():
        for t in range(2):
            total = early_ref[t] + acc_ref[t].reshape(HR, WCOL, -1)
            o_ref[t] = total.astype(o_ref.dtype)


def prev_conv(validity, wide, weights, early, decoded):
    return pl.pallas_call(
        prev_kernel,
        grid_spec=pltpu.PrefetchScalarGridSpec(
            num_scalar_prefetch=1,
            grid=(2, 3),
            in_specs=[
                pl.BlockSpec(wide.shape, lambda a, b, v: (0, 0, 0, 0), pipeline_mode=pl.Buffered(1)),
                pl.BlockSpec((1,) + weights.shape[1:], lambda a, b, v: (a * 3 + b, 0, 0)),
                pl.BlockSpec(early.shape, lambda a, b, v: (0, 0, 0, 0), pipeline_mode=pl.Buffered(1)),
                pl.BlockSpec(memory_space=pl.ANY),
            ],
            out_specs=pl.BlockSpec(early.shape, lambda a, b, v: (0, 0, 0, 0)),
            scratch_shapes=[pltpu.VMEM((2, HR * WCOL, early.shape[-1]), jnp.float32)],
        ),
        out_shape=jax.ShapeDtypeStruct(decoded.shape, decoded.dtype),
        input_output_aliases={4: 0},
        compiler_params=pltpu.CompilerParams(
            dimension_semantics=("arbitrary", "arbitrary"), vmem_limit_bytes=60 * 1024 * 1024
        ),
    )(validity, wide, weights, early, decoded)


def solution(mesh):
    placed = (
        P(("src", "frame", "tile"), None),
        P(("src", "frame", "tile")),
        P(),
        P(),
        P(),
        P(),
        P(),
    )
    return jax.shard_map(
        shards,
        mesh=mesh,
        in_specs=placed,
        out_specs=P("frame", "tile", "src", None),
        check_vma=False,
    )
```
